32 devices in a mesh: pulse: 16 (over z, y, core), range: 2 (over x).
Axes of the slice: x: 2, y: 2, z: 4, core: 2. Of those that a mesh axis runs over, the one named last changes fastest.
Arguments:
- raw: bfloat16 [2, 256, 8192], P(None, 'pulse', 'range'), may hold values from -6 to 6
- filt: bfloat16 [2, 512], replicated, may hold values from -0.1875 to 0.1875
- tap_index: int32 [8, 2, 4], replicated, may hold values from 0 to 7
- tap_weight: float32 [8, 2, 4], replicated, may hold values from 0.25 to 0.7
- beam_shift: int32 [2, 510], replicated, may hold values from 0 to 7
- beam_phase: float32 [2, 510], replicated, may hold values from -3.140625 to 3.140625
Outputs:
- image: float32 [2, 256, 8192], P(None, 'pulse', 'range')
The draws below stay inside these ranges and needn't reach their ends.
All inputs are finite; a program needn't handle non-finite values.
Results may differ from the reference program's by a relative error of at most 0.0003.
Values may be sent and summed in bfloat16 or wider, within the bound.
No kernel may reach another device: no remote copies, remote signals or barrier semaphores. Data moves between devices by JAX's collectives and lax.ppermute only.
A program may use at most 128 MiB of HBM per device.

```python
import jax
import jax.numpy as jnp
from jax import lax

K = 512
TAPS = 4
MAXOFF = 8
MARGIN = 15
SECTIONS = 8
PULSES = 256
RANGE = 8192


def place_ends(drawn, stream_key, smallest, high):
    longest = drawn.shape.index(max(drawn.shape))
    spots = []
    for shift in (0, 1):
        where = [jax.random.randint(jax.random.fold_in(stream_key, axis), (), 0, length) for axis, length in enumerate(drawn.shape)]
        where[longest] = (where[longest] + shift) % drawn.shape[longest]
        spots.append(tuple(where))
    return drawn.at[spots[0]].set(smallest).at[spots[1]].set(high)


def block_levels(own_key, shape, shards, least, largest):
    def one(dim, shards_of):
        draws = jax.random.uniform(jax.random.fold_in(jax.random.fold_in(own_key, 6), dim), (shards_of,), jnp.float32, least / len(shards), largest / len(shards))
        return jnp.repeat(jnp.exp(draws), shape[dim] // shards_of).reshape((-1,) + (1,) * (len(shape) - dim - 1))

    loudness = one(*shards[0])
    for cut in shards[1:]:
        loudness = loudness * one(*cut)
    return loudness


def normal_values(key, dims, width, bound, shards=(), kind=jnp.bfloat16):
    entries = jax.random.normal(key, dims, jnp.float32) * width
    if len(shards) > 0:
        entries = block_levels(key, dims, shards, -0.22, 0.18) * entries
    return jnp.clip(entries, min=-bound, max=bound).astype(kind)


def setup_inputs(seed: int = 0) -> dict:
    arg_keys = jax.random.split(jax.random.key(seed), 7)
    raw = normal_values(arg_keys[0], (2, PULSES, RANGE), 1.0, 6.0, ((1, 16), (2, 2)))
    filt = normal_values(arg_keys[1], (2, K), (2 * K) ** -0.5, 0.1875)
    tap_index = place_ends(jax.random.randint(arg_keys[2], (SECTIONS, 2, TAPS), 0, 2 * TAPS), jax.random.fold_in(arg_keys[2], 1), 0, (2 * TAPS) - 1).astype(jnp.int32)
    tap_weight = jnp.clip(jax.random.uniform(arg_keys[3], (SECTIONS, 2, TAPS), jnp.float32, 0.25, 0.7), 0.25, 0.7)
    beam_shift = place_ends(jax.random.randint(arg_keys[4], (2, 2 * PULSES - 2), 0, MAXOFF), jax.random.fold_in(arg_keys[4], 1), 0, MAXOFF - 1).astype(jnp.int32)
    beam_phase = jnp.clip(jax.random.uniform(arg_keys[5], (2, 2 * PULSES - 2), jnp.float32, -3.140625, 3.140625), -3.140625, 3.140625)
    return {"raw": raw, "filt": filt, "tap_index": tap_index, "tap_weight": tap_weight, "beam_shift": beam_shift, "beam_phase": beam_phase}


half_root = 0.7071067811865476


def compress_field(raw, filt):
    parts, count, bins = raw.shape
    taps_len = filt.shape[1]
    size = bins + taps_len
    kernel = lax.complex(filt[0].astype(jnp.float32), filt[1].astype(jnp.float32))
    padded = jnp.concatenate([kernel[:1], jnp.zeros((size - taps_len,), kernel.dtype), kernel[:0:-1]])
    spectrum = jnp.fft.fft(padded)
    group = min(256, count)
    blocks = raw.reshape(parts, count // group, group, bins).transpose(1, 0, 2, 3)

    def one_block(block_rows):
        signal = lax.complex(block_rows[0].astype(jnp.float32), block_rows[1].astype(jnp.float32))
        signal = jnp.pad(signal, ((0, 0), (0, size - bins)))
        output = jnp.fft.ifft(jnp.fft.fft(signal, axis=1) * spectrum[None, :], axis=1)[:, :bins]
        return jnp.stack([jnp.real(output), jnp.imag(output)]).astype(jnp.float32)

    result = lax.map(one_block, blocks)
    return result.transpose(1, 0, 2, 3).reshape(parts, count, bins)


def side_term(kid, taps, weights, shifts, angles):
    length = kid.shape[3]
    span = length - MARGIN
    inner = span + MAXOFF - 1
    interp = jnp.zeros(kid.shape[:3] + (inner,), jnp.float32)
    for tap in range(TAPS):
        interp = interp + weights[tap] * lax.dynamic_slice_in_dim(kid, taps[tap], inner, axis=3)

    def cut_row(row, start):
        return lax.dynamic_slice_in_dim(row, start, span, 0)

    per_beam = jax.vmap(cut_row, in_axes=(0, 0))
    per_half = jax.vmap(per_beam, in_axes=(None, 0))
    per_group = jax.vmap(per_half, in_axes=(0, None))
    per_part = jax.vmap(per_group, in_axes=(0, None))
    moved = per_part(interp, shifts)
    cosine = jnp.cos(angles)[None, :, :, None]
    sine = jnp.sin(angles)[None, :, :, None]
    real_part = cosine * moved[0] - sine * moved[1]
    imag_part = sine * moved[0] + cosine * moved[1]
    return jnp.stack([real_part, imag_part])


def merge_section(child, taps, weights, shifts, angles):
    parts, count, beams, length = child.shape
    pairs = child.reshape(parts, count // 2, 2, beams, length)
    first = side_term(pairs[:, :, 0], taps[0], weights[0], shifts[0].reshape(2, beams), angles[0].reshape(2, beams))
    second = side_term(pairs[:, :, 1], taps[1], weights[1], shifts[1].reshape(2, beams), angles[1].reshape(2, beams))
    merged = (first + second) * half_root
    return merged.reshape(parts, count // 2, 2 * beams, length - MARGIN)


def reference(raw, filt, tap_index, tap_weight, beam_shift, beam_phase):
    level = compress_field(raw, filt)[:, :, None, :]
    for section in range(SECTIONS):
        beams = 2 ** section
        start = 2 * beams - 2
        padded = jnp.pad(level, ((0, 0), (0, 0), (0, 0), (0, MARGIN)))
        level = merge_section(padded, tap_index[section], tap_weight[section], beam_shift[:, start:start + 2 * beams], beam_phase[:, start:start + 2 * beams])
    return level.reshape(2, PULSES, RANGE)
```

```python
import jax
import jax.numpy as jnp
from jax import lax
from jax.sharding import PartitionSpec as P

TAPS = 4
MAXOFF = 8
MARGIN = 15
BLOCK = 256


half_root = 0.7071067811865476


def shifted(shard, axis, by):
    count = lax.axis_size(axis)
    pairs = [(i, i + by) for i in range(count) if 0 <= i + by < count]
    return lax.ppermute(shard, axis, pairs)


def toeplitz_rows(vector, block, rows):
    taps_len = vector.shape[0]
    width = rows + 1
    line = jnp.concatenate([vector, jnp.zeros((width - taps_len,), vector.dtype)])
    return jnp.tile(line, block)[: block * rows].reshape(block, rows)


def band_matrix(filt, block, rows):
    real_band = toeplitz_rows(filt[0], block, rows).T
    imag_band = toeplitz_rows(filt[1], block, rows).T
    upper = jnp.concatenate([real_band, imag_band], axis=1)
    lower = jnp.concatenate([-imag_band, real_band], axis=1)
    return jnp.concatenate([upper, lower], axis=0)


def compress(wide, filt, blocks):
    parts, count, length = wide.shape
    taps_len = filt.shape[1]
    reach = -(-(BLOCK + taps_len - 1) // BLOCK)
    rows = reach * BLOCK
    cut = wide.reshape(parts, count, length // BLOCK, BLOCK)
    window = jnp.concatenate([cut[:, :, c : c + blocks] for c in range(reach)], axis=3)
    segments = jnp.concatenate([window[0], window[1]], axis=2)
    product = lax.dot_general(
        segments,
        band_matrix(filt, BLOCK, rows),
        (((2,), (0,)), ((), ())),
        preferred_element_type=jnp.float32,
    )
    real_part = product[:, :, :BLOCK].reshape(count, blocks * BLOCK)
    imag_part = product[:, :, BLOCK:].reshape(count, blocks * BLOCK)
    return jnp.stack([real_part, imag_part])


def side_term(kid, taps, weights, shifts, angles):
    length = kid.shape[3]
    span = length - MARGIN
    inner = span + MAXOFF - 1
    interp = jnp.zeros(kid.shape[:3] + (inner,), jnp.float32)
    for tap in range(TAPS):
        interp = interp + weights[tap] * lax.dynamic_slice_in_dim(kid, taps[tap], inner, axis=3)
    wider = interp[:, :, None, :, :]
    moved = jnp.broadcast_to(wider[..., 0:span], interp.shape[:2] + shifts.shape + (span,))
    for offset in range(1, MAXOFF):
        chosen = (shifts == offset)[None, None, :, :, None]
        moved = jnp.where(chosen, wider[..., offset : offset + span], moved)
    cosine = jnp.cos(angles)[None, :, :, None]
    sine = jnp.sin(angles)[None, :, :, None]
    real_part = cosine * moved[0] - sine * moved[1]
    imag_part = sine * moved[0] + cosine * moved[1]
    return jnp.stack([real_part, imag_part])


def merge_section(child, taps, weights, shifts, angles):
    parts, count, beams, length = child.shape
    pairs = child.reshape(parts, count // 2, 2, beams, length)
    first = side_term(
        pairs[:, :, 0],
        taps[0],
        weights[0],
        shifts[0].reshape(2, beams),
        angles[0].reshape(2, beams),
    )
    second = side_term(
        pairs[:, :, 1],
        taps[1],
        weights[1],
        shifts[1].reshape(2, beams),
        angles[1].reshape(2, beams),
    )
    merged = (first + second) * half_root
    return merged.reshape(parts, count // 2, 2 * beams, length - MARGIN)


def on_device(raw, filt, tap_index, tap_weight, beam_shift, beam_phase):
    pulse_count = lax.axis_size("pulse")
    parts, local_beams, bins = raw.shape
    taps_len = filt.shape[1]
    local_sections = local_beams.bit_length() - 1
    cross_sections = pulse_count.bit_length() - 1
    sections = local_sections + cross_sections
    extra = sections * MARGIN
    blocks = -(-(bins + extra) // BLOCK)
    reach = -(-(BLOCK + taps_len - 1) // BLOCK)
    rim_len = (blocks + reach - 1) * BLOCK - bins
    rim = shifted(raw[:, :, :rim_len], "range", -1)
    wide = jnp.concatenate([raw, rim], axis=2)
    level = compress(wide, filt, blocks)[:, :, None, : bins + extra]
    for section in range(local_sections):
        beams = 1 << section
        start = 2 * beams - 2
        level = merge_section(
            level,
            tap_index[section],
            tap_weight[section],
            beam_shift[:, start : start + 2 * beams],
            beam_phase[:, start : start + 2 * beams],
        )
    piece_bins = bins // pulse_count
    need = cross_sections * MARGIN
    flat = level.reshape(parts, local_beams, level.shape[3])[:, :, : bins + need]
    flat = jnp.pad(flat, ((0, 0), (0, 0), (0, piece_bins - need)))
    head = flat[:, :, :bins].reshape(parts, local_beams, pulse_count, piece_bins)
    tail = flat[:, :, piece_bins:].reshape(parts, local_beams, pulse_count, piece_bins)[
        :, :, :, :need
    ]
    pieces = jnp.transpose(jnp.concatenate([head, tail], axis=3), (0, 2, 1, 3))
    level = lax.all_to_all(pieces, "pulse", split_axis=1, concat_axis=1, tiled=True)
    for bit in range(cross_sections):
        section = local_sections + bit
        beams = local_beams << bit
        start = 2 * beams - 2
        level = merge_section(
            level,
            tap_index[section],
            tap_weight[section],
            beam_shift[:, start : start + 2 * beams],
            beam_phase[:, start : start + 2 * beams],
        )
    level = level.reshape(parts, pulse_count, local_beams, piece_bins)
    level = lax.all_to_all(level, "pulse", split_axis=1, concat_axis=3, tiled=True)
    return level.reshape(parts, local_beams, bins)


def solution(mesh):
    return jax.shard_map(
        on_device,
        mesh=mesh,
        in_specs=(P(None, "pulse", "range"), P(), P(), P(), P(), P()),
        out_specs=P(None, "pulse", "range"),
        check_vma=False,
    )
```

```python
import jax
import jax.numpy as jnp
from jax import lax
from jax.sharding import PartitionSpec as P

TAPS = 4
MAXOFF = 8
MARGIN = 15
BLOCK = 256


half_root = 0.7071067811865476


def shifted(shard, axis, by):
    count = lax.axis_size(axis)
    pairs = [(i, i + by) for i in range(count) if 0 <= i + by < count]
    return lax.ppermute(shard, axis, pairs)


def toeplitz_rows(vector, block, rows):
    taps_len = vector.shape[0]
    width = rows + 1
    line = jnp.concatenate([vector, jnp.zeros((width - taps_len,), vector.dtype)])
    return jnp.tile(line, block)[: block * rows].reshape(block, rows)


def band_matrix(filt, block, rows):
    real_band = toeplitz_rows(filt[0], block, rows).T
    imag_band = toeplitz_rows(filt[1], block, rows).T
    upper = jnp.concatenate([real_band, imag_band], axis=1)
    lower = jnp.concatenate([-imag_band, real_band], axis=1)
    return jnp.concatenate([upper, lower], axis=0)


def compress(wide, filt, blocks):
    parts, count, length = wide.shape
    taps_len = filt.shape[1]
    reach = -(-(BLOCK + taps_len - 1) // BLOCK)
    rows = reach * BLOCK
    cut = wide.reshape(parts, count, length // BLOCK, BLOCK)
    window = jnp.concatenate([cut[:, :, c : c + blocks] for c in range(reach)], axis=3)
    segments = jnp.concatenate([window[0], window[1]], axis=2)
    product = lax.dot_general(
        segments,
        band_matrix(filt, BLOCK, rows),
        (((2,), (0,)), ((), ())),
        preferred_element_type=jnp.float32,
    )
    real_part = product[:, :, :BLOCK].reshape(count, blocks * BLOCK)
    imag_part = product[:, :, BLOCK:].reshape(count, blocks * BLOCK)
    return jnp.stack([real_part, imag_part])


def side_term(kid, weights, chosen, cosine, sine):
    length = kid.shape[3]
    span = length - MARGIN
    inner = span + MAXOFF - 1
    reach = MARGIN - MAXOFF + 1
    interp = weights[0] * kid[..., 0:inner]
    for offset in range(1, reach):
        interp = interp + weights[offset] * kid[..., offset : offset + inner]
    wider = interp[:, :, None, :, :]
    moved = jnp.broadcast_to(wider[..., 0:span], interp.shape[:2] + chosen.shape[1:] + (span,))
    for offset in range(1, MAXOFF):
        moved = jnp.where(chosen[offset][None, None, :, :, None], wider[..., offset : offset + span], moved)
    cosine = cosine[None, :, :, None]
    sine = sine[None, :, :, None]
    real_part = cosine * moved[0] - sine * moved[1]
    imag_part = sine * moved[0] + cosine * moved[1]
    return jnp.stack([real_part, imag_part])


def tap_weights(taps, weights):
    reach = MARGIN - MAXOFF + 1
    hit = taps[..., :, None] == jnp.arange(reach, dtype=taps.dtype)
    return jnp.sum(jnp.where(hit, weights[..., :, None], 0.0), axis=-2)


def merge_section(child, weights, chosen, cosine, sine):
    parts, count, beams, length = child.shape
    pairs = child.reshape(parts, count // 2, 2, beams, length)
    terms = [
        side_term(
            pairs[:, :, c],
            weights[c],
            chosen[:, c].reshape(MAXOFF, 2, beams),
            cosine[c].reshape(2, beams),
            sine[c].reshape(2, beams),
        )
        for c in range(2)
    ]
    merged = (terms[0] + terms[1]) * half_root
    return merged.reshape(parts, count // 2, 2 * beams, length - MARGIN)


def on_device(raw, filt, tap_index, tap_weight, beam_shift, beam_phase):
    pulse_count = lax.axis_size("pulse")
    parts, local_beams, bins = raw.shape
    taps_len = filt.shape[1]
    local_sections = local_beams.bit_length() - 1
    cross_sections = pulse_count.bit_length() - 1
    sections = local_sections + cross_sections
    extra = sections * MARGIN
    blocks = -(-(bins + extra) // BLOCK)
    reach = -(-(BLOCK + taps_len - 1) // BLOCK)
    rim_len = (blocks + reach - 1) * BLOCK - bins
    rim = shifted(raw[:, :, :rim_len], "range", -1)
    wide = jnp.concatenate([raw, rim], axis=2)
    level = compress(wide, filt, blocks)[:, :, None, : bins + extra]
    all_weights = tap_weights(tap_index, tap_weight)
    all_chosen = beam_shift[None] == jnp.arange(MAXOFF, dtype=beam_shift.dtype)[:, None, None]
    all_cos = jnp.cos(beam_phase)
    all_sin = jnp.sin(beam_phase)

    def run_section(level, section, beams):
        start = 2 * beams - 2
        stop = start + 2 * beams
        return merge_section(
            level,
            all_weights[section],
            all_chosen[:, :, start:stop],
            all_cos[:, start:stop],
            all_sin[:, start:stop],
        )

    for section in range(local_sections):
        level = run_section(level, section, 1 << section)
    piece_bins = bins // pulse_count
    need = cross_sections * MARGIN
    flat = level.reshape(parts, local_beams, level.shape[3])[:, :, : bins + need]
    flat = jnp.pad(flat, ((0, 0), (0, 0), (0, piece_bins - need)))
    head = flat[:, :, :bins].reshape(parts, local_beams, pulse_count, piece_bins)
    tail = flat[:, :, piece_bins:].reshape(parts, local_beams, pulse_count, piece_bins)[
        :, :, :, :need
    ]
    pieces = jnp.transpose(jnp.concatenate([head, tail], axis=3), (0, 2, 1, 3))
    level = lax.all_to_all(pieces, "pulse", split_axis=1, concat_axis=1, tiled=True)
    for bit in range(cross_sections):
        section = local_sections + bit
        level = run_section(level, section, local_beams << bit)
    level = level.reshape(parts, pulse_count, local_beams, piece_bins)
    level = lax.all_to_all(level, "pulse", split_axis=1, concat_axis=3, tiled=True)
    return level.reshape(parts, local_beams, bins)


def solution(mesh):
    return jax.shard_map(
        on_device,
        mesh=mesh,
        in_specs=(P(None, "pulse", "range"), P(), P(), P(), P(), P()),
        out_specs=P(None, "pulse", "range"),
        check_vma=False,
    )
```

```python
import jax
import jax.numpy as jnp
from jax import lax
from jax.sharding import PartitionSpec as P

TAPS = 4
MAXOFF = 8
MARGIN = 15
BLOCK = 256


half_root = 0.7071067811865476


def shifted(shard, axis, by):
    count = lax.axis_size(axis)
    pairs = [(i, i + by) for i in range(count) if 0 <= i + by < count]
    return lax.ppermute(shard, axis, pairs)


def toeplitz_rows(vector, block, rows):
    taps_len = vector.shape[0]
    width = rows + 1
    line = jnp.concatenate([vector, jnp.zeros((width - taps_len,), vector.dtype)])
    return jnp.tile(line, block)[: block * rows].reshape(block, rows)


def band_matrix(filt, block, rows):
    real_band = toeplitz_rows(filt[0], block, rows).T
    imag_band = toeplitz_rows(filt[1], block, rows).T
    upper = jnp.concatenate([real_band, imag_band], axis=1)
    lower = jnp.concatenate([-imag_band, real_band], axis=1)
    return jnp.concatenate([upper, lower], axis=0)


def compress(wide, filt, blocks):
    parts, count, length = wide.shape
    taps_len = filt.shape[1]
    reach = -(-(BLOCK + taps_len - 1) // BLOCK)
    rows = reach * BLOCK
    cut = wide.reshape(parts, count, length // BLOCK, BLOCK)
    window = jnp.concatenate([cut[:, :, c : c + blocks] for c in range(reach)], axis=3)
    segments = jnp.concatenate([window[0], window[1]], axis=2)
    product = lax.dot_general(
        segments,
        band_matrix(filt, BLOCK, rows),
        (((2,), (0,)), ((), ())),
        preferred_element_type=jnp.float32,
    )
    real_part = product[:, :, :BLOCK].reshape(count, blocks * BLOCK)
    imag_part = product[:, :, BLOCK:].reshape(count, blocks * BLOCK)
    return jnp.stack([real_part, imag_part])


def side_term(kid, weights, chosen, cosine, sine):
    length = kid[0].shape[-1]
    span = length - MARGIN
    inner = span + MAXOFF - 1
    reach = MARGIN - MAXOFF + 1
    interp = []
    for part in kid:
        total = weights[0] * part[..., 0:inner]
        for offset in range(1, reach):
            total = total + weights[offset] * part[..., offset : offset + inner]
        interp.append(total)
    terms = []
    for half in range(2):
        moved = []
        for part in interp:
            pick = part[..., 0:span]
            for offset in range(1, MAXOFF):
                pick = jnp.where(chosen[half, offset][:, None], part[..., offset : offset + span], pick)
            moved.append(pick)
        cos_row = cosine[half][:, None]
        sin_row = sine[half][:, None]
        real_part = cos_row * moved[0] - sin_row * moved[1]
        imag_part = sin_row * moved[0] + cos_row * moved[1]
        terms.append((real_part, imag_part))
    return terms


def tap_weights(taps, weights):
    reach = MARGIN - MAXOFF + 1
    hit = taps[..., :, None] == jnp.arange(reach, dtype=taps.dtype)
    return jnp.sum(jnp.where(hit, weights[..., :, None], 0.0), axis=-2)


def per_row(table, groups):
    beams = table.shape[-1] // 2
    halves = table.reshape(table.shape[:-1] + (2, beams))
    return jnp.tile(halves, (1,) * (halves.ndim - 1) + (groups,))


def merge_section(level, beams, weights, chosen, cosine, sine):
    rows, length = level[0].shape
    groups = rows // (2 * beams)
    span = length - MARGIN
    chosen_rows = per_row(chosen, groups)
    cos_rows = per_row(cosine, groups)
    sin_rows = per_row(sine, groups)
    terms = []
    for c in range(2):
        kid = [part.reshape(groups, 2, beams, length)[:, c].reshape(rows // 2, length) for part in level]
        terms.append(
            side_term(kid, weights[c], jnp.moveaxis(chosen_rows[:, c], 0, 1), cos_rows[c], sin_rows[c])
        )
    merged = []
    for p in range(2):
        halves = [((terms[0][h][p] + terms[1][h][p]) * half_root).reshape(groups, beams, span) for h in range(2)]
        merged.append(jnp.stack(halves, axis=1).reshape(rows, span))
    return tuple(merged)


def on_device(raw, filt, tap_index, tap_weight, beam_shift, beam_phase):
    pulse_count = lax.axis_size("pulse")
    parts, local_beams, bins = raw.shape
    taps_len = filt.shape[1]
    local_sections = local_beams.bit_length() - 1
    cross_sections = pulse_count.bit_length() - 1
    sections = local_sections + cross_sections
    extra = sections * MARGIN
    blocks = -(-(bins + extra) // BLOCK)
    reach = -(-(BLOCK + taps_len - 1) // BLOCK)
    rim_len = (blocks + reach - 1) * BLOCK - bins
    rim = shifted(raw[:, :, :rim_len], "range", -1)
    wide = jnp.concatenate([raw, rim], axis=2)
    level = compress(wide, filt, blocks)[:, :, : bins + extra]
    level = (level[0], level[1])
    all_weights = tap_weights(tap_index, tap_weight)
    all_chosen = beam_shift[None] == jnp.arange(MAXOFF, dtype=beam_shift.dtype)[:, None, None]
    all_cos = jnp.cos(beam_phase)
    all_sin = jnp.sin(beam_phase)

    def run_section(level, section, beams):
        start = 2 * beams - 2
        stop = start + 2 * beams
        return merge_section(
            level,
            beams,
            all_weights[section],
            all_chosen[:, :, start:stop],
            all_cos[:, start:stop],
            all_sin[:, start:stop],
        )

    for section in range(local_sections):
        level = run_section(level, section, 1 << section)
    piece_bins = bins // pulse_count
    need = cross_sections * MARGIN
    flat = jnp.stack(level)[:, :, : bins + need]
    flat = jnp.pad(flat, ((0, 0), (0, 0), (0, piece_bins - need)))
    head = flat[:, :, :bins].reshape(parts, local_beams, pulse_count, piece_bins)
    tail = flat[:, :, piece_bins:].reshape(parts, local_beams, pulse_count, piece_bins)[
        :, :, :, :need
    ]
    pieces = jnp.transpose(jnp.concatenate([head, tail], axis=3), (0, 2, 1, 3))
    level = lax.all_to_all(pieces, "pulse", split_axis=1, concat_axis=1, tiled=True)
    level = level.reshape(parts, pulse_count * local_beams, piece_bins + need)
    level = (level[0], level[1])
    for bit in range(cross_sections):
        section = local_sections + bit
        level = run_section(level, section, local_beams << bit)
    level = jnp.stack(level).reshape(parts, pulse_count, local_beams, piece_bins)
    level = lax.all_to_all(level, "pulse", split_axis=1, concat_axis=3, tiled=True)
    return level.reshape(parts, local_beams, bins)


def solution(mesh):
    return jax.shard_map(
        on_device,
        mesh=mesh,
        in_specs=(P(None, "pulse", "range"), P(), P(), P(), P(), P()),
        out_specs=P(None, "pulse", "range"),
        check_vma=False,
    )
```

```python
import jax
import jax.numpy as jnp
from jax import lax
from jax.sharding import PartitionSpec as P

TAPS = 4
MAXOFF = 8
MARGIN = 15
BLOCK = 256


half_root = 0.7071067811865476


def shifted(shard, axis, by):
    count = lax.axis_size(axis)
    pairs = [(i, i + by) for i in range(count) if 0 <= i + by < count]
    return lax.ppermute(shard, axis, pairs)


def toeplitz_rows(vector, block, rows):
    taps_len = vector.shape[0]
    width = rows + 1
    line = jnp.concatenate([vector, jnp.zeros((width - taps_len,), vector.dtype)])
    return jnp.tile(line, block)[: block * rows].reshape(block, rows)


def band_matrix(filt, block, rows):
    real_band = toeplitz_rows(filt[0], block, rows).T
    imag_band = toeplitz_rows(filt[1], block, rows).T
    upper = jnp.concatenate([real_band, imag_band], axis=1)
    lower = jnp.concatenate([-imag_band, real_band], axis=1)
    return jnp.concatenate([upper, lower], axis=0)


def compress(wide, filt, blocks):
    parts, count, length = wide.shape
    taps_len = filt.shape[1]
    reach = -(-(BLOCK + taps_len - 1) // BLOCK)
    rows = reach * BLOCK
    cut = wide.reshape(parts, count, length // BLOCK, BLOCK)
    window = jnp.concatenate([cut[:, :, c : c + blocks] for c in range(reach)], axis=3)
    segments = jnp.concatenate([window[0], window[1]], axis=2)
    product = lax.dot_general(
        segments,
        band_matrix(filt, BLOCK, rows),
        (((2,), (0,)), ((), ())),
        preferred_element_type=jnp.float32,
    )
    real_part = product[:, :, :BLOCK].reshape(count, blocks * BLOCK)
    imag_part = product[:, :, BLOCK:].reshape(count, blocks * BLOCK)
    return jnp.stack([real_part, imag_part])


def side_term(kid, weights, chosen, cosine, sine):
    length = kid[0].shape[-1]
    span = length - MARGIN
    inner = span + MAXOFF - 1
    reach = MARGIN - MAXOFF + 1
    interp = []
    for part in kid:
        total = weights[0] * part[..., 0:inner]
        for offset in range(1, reach):
            total = total + weights[offset] * part[..., offset : offset + inner]
        interp.append(total)
    interp = lax.optimization_barrier(interp)
    terms = []
    for half in range(2):
        moved = []
        for part in interp:
            pick = part[..., 0:span]
            for offset in range(1, MAXOFF):
                pick = jnp.where(chosen[half, offset][:, None], part[..., offset : offset + span], pick)
            moved.append(pick)
        cos_row = cosine[half][:, None]
        sin_row = sine[half][:, None]
        real_part = cos_row * moved[0] - sin_row * moved[1]
        imag_part = sin_row * moved[0] + cos_row * moved[1]
        terms.append((real_part, imag_part))
    return terms


def tap_weights(taps, weights):
    reach = MARGIN - MAXOFF + 1
    hit = taps[..., :, None] == jnp.arange(reach, dtype=taps.dtype)
    return jnp.sum(jnp.where(hit, weights[..., :, None], 0.0), axis=-2)


def per_row(table, groups):
    beams = table.shape[-1] // 2
    halves = table.reshape(table.shape[:-1] + (2, beams))
    return jnp.tile(halves, (1,) * (halves.ndim - 1) + (groups,))


def merge_section(level, beams, weights, chosen, cosine, sine):
    rows, length = level[0].shape
    groups = rows // (2 * beams)
    span = length - MARGIN
    chosen_rows = per_row(chosen, groups)
    cos_rows = per_row(cosine, groups)
    sin_rows = per_row(sine, groups)
    terms = []
    for c in range(2):
        kid = [part.reshape(groups, 2, beams, length)[:, c].reshape(rows // 2, length) for part in level]
        terms.append(
            side_term(kid, weights[c], jnp.moveaxis(chosen_rows[:, c], 0, 1), cos_rows[c], sin_rows[c])
        )
    merged = []
    for p in range(2):
        halves = [((terms[0][h][p] + terms[1][h][p]) * half_root).reshape(groups, beams, span) for h in range(2)]
        merged.append(jnp.stack(halves, axis=1).reshape(rows, span))
    return tuple(merged)


def on_device(raw, filt, tap_index, tap_weight, beam_shift, beam_phase):
    pulse_count = lax.axis_size("pulse")
    parts, local_beams, bins = raw.shape
    taps_len = filt.shape[1]
    local_sections = local_beams.bit_length() - 1
    cross_sections = pulse_count.bit_length() - 1
    sections = local_sections + cross_sections
    extra = sections * MARGIN
    blocks = -(-(bins + extra) // BLOCK)
    reach = -(-(BLOCK + taps_len - 1) // BLOCK)
    rim_len = (blocks + reach - 1) * BLOCK - bins
    rim = shifted(raw[:, :, :rim_len], "range", -1)
    wide = jnp.concatenate([raw, rim], axis=2)
    level = compress(wide, filt, blocks)[:, :, : bins + extra]
    level = (level[0], level[1])
    all_weights = tap_weights(tap_index, tap_weight)
    all_chosen = beam_shift[None] == jnp.arange(MAXOFF, dtype=beam_shift.dtype)[:, None, None]
    all_cos = jnp.cos(beam_phase)
    all_sin = jnp.sin(beam_phase)

    def run_section(level, section, beams):
        start = 2 * beams - 2
        stop = start + 2 * beams
        return merge_section(
            level,
            beams,
            all_weights[section],
            all_chosen[:, :, start:stop],
            all_cos[:, start:stop],
            all_sin[:, start:stop],
        )

    for section in range(local_sections):
        level = run_section(level, section, 1 << section)
    piece_bins = bins // pulse_count
    need = cross_sections * MARGIN
    flat = jnp.stack(level)[:, :, : bins + need]
    flat = jnp.pad(flat, ((0, 0), (0, 0), (0, piece_bins - need)))
    head = flat[:, :, :bins].reshape(parts, local_beams, pulse_count, piece_bins)
    tail = flat[:, :, piece_bins:].reshape(parts, local_beams, pulse_count, piece_bins)[
        :, :, :, :need
    ]
    pieces = jnp.transpose(jnp.concatenate([head, tail], axis=3), (0, 2, 1, 3))
    level = lax.all_to_all(pieces, "pulse", split_axis=1, concat_axis=1, tiled=True)
    level = level.reshape(parts, pulse_count * local_beams, piece_bins + need)
    level = (level[0], level[1])
    for bit in range(cross_sections):
        section = local_sections + bit
        level = run_section(level, section, local_beams << bit)
    level = jnp.stack(level).reshape(parts, pulse_count, local_beams, piece_bins)
    level = lax.all_to_all(level, "pulse", split_axis=1, concat_axis=3, tiled=True)
    return level.reshape(parts, local_beams, bins)


def solution(mesh):
    return jax.shard_map(
        on_device,
        mesh=mesh,
        in_specs=(P(None, "pulse", "range"), P(), P(), P(), P(), P()),
        out_specs=P(None, "pulse", "range"),
        check_vma=False,
    )
```

```python
import jax
import jax.numpy as jnp
from jax import lax
from jax.sharding import PartitionSpec as P
from jax.experimental import pallas as pl
from jax.experimental.pallas import tpu as pltpu

TAPS = 4
MAXOFF = 8
MARGIN = 15
BLOCK = 256
LANE = 128


half_root = 0.7071067811865476


def shifted(shard, axis, by):
    count = lax.axis_size(axis)
    pairs = [(i, i + by) for i in range(count) if 0 <= i + by < count]
    return lax.ppermute(shard, axis, pairs)


def toeplitz_rows(vector, block, rows):
    taps_len = vector.shape[0]
    width = rows + 1
    line = jnp.concatenate([vector, jnp.zeros((width - taps_len,), vector.dtype)])
    return jnp.tile(line, block)[: block * rows].reshape(block, rows)


def band_matrix(filt, block, rows):
    real_band = toeplitz_rows(filt[0], block, rows).T
    imag_band = toeplitz_rows(filt[1], block, rows).T
    upper = jnp.concatenate([real_band, imag_band], axis=1)
    lower = jnp.concatenate([-imag_band, real_band], axis=1)
    return jnp.concatenate([upper, lower], axis=0)


def compress(wide, filt, blocks):
    parts, count, length = wide.shape
    taps_len = filt.shape[1]
    reach = -(-(BLOCK + taps_len - 1) // BLOCK)
    rows = reach * BLOCK
    cut = wide.reshape(parts, count, length // BLOCK, BLOCK)
    window = jnp.concatenate([cut[:, :, c : c + blocks] for c in range(reach)], axis=3)
    segments = jnp.concatenate([window[0], window[1]], axis=2)
    product = lax.dot_general(
        segments,
        band_matrix(filt, BLOCK, rows),
        (((2,), (0,)), ((), ())),
        preferred_element_type=jnp.float32,
    )
    real_part = product[:, :, :BLOCK].reshape(count, blocks * BLOCK)
    imag_part = product[:, :, BLOCK:].reshape(count, blocks * BLOCK)
    return jnp.stack([real_part, imag_part])


def merge_kernel(weight_ref, kid_ref, shift_ref, cos_ref, sin_ref, out_ref):
    length = kid_ref.shape[-1]
    reach = MARGIN - MAXOFF + 1
    acc = [[None, None], [None, None]]
    for c in range(2):
        interp = []
        for part in range(2):
            x = kid_ref[c, part]
            total = weight_ref[c, 0] * x
            for offset in range(1, reach):
                total = total + weight_ref[c, offset] * pltpu.roll(x, length - offset, 1)
            interp.append(total)
        rolled = [[p] + [pltpu.roll(p, length - offset, 1) for offset in range(1, MAXOFF)] for p in interp]
        for half in range(2):
            shift = shift_ref[c, half]
            moved = []
            for part in range(2):
                pick = rolled[part][0]
                for offset in range(1, MAXOFF):
                    pick = jnp.where(shift == offset, rolled[part][offset], pick)
                moved.append(pick)
            cos_row = cos_ref[c, half]
            sin_row = sin_ref[c, half]
            real_part = cos_row * moved[0] - sin_row * moved[1]
            imag_part = sin_row * moved[0] + cos_row * moved[1]
            if c == 0:
                acc[half] = [real_part, imag_part]
            else:
                acc[half] = [acc[half][0] + real_part, acc[half][1] + imag_part]
    for half in range(2):
        for part in range(2):
            out_ref[half, part] = acc[half][part] * half_root


def merge_call(weights, kids, shifts, cosines, sines):
    _, _, rows, length = kids.shape
    vmem = pltpu.VMEM
    elems = 2 * 2 * rows * length
    return pl.pallas_call(
        merge_kernel,
        out_shape=jax.ShapeDtypeStruct((2, 2, rows, length), jnp.float32),
        in_specs=[
            pl.BlockSpec(memory_space=pltpu.SMEM),
            pl.BlockSpec(memory_space=vmem),
            pl.BlockSpec(memory_space=vmem),
            pl.BlockSpec(memory_space=vmem),
            pl.BlockSpec(memory_space=vmem),
        ],
        out_specs=pl.BlockSpec(memory_space=vmem),
        cost_estimate=pl.CostEstimate(flops=60 * elems, transcendentals=0, bytes_accessed=8 * elems),
    )(weights, kids, shifts, cosines, sines)


def tap_weights(taps, weights):
    reach = MARGIN - MAXOFF + 1
    hit = taps[..., :, None] == jnp.arange(reach, dtype=taps.dtype)
    return jnp.sum(jnp.where(hit, weights[..., :, None], 0.0), axis=-2)


def per_row(table, groups):
    beams = table.shape[-1] // 2
    halves = table.reshape(table.shape[:-1] + (2, beams))
    return jnp.tile(halves, (1,) * (halves.ndim - 1) + (groups,))


def merge_section(level, beams, weights, chosen, cosine, sine):
    parts, rows, length = level.shape
    groups = rows // (2 * beams)
    pairs = level.reshape(parts, groups, 2, beams, length)
    kids = jnp.stack([pairs[:, :, c].reshape(parts, rows // 2, length) for c in range(2)])
    shifts = per_row(chosen, groups)[..., None]
    cosines = per_row(cosine, groups)[..., None]
    sines = per_row(sine, groups)[..., None]
    out = merge_call(weights, kids, shifts, cosines, sines)
    merged = jnp.stack([out[h].reshape(parts, groups, beams, length) for h in range(2)], axis=2)
    return merged.reshape(parts, rows, length)


def padded_lanes(level, width):
    length = level.shape[-1]
    target = -(-width // LANE) * LANE
    if target > length:
        return jnp.pad(level, ((0, 0), (0, 0), (0, target - length)))
    return level[..., :target]


def on_device(raw, filt, tap_index, tap_weight, beam_shift, beam_phase):
    pulse_count = lax.axis_size("pulse")
    parts, local_beams, bins = raw.shape
    taps_len = filt.shape[1]
    local_sections = local_beams.bit_length() - 1
    cross_sections = pulse_count.bit_length() - 1
    sections = local_sections + cross_sections
    extra = sections * MARGIN
    blocks = -(-(bins + extra) // BLOCK)
    reach = -(-(BLOCK + taps_len - 1) // BLOCK)
    rim_len = (blocks + reach - 1) * BLOCK - bins
    rim = shifted(raw[:, :, :rim_len], "range", -1)
    wide = jnp.concatenate([raw, rim], axis=2)
    level = padded_lanes(compress(wide, filt, blocks), bins + extra)
    all_weights = tap_weights(tap_index, tap_weight)
    all_cos = jnp.cos(beam_phase)
    all_sin = jnp.sin(beam_phase)

    def run_section(level, section, beams):
        start = 2 * beams - 2
        stop = start + 2 * beams
        return merge_section(
            level,
            beams,
            all_weights[section],
            beam_shift[:, start:stop],
            all_cos[:, start:stop],
            all_sin[:, start:stop],
        )

    for section in range(local_sections):
        level = run_section(level, section, 1 << section)
    piece_bins = bins // pulse_count
    need = cross_sections * MARGIN
    flat = level[:, :, : bins + need]
    flat = jnp.pad(flat, ((0, 0), (0, 0), (0, piece_bins - need)))
    head = flat[:, :, :bins].reshape(parts, local_beams, pulse_count, piece_bins)
    tail = flat[:, :, piece_bins:].reshape(parts, local_beams, pulse_count, piece_bins)[
        :, :, :, :need
    ]
    pieces = jnp.transpose(jnp.concatenate([head, tail], axis=3), (0, 2, 1, 3))
    level = lax.all_to_all(pieces, "pulse", split_axis=1, concat_axis=1, tiled=True)
    level = padded_lanes(level.reshape(parts, pulse_count * local_beams, piece_bins + need), piece_bins + need)
    for bit in range(cross_sections):
        section = local_sections + bit
        level = run_section(level, section, local_beams << bit)
    level = level[..., :piece_bins].reshape(parts, pulse_count, local_beams, piece_bins)
    level = lax.all_to_all(level, "pulse", split_axis=1, concat_axis=3, tiled=True)
    return level.reshape(parts, local_beams, bins)


def solution(mesh):
    return jax.shard_map(
        on_device,
        mesh=mesh,
        in_specs=(P(None, "pulse", "range"), P(), P(), P(), P(), P()),
        out_specs=P(None, "pulse", "range"),
        check_vma=False,
    )
```

```python
import jax
import jax.numpy as jnp
from jax import lax
from jax.sharding import PartitionSpec as P
from jax.experimental import pallas as pl
from jax.experimental.pallas import tpu as pltpu

TAPS = 4
MAXOFF = 8
MARGIN = 15
BLOCK = 256
LANE = 128


half_root = 0.7071067811865476


def shifted(shard, axis, by):
    count = lax.axis_size(axis)
    pairs = [(i, i + by) for i in range(count) if 0 <= i + by < count]
    return lax.ppermute(shard, axis, pairs)


def toeplitz_rows(vector, block, rows):
    taps_len = vector.shape[0]
    width = rows + 1
    line = jnp.concatenate([vector, jnp.zeros((width - taps_len,), vector.dtype)])
    return jnp.tile(line, block)[: block * rows].reshape(block, rows)


def band_matrix(filt, block, rows):
    real_band = toeplitz_rows(filt[0], block, rows).T
    imag_band = toeplitz_rows(filt[1], block, rows).T
    upper = jnp.concatenate([real_band, imag_band], axis=1)
    lower = jnp.concatenate([-imag_band, real_band], axis=1)
    return jnp.concatenate([upper, lower], axis=0)


def compress(wide, filt, blocks):
    parts, count, length = wide.shape
    taps_len = filt.shape[1]
    reach = -(-(BLOCK + taps_len - 1) // BLOCK)
    rows = reach * BLOCK
    cut = wide.reshape(parts, count, length // BLOCK, BLOCK)
    window = jnp.concatenate([cut[:, :, c : c + blocks] for c in range(reach)], axis=3)
    segments = jnp.concatenate([window[0], window[1]], axis=2)
    product = lax.dot_general(
        segments,
        band_matrix(filt, BLOCK, rows),
        (((2,), (0,)), ((), ())),
        preferred_element_type=jnp.float32,
    )
    real_part = product[:, :, :BLOCK].reshape(count, blocks * BLOCK)
    imag_part = product[:, :, BLOCK:].reshape(count, blocks * BLOCK)
    return jnp.stack([real_part, imag_part])


def merge_kernel(weight_ref, kid_ref, table_ref, out_ref):
    length = kid_ref.shape[-1]
    reach = MARGIN - MAXOFF + 1
    acc = [[None, None], [None, None]]
    for c in range(2):
        interp = []
        for part in range(2):
            x = kid_ref[c, part]
            total = weight_ref[c, 0] * x
            for offset in range(1, reach):
                total = total + weight_ref[c, offset] * pltpu.roll(x, length - offset, 1)
            interp.append(total)
        rolled = [[p] + [pltpu.roll(p, length - offset, 1) for offset in range(1, MAXOFF)] for p in interp]
        for half in range(2):
            shift = table_ref[0, c, half][:, 0:1]
            moved = []
            for part in range(2):
                pick = rolled[part][0]
                for offset in range(1, MAXOFF):
                    pick = jnp.where(shift == float(offset), rolled[part][offset], pick)
                moved.append(pick)
            cos_row = table_ref[1, c, half][:, 0:1]
            sin_row = table_ref[2, c, half][:, 0:1]
            real_part = cos_row * moved[0] - sin_row * moved[1]
            imag_part = sin_row * moved[0] + cos_row * moved[1]
            if c == 0:
                acc[half] = [real_part, imag_part]
            else:
                acc[half] = [acc[half][0] + real_part, acc[half][1] + imag_part]
    for half in range(2):
        for part in range(2):
            out_ref[half, part] = acc[half][part] * half_root


def merge_call(weights, kids, table):
    _, _, rows, length = kids.shape
    vmem = pltpu.VMEM
    elems = 2 * 2 * rows * length
    return pl.pallas_call(
        merge_kernel,
        out_shape=jax.ShapeDtypeStruct((2, 2, rows, length), jnp.float32),
        in_specs=[
            pl.BlockSpec(memory_space=pltpu.SMEM),
            pl.BlockSpec(memory_space=vmem),
            pl.BlockSpec(memory_space=vmem),
        ],
        out_specs=pl.BlockSpec(memory_space=vmem),
        cost_estimate=pl.CostEstimate(flops=60 * elems, transcendentals=0, bytes_accessed=8 * elems),
    )(weights, kids, table)


def tap_weights(taps, weights):
    reach = MARGIN - MAXOFF + 1
    hit = taps[..., :, None] == jnp.arange(reach, dtype=taps.dtype)
    return jnp.sum(jnp.where(hit, weights[..., :, None], 0.0), axis=-2)


def per_row(table, groups):
    beams = table.shape[-1] // 2
    halves = table.reshape(table.shape[:-1] + (2, beams))
    return jnp.tile(halves, (1,) * (halves.ndim - 1) + (groups,))


def merge_section(level, beams, weights, chosen, cosine, sine):
    parts, rows, length = level.shape
    groups = rows // (2 * beams)
    pairs = level.reshape(parts, groups, 2, beams, length)
    kids = jnp.stack([pairs[:, :, c].reshape(parts, rows // 2, length) for c in range(2)])
    packed = jnp.stack([chosen.astype(jnp.float32), cosine, sine])
    table = jnp.broadcast_to(per_row(packed, groups)[..., None], (3, 2, 2, rows // 2, LANE))
    out = merge_call(weights, kids, table)
    merged = jnp.stack([out[h].reshape(parts, groups, beams, length) for h in range(2)], axis=2)
    return merged.reshape(parts, rows, length)


def padded_lanes(level, width):
    length = level.shape[-1]
    target = -(-width // LANE) * LANE
    if target > length:
        return jnp.pad(level, ((0, 0), (0, 0), (0, target - length)))
    return level[..., :target]


def on_device(raw, filt, tap_index, tap_weight, beam_shift, beam_phase):
    pulse_count = lax.axis_size("pulse")
    parts, local_beams, bins = raw.shape
    taps_len = filt.shape[1]
    local_sections = local_beams.bit_length() - 1
    cross_sections = pulse_count.bit_length() - 1
    sections = local_sections + cross_sections
    extra = sections * MARGIN
    blocks = -(-(bins + extra) // BLOCK)
    reach = -(-(BLOCK + taps_len - 1) // BLOCK)
    rim_len = (blocks + reach - 1) * BLOCK - bins
    rim = shifted(raw[:, :, :rim_len], "range", -1)
    wide = jnp.concatenate([raw, rim], axis=2)
    level = padded_lanes(compress(wide, filt, blocks), bins + extra)
    all_weights = tap_weights(tap_index, tap_weight)
    all_cos = jnp.cos(beam_phase)
    all_sin = jnp.sin(beam_phase)

    def run_section(level, section, beams):
        start = 2 * beams - 2
        stop = start + 2 * beams
        return merge_section(
            level,
            beams,
            all_weights[section],
            beam_shift[:, start:stop],
            all_cos[:, start:stop],
            all_sin[:, start:stop],
        )

    for section in range(local_sections):
        level = run_section(level, section, 1 << section)
    piece_bins = bins // pulse_count
    need = cross_sections * MARGIN
    flat = level[:, :, : bins + need]
    flat = jnp.pad(flat, ((0, 0), (0, 0), (0, piece_bins - need)))
    head = flat[:, :, :bins].reshape(parts, local_beams, pulse_count, piece_bins)
    tail = flat[:, :, piece_bins:].reshape(parts, local_beams, pulse_count, piece_bins)[
        :, :, :, :need
    ]
    pieces = jnp.transpose(jnp.concatenate([head, tail], axis=3), (0, 2, 1, 3))
    level = lax.all_to_all(pieces, "pulse", split_axis=1, concat_axis=1, tiled=True)
    level = padded_lanes(level.reshape(parts, pulse_count * local_beams, piece_bins + need), piece_bins + need)
    for bit in range(cross_sections):
        section = local_sections + bit
        level = run_section(level, section, local_beams << bit)
    level = level[..., :piece_bins].reshape(parts, pulse_count, local_beams, piece_bins)
    level = lax.all_to_all(level, "pulse", split_axis=1, concat_axis=3, tiled=True)
    return level.reshape(parts, local_beams, bins)


def solution(mesh):
    return jax.shard_map(
        on_device,
        mesh=mesh,
        in_specs=(P(None, "pulse", "range"), P(), P(), P(), P(), P()),
        out_specs=P(None, "pulse", "range"),
        check_vma=False,
    )
```

```python
import jax
import jax.numpy as jnp
from jax import lax
from jax.sharding import PartitionSpec as P
from jax.experimental import pallas as pl
from jax.experimental.pallas import tpu as pltpu

TAPS = 4
MAXOFF = 8
MARGIN = 15
BLOCK = 256
LANE = 128


half_root = 0.7071067811865476


def shifted(shard, axis, by):
    count = lax.axis_size(axis)
    pairs = [(i, i + by) for i in range(count) if 0 <= i + by < count]
    return lax.ppermute(shard, axis, pairs)


def toeplitz_rows(vector, block, rows):
    taps_len = vector.shape[0]
    width = rows + 1
    line = jnp.concatenate([vector, jnp.zeros((width - taps_len,), vector.dtype)])
    return jnp.tile(line, block)[: block * rows].reshape(block, rows)


def band_matrix(filt, block, rows):
    real_band = toeplitz_rows(filt[0], block, rows).T
    imag_band = toeplitz_rows(filt[1], block, rows).T
    upper = jnp.concatenate([real_band, imag_band], axis=1)
    lower = jnp.concatenate([-imag_band, real_band], axis=1)
    return jnp.concatenate([upper, lower], axis=0)


def compress(wide, filt, blocks):
    parts, count, length = wide.shape
    taps_len = filt.shape[1]
    reach = -(-(BLOCK + taps_len - 1) // BLOCK)
    rows = reach * BLOCK
    cut = wide.reshape(parts, count, length // BLOCK, BLOCK)
    window = jnp.concatenate([cut[:, :, c : c + blocks] for c in range(reach)], axis=3)
    segments = jnp.concatenate([window[0], window[1]], axis=2)
    product = lax.dot_general(
        segments,
        band_matrix(filt, BLOCK, rows),
        (((2,), (0,)), ((), ())),
        preferred_element_type=jnp.float32,
    )
    real_part = product[:, :, :BLOCK].reshape(count, blocks * BLOCK)
    imag_part = product[:, :, BLOCK:].reshape(count, blocks * BLOCK)
    return jnp.stack([real_part, imag_part])


def merge_kernel(weight_ref, kid_ref, table_ref, out_ref):
    length = kid_ref.shape[-1]
    reach = MARGIN - MAXOFF + 1
    halves = table_ref.shape[2]
    acc = [[None, None] for _ in range(halves)]
    for c in range(2):
        interp = []
        for part in range(2):
            x = kid_ref[c, part]
            total = weight_ref[c, 0] * x
            for offset in range(1, reach):
                total = total + weight_ref[c, offset] * pltpu.roll(x, length - offset, 1)
            interp.append(total)
        rolled = [[p] + [pltpu.roll(p, length - offset, 1) for offset in range(1, MAXOFF)] for p in interp]
        for half in range(halves):
            shift = table_ref[0, c, half][:, 0:1]
            moved = []
            for part in range(2):
                pick = rolled[part][0]
                for offset in range(1, MAXOFF):
                    pick = jnp.where(shift == float(offset), rolled[part][offset], pick)
                moved.append(pick)
            cos_row = table_ref[1, c, half][:, 0:1]
            sin_row = table_ref[2, c, half][:, 0:1]
            real_part = cos_row * moved[0] - sin_row * moved[1]
            imag_part = sin_row * moved[0] + cos_row * moved[1]
            if c == 0:
                acc[half] = [real_part, imag_part]
            else:
                acc[half] = [acc[half][0] + real_part, acc[half][1] + imag_part]
    for half in range(halves):
        for part in range(2):
            out_ref[half, part] = acc[half][part] * half_root


def merge_call(weights, kids, table):
    _, _, rows, length = kids.shape
    halves = table.shape[2]
    vmem = pltpu.VMEM
    elems = halves * 2 * rows * length
    return pl.pallas_call(
        merge_kernel,
        out_shape=jax.ShapeDtypeStruct((halves, 2, rows, length), jnp.float32),
        in_specs=[
            pl.BlockSpec(memory_space=pltpu.SMEM),
            pl.BlockSpec(memory_space=vmem),
            pl.BlockSpec(memory_space=vmem),
        ],
        out_specs=pl.BlockSpec(memory_space=vmem),
        cost_estimate=pl.CostEstimate(flops=60 * elems, transcendentals=0, bytes_accessed=8 * elems),
    )(weights, kids, table)


def tap_weights(taps, weights):
    reach = MARGIN - MAXOFF + 1
    hit = taps[..., :, None] == jnp.arange(reach, dtype=taps.dtype)
    return jnp.sum(jnp.where(hit, weights[..., :, None], 0.0), axis=-2)


def per_row(table, groups):
    beams = table.shape[-1] // 2
    halves = table.reshape(table.shape[:-1] + (2, beams))
    return jnp.tile(halves, (1,) * (halves.ndim - 1) + (groups,))


def merge_section(level, beams, weights, chosen, cosine, sine):
    parts, rows, length = level.shape
    groups = rows // (2 * beams)
    pairs = level.reshape(parts, groups, 2, beams, length)
    kids = jnp.stack([pairs[:, :, c].reshape(parts, rows // 2, length) for c in range(2)])
    packed = jnp.stack([chosen.astype(jnp.float32), cosine, sine])
    table = jnp.broadcast_to(per_row(packed, groups)[..., None], (3, 2, 2, rows // 2, LANE))
    out = merge_call(weights, kids, table)
    merged = jnp.stack([out[h].reshape(parts, groups, beams, length) for h in range(2)], axis=2)
    return merged.reshape(parts, rows, length)


def padded_lanes(level, width):
    length = level.shape[-1]
    target = -(-width // LANE) * LANE
    if target > length:
        return jnp.pad(level, ((0, 0), (0, 0), (0, target - length)))
    return level[..., :target]


def on_device(raw, filt, tap_index, tap_weight, beam_shift, beam_phase):
    pulse_count = lax.axis_size("pulse")
    parts, local_beams, bins = raw.shape
    taps_len = filt.shape[1]
    local_sections = local_beams.bit_length() - 1
    cross_sections = pulse_count.bit_length() - 1
    sections = local_sections + cross_sections
    extra = sections * MARGIN
    blocks = -(-(bins + extra) // BLOCK)
    reach = -(-(BLOCK + taps_len - 1) // BLOCK)
    rim_len = (blocks + reach - 1) * BLOCK - bins
    rim = shifted(raw[:, :, :rim_len], "range", -1)
    wide = jnp.concatenate([raw, rim], axis=2)
    level = padded_lanes(compress(wide, filt, blocks), bins + extra)
    all_weights = tap_weights(tap_index, tap_weight)
    all_cos = jnp.cos(beam_phase)
    all_sin = jnp.sin(beam_phase)

    def run_section(level, section, beams):
        start = 2 * beams - 2
        stop = start + 2 * beams
        return merge_section(
            level,
            beams,
            all_weights[section],
            beam_shift[:, start:stop],
            all_cos[:, start:stop],
            all_sin[:, start:stop],
        )

    for section in range(local_sections):
        level = run_section(level, section, 1 << section)
    pulse_pos = lax.axis_index("pulse")
    for bit in range(cross_sections):
        section = local_sections + bit
        beams = local_beams << bit
        own = (pulse_pos >> bit) & 1
        pairs = [(i, i ^ (1 << bit)) for i in range(pulse_count)]
        other = lax.ppermute(level, "pulse", pairs)
        kids = jnp.stack([level, other])
        first = 2 * beams - 2 + own * beams + (pulse_pos % (1 << bit)) * local_beams
        rows = [
            lax.dynamic_slice_in_dim(table, first, local_beams, axis=1)
            for table in (beam_shift.astype(jnp.float32), all_cos, all_sin)
        ]
        packed = jnp.stack(rows)
        swap = own == 1
        packed = jnp.where(swap, packed[:, ::-1], packed)
        weights = jnp.where(swap, all_weights[section][::-1], all_weights[section])
        table = jnp.broadcast_to(packed[:, :, None, :, None], (3, 2, 1, local_beams, LANE))
        level = merge_call(weights, kids, table)[0]
    return level[:, :, :bins]


def solution(mesh):
    return jax.shard_map(
        on_device,
        mesh=mesh,
        in_specs=(P(None, "pulse", "range"), P(), P(), P(), P(), P()),
        out_specs=P(None, "pulse", "range"),
        check_vma=False,
    )
```

```python
import jax
import jax.numpy as jnp
from jax import lax
from jax.sharding import PartitionSpec as P
from jax.experimental import pallas as pl
from jax.experimental.pallas import tpu as pltpu

TAPS = 4
MAXOFF = 8
MARGIN = 15
BLOCK = 256
LANE = 128


half_root = 0.7071067811865476


def shifted(shard, axis, by):
    count = lax.axis_size(axis)
    pairs = [(i, i + by) for i in range(count) if 0 <= i + by < count]
    return lax.ppermute(shard, axis, pairs)


def toeplitz_rows(vector, block, rows):
    taps_len = vector.shape[0]
    width = rows + 1
    line = jnp.concatenate([vector, jnp.zeros((width - taps_len,), vector.dtype)])
    return jnp.tile(line, block)[: block * rows].reshape(block, rows)


def band_matrix(filt, block, rows):
    real_band = toeplitz_rows(filt[0], block, rows).T
    imag_band = toeplitz_rows(filt[1], block, rows).T
    upper = jnp.concatenate([real_band, imag_band], axis=1)
    lower = jnp.concatenate([-imag_band, real_band], axis=1)
    return jnp.concatenate([upper, lower], axis=0)


def compress(wide, filt, blocks):
    parts, count, length = wide.shape
    taps_len = filt.shape[1]
    reach = -(-(BLOCK + taps_len - 1) // BLOCK)
    rows = reach * BLOCK
    cut = wide.reshape(parts, count, length // BLOCK, BLOCK)
    window = jnp.concatenate([cut[:, :, c : c + blocks] for c in range(reach)], axis=3)
    segments = jnp.concatenate([window[0], window[1]], axis=2)
    product = lax.dot_general(
        segments,
        band_matrix(filt, BLOCK, rows),
        (((2,), (0,)), ((), ())),
        preferred_element_type=jnp.float32,
    )
    real_part = product[:, :, :BLOCK].reshape(count, blocks * BLOCK)
    imag_part = product[:, :, BLOCK:].reshape(count, blocks * BLOCK)
    return jnp.stack([real_part, imag_part])


def merge_kernel(weight_ref, kid_ref, table_ref, out_ref):
    halves = table_ref.shape[2]
    rows = kid_ref.shape[2]
    length = out_ref.shape[-1]
    reach = MARGIN - MAXOFF + 1
    row_step = 8 if rows % 8 == 0 else rows
    lane_step = 3 * LANE if length % (3 * LANE) == 0 else LANE
    width = lane_step + LANE
    lane_count = length // lane_step
    weight = [[weight_ref[c, d] for d in range(reach)] for c in range(2)]

    def body(step, carry):
        r0 = pl.multiple_of((step // lane_count) * row_step, row_step)
        l0 = pl.multiple_of((step % lane_count) * lane_step, LANE)
        acc = [[None, None] for _ in range(halves)]
        for c in range(2):
            interp = []
            for part in range(2):
                x = kid_ref[c, part, pl.ds(r0, row_step), pl.ds(l0, width)]
                total = weight[c][0] * x
                for offset in range(1, reach):
                    total = total + weight[c][offset] * pltpu.roll(x, width - offset, 1)
                interp.append(total)
            rolled = [[p] + [pltpu.roll(p, width - offset, 1) for offset in range(1, MAXOFF)] for p in interp]
            for half in range(halves):
                shift = table_ref[0, c, half, pl.ds(r0, row_step), 0:1]
                moved = []
                for part in range(2):
                    pick = rolled[part][0]
                    for offset in range(1, MAXOFF):
                        pick = jnp.where(shift == float(offset), rolled[part][offset], pick)
                    moved.append(pick)
                cos_row = table_ref[1, c, half, pl.ds(r0, row_step), 0:1]
                sin_row = table_ref[2, c, half, pl.ds(r0, row_step), 0:1]
                real_part = cos_row * moved[0] - sin_row * moved[1]
                imag_part = sin_row * moved[0] + cos_row * moved[1]
                if c == 0:
                    acc[half] = [real_part, imag_part]
                else:
                    acc[half] = [acc[half][0] + real_part, acc[half][1] + imag_part]
        for half in range(halves):
            for part in range(2):
                value = acc[half][part] * half_root
                out_ref[half, part, pl.ds(r0, row_step), pl.ds(l0, lane_step)] = value[:, :lane_step]
        return carry

    lax.fori_loop(0, (rows // row_step) * lane_count, body, 0)


def merge_call(weights, kids, table):
    _, _, rows, wide = kids.shape
    length = wide - LANE
    halves = table.shape[2]
    vmem = pltpu.VMEM
    elems = halves * 2 * rows * length
    return pl.pallas_call(
        merge_kernel,
        out_shape=jax.ShapeDtypeStruct((halves, 2, rows, length), jnp.float32),
        in_specs=[
            pl.BlockSpec(memory_space=pltpu.SMEM),
            pl.BlockSpec(memory_space=vmem),
            pl.BlockSpec(memory_space=vmem),
        ],
        out_specs=pl.BlockSpec(memory_space=vmem),
        cost_estimate=pl.CostEstimate(flops=60 * elems, transcendentals=0, bytes_accessed=8 * elems),
    )(weights, kids, table)


def tap_weights(taps, weights):
    reach = MARGIN - MAXOFF + 1
    hit = taps[..., :, None] == jnp.arange(reach, dtype=taps.dtype)
    return jnp.sum(jnp.where(hit, weights[..., :, None], 0.0), axis=-2)


def per_row(table, groups):
    beams = table.shape[-1] // 2
    halves = table.reshape(table.shape[:-1] + (2, beams))
    return jnp.tile(halves, (1,) * (halves.ndim - 1) + (groups,))


def merge_section(level, beams, weights, chosen, cosine, sine):
    parts, rows, length = level.shape
    groups = rows // (2 * beams)
    pairs = level.reshape(parts, groups, 2, beams, length)
    kids = jnp.stack([pairs[:, :, c].reshape(parts, rows // 2, length) for c in range(2)])
    kids = jnp.pad(kids, ((0, 0), (0, 0), (0, 0), (0, LANE)))
    packed = jnp.stack([chosen.astype(jnp.float32), cosine, sine])
    table = jnp.broadcast_to(per_row(packed, groups)[..., None], (3, 2, 2, rows // 2, LANE))
    out = merge_call(weights, kids, table)
    merged = jnp.stack([out[h].reshape(parts, groups, beams, length) for h in range(2)], axis=2)
    return merged.reshape(parts, rows, length)


def padded_lanes(level, width):
    length = level.shape[-1]
    target = -(-width // LANE) * LANE
    if target > length:
        return jnp.pad(level, ((0, 0), (0, 0), (0, target - length)))
    return level[..., :target]


def on_device(raw, filt, tap_index, tap_weight, beam_shift, beam_phase):
    pulse_count = lax.axis_size("pulse")
    parts, local_beams, bins = raw.shape
    taps_len = filt.shape[1]
    local_sections = local_beams.bit_length() - 1
    cross_sections = pulse_count.bit_length() - 1
    sections = local_sections + cross_sections
    extra = sections * MARGIN
    blocks = -(-(bins + extra) // BLOCK)
    reach = -(-(BLOCK + taps_len - 1) // BLOCK)
    rim_len = (blocks + reach - 1) * BLOCK - bins
    rim = shifted(raw[:, :, :rim_len], "range", -1)
    wide = jnp.concatenate([raw, rim], axis=2)
    level = padded_lanes(compress(wide, filt, blocks), bins + extra)
    all_weights = tap_weights(tap_index, tap_weight)
    all_cos = jnp.cos(beam_phase)
    all_sin = jnp.sin(beam_phase)

    def run_section(level, section, beams):
        start = 2 * beams - 2
        stop = start + 2 * beams
        return merge_section(
            level,
            beams,
            all_weights[section],
            beam_shift[:, start:stop],
            all_cos[:, start:stop],
            all_sin[:, start:stop],
        )

    for section in range(local_sections):
        level = run_section(level, section, 1 << section)
    piece_bins = bins // pulse_count
    need = cross_sections * MARGIN
    flat = level[:, :, : bins + need]
    flat = jnp.pad(flat, ((0, 0), (0, 0), (0, piece_bins - need)))
    head = flat[:, :, :bins].reshape(parts, local_beams, pulse_count, piece_bins)
    tail = flat[:, :, piece_bins:].reshape(parts, local_beams, pulse_count, piece_bins)[
        :, :, :, :need
    ]
    pieces = jnp.transpose(jnp.concatenate([head, tail], axis=3), (0, 2, 1, 3))
    level = lax.all_to_all(pieces, "pulse", split_axis=1, concat_axis=1, tiled=True)
    level = padded_lanes(level.reshape(parts, pulse_count * local_beams, piece_bins + need), piece_bins + need)
    for bit in range(cross_sections):
        section = local_sections + bit
        level = run_section(level, section, local_beams << bit)
    level = level[..., :piece_bins].reshape(parts, pulse_count, local_beams, piece_bins)
    level = lax.all_to_all(level, "pulse", split_axis=1, concat_axis=3, tiled=True)
    return level.reshape(parts, local_beams, bins)


def solution(mesh):
    return jax.shard_map(
        on_device,
        mesh=mesh,
        in_specs=(P(None, "pulse", "range"), P(), P(), P(), P(), P()),
        out_specs=P(None, "pulse", "range"),
        check_vma=False,
    )
```

```python
import jax
import jax.numpy as jnp
from jax import lax
from jax.sharding import PartitionSpec as P
from jax.experimental import pallas as pl
from jax.experimental.pallas import tpu as pltpu

TAPS = 4
MAXOFF = 8
MARGIN = 15
BLOCK = 256
LANE = 128


half_root = 0.7071067811865476


def shifted(shard, axis, by):
    count = lax.axis_size(axis)
    pairs = [(i, i + by) for i in range(count) if 0 <= i + by < count]
    return lax.ppermute(shard, axis, pairs)


def toeplitz_rows(vector, block, rows):
    taps_len = vector.shape[0]
    width = rows + 1
    line = jnp.concatenate([vector, jnp.zeros((width - taps_len,), vector.dtype)])
    return jnp.tile(line, block)[: block * rows].reshape(block, rows)


def band_matrix(filt, block, rows):
    real_band = toeplitz_rows(filt[0], block, rows).T
    imag_band = toeplitz_rows(filt[1], block, rows).T
    upper = jnp.concatenate([real_band, imag_band], axis=1)
    lower = jnp.concatenate([-imag_band, real_band], axis=1)
    return jnp.concatenate([upper, lower], axis=0)


def compress(wide, filt, blocks):
    parts, count, length = wide.shape
    taps_len = filt.shape[1]
    reach = -(-(BLOCK + taps_len - 1) // BLOCK)
    rows = reach * BLOCK
    cut = wide.reshape(parts, count, length // BLOCK, BLOCK)
    window = jnp.concatenate([cut[:, :, c : c + blocks] for c in range(reach)], axis=3)
    segments = jnp.concatenate([window[0], window[1]], axis=2)
    product = lax.dot_general(
        segments,
        band_matrix(filt, BLOCK, rows),
        (((2,), (0,)), ((), ())),
        preferred_element_type=jnp.float32,
    )
    real_part = product[:, :, :BLOCK].reshape(count, blocks * BLOCK)
    imag_part = product[:, :, BLOCK:].reshape(count, blocks * BLOCK)
    return jnp.stack([real_part, imag_part])


def merge_kernel(weight_ref, kid_ref, table_ref, out_ref):
    length = kid_ref.shape[-1]
    reach = MARGIN - MAXOFF + 1
    acc = [[None, None], [None, None]]
    for c in range(2):
        interp = []
        for part in range(2):
            x = kid_ref[c, part]
            total = weight_ref[c, 0] * x
            for offset in range(1, reach):
                total = total + weight_ref[c, offset] * pltpu.roll(x, length - offset, 1)
            interp.append(total)
        for half in range(2):
            moved = []
            for part in range(2):
                pick = interp[part]
                for bit in (2, 1, 0):
                    hit = table_ref[bit, c, half][:, 0:1] > 0.5
                    pick = jnp.where(hit, pltpu.roll(pick, length - (1 << bit), 1), pick)
                moved.append(pick)
            cos_row = table_ref[3, c, half][:, 0:1]
            sin_row = table_ref[4, c, half][:, 0:1]
            real_part = cos_row * moved[0] - sin_row * moved[1]
            imag_part = sin_row * moved[0] + cos_row * moved[1]
            if c == 0:
                acc[half] = [real_part, imag_part]
            else:
                acc[half] = [acc[half][0] + real_part, acc[half][1] + imag_part]
    for half in range(2):
        for part in range(2):
            out_ref[half, part] = acc[half][part] * half_root


def merge_call(weights, kids, table):
    _, _, rows, length = kids.shape
    vmem = pltpu.VMEM
    elems = 2 * 2 * rows * length
    return pl.pallas_call(
        merge_kernel,
        out_shape=jax.ShapeDtypeStruct((2, 2, rows, length), jnp.float32),
        in_specs=[
            pl.BlockSpec(memory_space=pltpu.SMEM),
            pl.BlockSpec(memory_space=vmem),
            pl.BlockSpec(memory_space=vmem),
        ],
        out_specs=pl.BlockSpec(memory_space=vmem),
        cost_estimate=pl.CostEstimate(flops=60 * elems, transcendentals=0, bytes_accessed=8 * elems),
    )(weights, kids, table)


def tap_weights(taps, weights):
    reach = MARGIN - MAXOFF + 1
    hit = taps[..., :, None] == jnp.arange(reach, dtype=taps.dtype)
    return jnp.sum(jnp.where(hit, weights[..., :, None], 0.0), axis=-2)


def per_row(table, groups):
    beams = table.shape[-1] // 2
    halves = table.reshape(table.shape[:-1] + (2, beams))
    return jnp.tile(halves, (1,) * (halves.ndim - 1) + (groups,))


def merge_section(level, beams, weights, chosen, cosine, sine):
    parts, rows, length = level.shape
    groups = rows // (2 * beams)
    pairs = level.reshape(parts, groups, 2, beams, length)
    kids = jnp.stack([pairs[:, :, c].reshape(parts, rows // 2, length) for c in range(2)])
    bits = [((chosen >> bit) & 1).astype(jnp.float32) for bit in range(3)]
    packed = jnp.stack(bits + [cosine, sine])
    table = jnp.broadcast_to(per_row(packed, groups)[..., None], (5, 2, 2, rows // 2, LANE))
    out = merge_call(weights, kids, table)
    merged = jnp.stack([out[h].reshape(parts, groups, beams, length) for h in range(2)], axis=2)
    return merged.reshape(parts, rows, length)


def padded_lanes(level, width):
    length = level.shape[-1]
    target = -(-width // LANE) * LANE
    if target > length:
        return jnp.pad(level, ((0, 0), (0, 0), (0, target - length)))
    return level[..., :target]


def on_device(raw, filt, tap_index, tap_weight, beam_shift, beam_phase):
    pulse_count = lax.axis_size("pulse")
    parts, local_beams, bins = raw.shape
    taps_len = filt.shape[1]
    local_sections = local_beams.bit_length() - 1
    cross_sections = pulse_count.bit_length() - 1
    sections = local_sections + cross_sections
    extra = sections * MARGIN
    blocks = -(-(bins + extra) // BLOCK)
    reach = -(-(BLOCK + taps_len - 1) // BLOCK)
    rim_len = (blocks + reach - 1) * BLOCK - bins
    rim = shifted(raw[:, :, :rim_len], "range", -1)
    wide = jnp.concatenate([raw, rim], axis=2)
    level = padded_lanes(compress(wide, filt, blocks), bins + extra)
    all_weights = tap_weights(tap_index, tap_weight)
    all_cos = jnp.cos(beam_phase)
    all_sin = jnp.sin(beam_phase)

    def run_section(level, section, beams):
        start = 2 * beams - 2
        stop = start + 2 * beams
        return merge_section(
            level,
            beams,
            all_weights[section],
            beam_shift[:, start:stop],
            all_cos[:, start:stop],
            all_sin[:, start:stop],
        )

    for section in range(local_sections):
        level = run_section(level, section, 1 << section)
    piece_bins = bins // pulse_count
    need = cross_sections * MARGIN
    flat = level[:, :, : bins + need]
    flat = jnp.pad(flat, ((0, 0), (0, 0), (0, piece_bins - need)))
    head = flat[:, :, :bins].reshape(parts, local_beams, pulse_count, piece_bins)
    tail = flat[:, :, piece_bins:].reshape(parts, local_beams, pulse_count, piece_bins)[
        :, :, :, :need
    ]
    pieces = jnp.transpose(jnp.concatenate([head, tail], axis=3), (0, 2, 1, 3))
    level = lax.all_to_all(pieces, "pulse", split_axis=1, concat_axis=1, tiled=True)
    level = padded_lanes(level.reshape(parts, pulse_count * local_beams, piece_bins + need), piece_bins + need)
    for bit in range(cross_sections):
        section = local_sections + bit
        level = run_section(level, section, local_beams << bit)
    level = level[..., :piece_bins].reshape(parts, pulse_count, local_beams, piece_bins)
    level = lax.all_to_all(level, "pulse", split_axis=1, concat_axis=3, tiled=True)
    return level.reshape(parts, local_beams, bins)


def solution(mesh):
    return jax.shard_map(
        on_device,
        mesh=mesh,
        in_specs=(P(None, "pulse", "range"), P(), P(), P(), P(), P()),
        out_specs=P(None, "pulse", "range"),
        check_vma=False,
    )
```

```python
import jax
import jax.numpy as jnp
from jax import lax
from jax.sharding import PartitionSpec as P
from jax.experimental import pallas as pl
from jax.experimental.pallas import tpu as pltpu

TAPS = 4
MAXOFF = 8
MARGIN = 15
BLOCK = 256
LANE = 128


half_root = 0.7071067811865476


def shifted(shard, axis, by):
    count = lax.axis_size(axis)
    pairs = [(i, i + by) for i in range(count) if 0 <= i + by < count]
    return lax.ppermute(shard, axis, pairs)


def toeplitz_rows(vector, block, rows):
    taps_len = vector.shape[0]
    width = rows + 1
    line = jnp.concatenate([vector, jnp.zeros((width - taps_len,), vector.dtype)])
    return jnp.tile(line, block)[: block * rows].reshape(block, rows)


def band_matrix(filt, block, rows):
    real_band = toeplitz_rows(filt[0], block, rows).T
    imag_band = toeplitz_rows(filt[1], block, rows).T
    upper = jnp.concatenate([real_band, imag_band], axis=1)
    lower = jnp.concatenate([-imag_band, real_band], axis=1)
    return jnp.concatenate([upper, lower], axis=0)


def compress(wide, filt, blocks):
    parts, count, length = wide.shape
    taps_len = filt.shape[1]
    reach = -(-(BLOCK + taps_len - 1) // BLOCK)
    rows = reach * BLOCK
    cut = wide.reshape(parts, count, length // BLOCK, BLOCK)
    window = jnp.concatenate([cut[:, :, c : c + blocks] for c in range(reach)], axis=3)
    segments = jnp.concatenate([window[0], window[1]], axis=2)
    product = lax.dot_general(
        segments,
        band_matrix(filt, BLOCK, rows),
        (((2,), (0,)), ((), ())),
        preferred_element_type=jnp.float32,
    )
    real_part = product[:, :, :BLOCK].reshape(count, blocks * BLOCK)
    imag_part = product[:, :, BLOCK:].reshape(count, blocks * BLOCK)
    return jnp.stack([real_part, imag_part])


def merge_tile(weight_ref, kid_ref, table_ref, out_ref, r0, row_step, l0, lane_step):
    width = lane_step + LANE
    reach = MARGIN - MAXOFF + 1
    rows_at = slice(r0, r0 + row_step)
    acc = [[None, None], [None, None]]
    for c in range(2):
        interp = []
        for part in range(2):
            x = kid_ref[c, part, rows_at, l0 : l0 + width]
            total = weight_ref[c, 0] * x
            for offset in range(1, reach):
                total = total + weight_ref[c, offset] * pltpu.roll(x, width - offset, 1)
            interp.append(total)
        for half in range(2):
            moved = []
            for part in range(2):
                pick = interp[part]
                for bit in (2, 1, 0):
                    hit = table_ref[bit, c, half, rows_at, 0:1] > 0.5
                    pick = jnp.where(hit, pltpu.roll(pick, width - (1 << bit), 1), pick)
                moved.append(pick)
            cos_row = table_ref[3, c, half, rows_at, 0:1]
            sin_row = table_ref[4, c, half, rows_at, 0:1]
            real_part = cos_row * moved[0] - sin_row * moved[1]
            imag_part = sin_row * moved[0] + cos_row * moved[1]
            if c == 0:
                acc[half] = [real_part, imag_part]
            else:
                acc[half] = [acc[half][0] + real_part, acc[half][1] + imag_part]
    for half in range(2):
        for part in range(2):
            value = acc[half][part] * half_root
            out_ref[half, part, rows_at, l0 : l0 + lane_step] = value[:, :lane_step]


def merge_kernel(weight_ref, kid_ref, table_ref, out_ref):
    rows = kid_ref.shape[2]
    length = out_ref.shape[-1]
    row_step = 8 if rows % 8 == 0 else rows
    lane_step = 3 * LANE if length % (3 * LANE) == 0 else LANE
    for r0 in range(0, rows, row_step):
        for l0 in range(0, length, lane_step):
            merge_tile(weight_ref, kid_ref, table_ref, out_ref, r0, row_step, l0, lane_step)


def merge_call(weights, kids, table):
    _, _, rows, wide = kids.shape
    length = wide - LANE
    vmem = pltpu.VMEM
    elems = 2 * 2 * rows * length
    return pl.pallas_call(
        merge_kernel,
        out_shape=jax.ShapeDtypeStruct((2, 2, rows, length), jnp.float32),
        in_specs=[
            pl.BlockSpec(memory_space=pltpu.SMEM),
            pl.BlockSpec(memory_space=vmem),
            pl.BlockSpec(memory_space=vmem),
        ],
        out_specs=pl.BlockSpec(memory_space=vmem),
        cost_estimate=pl.CostEstimate(flops=60 * elems, transcendentals=0, bytes_accessed=8 * elems),
    )(weights, kids, table)


def tap_weights(taps, weights):
    reach = MARGIN - MAXOFF + 1
    hit = taps[..., :, None] == jnp.arange(reach, dtype=taps.dtype)
    return jnp.sum(jnp.where(hit, weights[..., :, None], 0.0), axis=-2)


def per_row(table, groups):
    beams = table.shape[-1] // 2
    halves = table.reshape(table.shape[:-1] + (2, beams))
    return jnp.tile(halves, (1,) * (halves.ndim - 1) + (groups,))


def merge_section(level, beams, weights, chosen, cosine, sine):
    parts, rows, length = level.shape
    groups = rows // (2 * beams)
    pairs = level.reshape(parts, groups, 2, beams, length)
    kids = jnp.stack([pairs[:, :, c].reshape(parts, rows // 2, length) for c in range(2)])
    kids = jnp.pad(kids, ((0, 0), (0, 0), (0, 0), (0, LANE)))
    bits = [((chosen >> bit) & 1).astype(jnp.float32) for bit in range(3)]
    packed = jnp.stack(bits + [cosine, sine])
    table = jnp.broadcast_to(per_row(packed, groups)[..., None], (5, 2, 2, rows // 2, LANE))
    out = merge_call(weights, kids, table)
    merged = jnp.stack([out[h].reshape(parts, groups, beams, length) for h in range(2)], axis=2)
    return merged.reshape(parts, rows, length)


def padded_lanes(level, width):
    length = level.shape[-1]
    target = -(-width // LANE) * LANE
    if target > length:
        return jnp.pad(level, ((0, 0), (0, 0), (0, target - length)))
    return level[..., :target]


def on_device(raw, filt, tap_index, tap_weight, beam_shift, beam_phase):
    pulse_count = lax.axis_size("pulse")
    parts, local_beams, bins = raw.shape
    taps_len = filt.shape[1]
    local_sections = local_beams.bit_length() - 1
    cross_sections = pulse_count.bit_length() - 1
    sections = local_sections + cross_sections
    extra = sections * MARGIN
    blocks = -(-(bins + extra) // BLOCK)
    reach = -(-(BLOCK + taps_len - 1) // BLOCK)
    rim_len = (blocks + reach - 1) * BLOCK - bins
    rim = shifted(raw[:, :, :rim_len], "range", -1)
    wide = jnp.concatenate([raw, rim], axis=2)
    level = padded_lanes(compress(wide, filt, blocks), bins + extra)
    all_weights = tap_weights(tap_index, tap_weight)
    all_cos = jnp.cos(beam_phase)
    all_sin = jnp.sin(beam_phase)

    def run_section(level, section, beams):
        start = 2 * beams - 2
        stop = start + 2 * beams
        return merge_section(
            level,
            beams,
            all_weights[section],
            beam_shift[:, start:stop],
            all_cos[:, start:stop],
            all_sin[:, start:stop],
        )

    for section in range(local_sections):
        level = run_section(level, section, 1 << section)
    piece_bins = bins // pulse_count
    need = cross_sections * MARGIN
    flat = level[:, :, : bins + need]
    flat = jnp.pad(flat, ((0, 0), (0, 0), (0, piece_bins - need)))
    head = flat[:, :, :bins].reshape(parts, local_beams, pulse_count, piece_bins)
    tail = flat[:, :, piece_bins:].reshape(parts, local_beams, pulse_count, piece_bins)[
        :, :, :, :need
    ]
    pieces = jnp.transpose(jnp.concatenate([head, tail], axis=3), (0, 2, 1, 3))
    level = lax.all_to_all(pieces, "pulse", split_axis=1, concat_axis=1, tiled=True)
    level = padded_lanes(level.reshape(parts, pulse_count * local_beams, piece_bins + need), piece_bins + need)
    for bit in range(cross_sections):
        section = local_sections + bit
        level = run_section(level, section, local_beams << bit)
    level = level[..., :piece_bins].reshape(parts, pulse_count, local_beams, piece_bins)
    level = lax.all_to_all(level, "pulse", split_axis=1, concat_axis=3, tiled=True)
    return level.reshape(parts, local_beams, bins)


def solution(mesh):
    return jax.shard_map(
        on_device,
        mesh=mesh,
        in_specs=(P(None, "pulse", "range"), P(), P(), P(), P(), P()),
        out_specs=P(None, "pulse", "range"),
        check_vma=False,
    )
```

```python
import jax
import jax.numpy as jnp
from jax import lax
from jax.sharding import PartitionSpec as P
from jax.experimental import pallas as pl
from jax.experimental.pallas import tpu as pltpu

TAPS = 4
MAXOFF = 8
MARGIN = 15
BLOCK = 256
LANE = 128


half_root = 0.7071067811865476


def shifted(shard, axis, by):
    count = lax.axis_size(axis)
    pairs = [(i, i + by) for i in range(count) if 0 <= i + by < count]
    return lax.ppermute(shard, axis, pairs)


def toeplitz_rows(vector, block, rows):
    taps_len = vector.shape[0]
    width = rows + 1
    line = jnp.concatenate([vector, jnp.zeros((width - taps_len,), vector.dtype)])
    return jnp.tile(line, block)[: block * rows].reshape(block, rows)


def band_matrix(filt, block, rows):
    real_band = toeplitz_rows(filt[0], block, rows).T
    imag_band = toeplitz_rows(filt[1], block, rows).T
    upper = jnp.concatenate([real_band, imag_band], axis=1)
    lower = jnp.concatenate([-imag_band, real_band], axis=1)
    return jnp.concatenate([upper, lower], axis=0)


def compress(wide, filt, blocks):
    parts, count, length = wide.shape
    taps_len = filt.shape[1]
    reach = -(-(BLOCK + taps_len - 1) // BLOCK)
    rows = reach * BLOCK
    cut = wide.reshape(parts, count, length // BLOCK, BLOCK)
    window = jnp.concatenate([cut[:, :, c : c + blocks] for c in range(reach)], axis=3)
    segments = jnp.concatenate([window[0], window[1]], axis=2)
    product = lax.dot_general(
        segments,
        band_matrix(filt, BLOCK, rows),
        (((2,), (0,)), ((), ())),
        preferred_element_type=jnp.float32,
    )
    real_part = product[:, :, :BLOCK].reshape(count, blocks * BLOCK)
    imag_part = product[:, :, BLOCK:].reshape(count, blocks * BLOCK)
    return jnp.stack([real_part, imag_part])


def merge_kernel(weight_ref, kid_ref, table_ref, out_ref):
    length = kid_ref.shape[-1]
    reach = MARGIN - MAXOFF + 1
    acc = [[None, None], [None, None]]
    for c in range(2):
        interp = []
        for part in range(2):
            x = kid_ref[c, part]
            total = weight_ref[c, 0] * x
            for offset in range(1, reach):
                total = total + weight_ref[c, offset] * pltpu.roll(x, length - offset, 1)
            interp.append(total)
        for half in range(2):
            moved = []
            for part in range(2):
                pick = interp[part]
                for bit in (2, 1, 0):
                    hit = table_ref[bit, c, half][:, 0:1] > 0.5
                    pick = jnp.where(hit, pltpu.roll(pick, length - (1 << bit), 1), pick)
                moved.append(pick)
            cos_row = table_ref[3, c, half][:, 0:1]
            sin_row = table_ref[4, c, half][:, 0:1]
            real_part = cos_row * moved[0] - sin_row * moved[1]
            imag_part = sin_row * moved[0] + cos_row * moved[1]
            if c == 0:
                acc[half] = [real_part, imag_part]
            else:
                acc[half] = [acc[half][0] + real_part, acc[half][1] + imag_part]
    for half in range(2):
        for part in range(2):
            out_ref[half, part] = acc[half][part] * half_root


def merge_call(weights, kids, table):
    _, _, rows, length = kids.shape
    vmem = pltpu.VMEM
    elems = 2 * 2 * rows * length
    return pl.pallas_call(
        merge_kernel,
        out_shape=jax.ShapeDtypeStruct((2, 2, rows, length), jnp.float32),
        in_specs=[
            pl.BlockSpec(memory_space=pltpu.SMEM),
            pl.BlockSpec(memory_space=vmem),
            pl.BlockSpec(memory_space=vmem),
        ],
        out_specs=pl.BlockSpec(memory_space=vmem),
        cost_estimate=pl.CostEstimate(flops=60 * elems, transcendentals=0, bytes_accessed=8 * elems),
    )(weights, kids, table)


def tap_weights(taps, weights):
    reach = MARGIN - MAXOFF + 1
    hit = taps[..., :, None] == jnp.arange(reach, dtype=taps.dtype)
    return jnp.sum(jnp.where(hit, weights[..., :, None], 0.0), axis=-2)


def per_row(table, groups):
    beams = table.shape[-1] // 2
    halves = table.reshape(table.shape[:-1] + (2, beams))
    return jnp.tile(halves, (1,) * (halves.ndim - 1) + (groups,))


def merge_section(level, beams, weights, packed):
    parts, rows, length = level.shape
    groups = rows // (2 * beams)
    pairs = level.reshape(parts, groups, 2, beams, length)
    kids = jnp.stack([pairs[:, :, c].reshape(parts, rows // 2, length) for c in range(2)])
    table = jnp.broadcast_to(per_row(packed, groups)[..., None], (5, 2, 2, rows // 2, LANE))
    out = merge_call(weights, kids, table)
    merged = jnp.stack([out[h].reshape(parts, groups, beams, length) for h in range(2)], axis=2)
    return merged.reshape(parts, rows, length)


def padded_lanes(level, width):
    length = level.shape[-1]
    target = -(-width // LANE) * LANE
    if target > length:
        return jnp.pad(level, ((0, 0), (0, 0), (0, target - length)))
    return level[..., :target]


def on_device(raw, filt, tap_index, tap_weight, beam_shift, beam_phase):
    pulse_count = lax.axis_size("pulse")
    parts, local_beams, bins = raw.shape
    taps_len = filt.shape[1]
    local_sections = local_beams.bit_length() - 1
    cross_sections = pulse_count.bit_length() - 1
    sections = local_sections + cross_sections
    extra = sections * MARGIN
    blocks = -(-(bins + extra) // BLOCK)
    reach = -(-(BLOCK + taps_len - 1) // BLOCK)
    rim_len = (blocks + reach - 1) * BLOCK - bins
    rim = shifted(raw[:, :, :rim_len], "range", -1)
    wide = jnp.concatenate([raw, rim], axis=2)
    level = padded_lanes(compress(wide, filt, blocks), bins + extra)
    all_weights = tap_weights(tap_index, tap_weight)
    bits = [((beam_shift >> bit) & 1).astype(jnp.float32) for bit in range(3)]
    all_rows = jnp.stack(bits + [jnp.cos(beam_phase), jnp.sin(beam_phase)])

    def run_section(level, section, beams):
        start = 2 * beams - 2
        stop = start + 2 * beams
        return merge_section(
            level,
            beams,
            all_weights[section],
            all_rows[:, :, start:stop],
        )

    for section in range(local_sections):
        level = run_section(level, section, 1 << section)
    piece_bins = bins // pulse_count
    need = cross_sections * MARGIN
    flat = level[:, :, : bins + need]
    flat = jnp.pad(flat, ((0, 0), (0, 0), (0, piece_bins - need)))
    head = flat[:, :, :bins].reshape(parts, local_beams, pulse_count, piece_bins)
    tail = flat[:, :, piece_bins:].reshape(parts, local_beams, pulse_count, piece_bins)[
        :, :, :, :need
    ]
    pieces = jnp.transpose(jnp.concatenate([head, tail], axis=3), (0, 2, 1, 3))
    level = lax.all_to_all(pieces, "pulse", split_axis=1, concat_axis=1, tiled=True)
    level = padded_lanes(level.reshape(parts, pulse_count * local_beams, piece_bins + need), piece_bins + need)
    for bit in range(cross_sections):
        section = local_sections + bit
        level = run_section(level, section, local_beams << bit)
    level = level[..., :piece_bins].reshape(parts, pulse_count, local_beams, piece_bins)
    level = lax.all_to_all(level, "pulse", split_axis=1, concat_axis=3, tiled=True)
    return level.reshape(parts, local_beams, bins)


def solution(mesh):
    return jax.shard_map(
        on_device,
        mesh=mesh,
        in_specs=(P(None, "pulse", "range"), P(), P(), P(), P(), P()),
        out_specs=P(None, "pulse", "range"),
        check_vma=False,
    )
```

```python
import functools

import jax
import jax.numpy as jnp
from jax import lax
from jax.sharding import PartitionSpec as P
from jax.experimental import pallas as pl
from jax.experimental.pallas import tpu as pltpu

TAPS = 4
MAXOFF = 8
MARGIN = 15
BLOCK = 256
LANE = 128


half_root = 0.7071067811865476


def shifted(shard, axis, by):
    count = lax.axis_size(axis)
    pairs = [(i, i + by) for i in range(count) if 0 <= i + by < count]
    return lax.ppermute(shard, axis, pairs)


def toeplitz_rows(vector, block, rows):
    taps_len = vector.shape[0]
    width = rows + 1
    line = jnp.concatenate([vector, jnp.zeros((width - taps_len,), vector.dtype)])
    return jnp.tile(line, block)[: block * rows].reshape(block, rows)


def band_matrix(filt, block, rows):
    real_band = toeplitz_rows(filt[0], block, rows).T
    imag_band = toeplitz_rows(filt[1], block, rows).T
    upper = jnp.concatenate([real_band, imag_band], axis=1)
    lower = jnp.concatenate([-imag_band, real_band], axis=1)
    return jnp.concatenate([upper, lower], axis=0)


def compress(wide, filt, blocks):
    parts, count, length = wide.shape
    taps_len = filt.shape[1]
    reach = -(-(BLOCK + taps_len - 1) // BLOCK)
    rows = reach * BLOCK
    cut = wide.reshape(parts, count, length // BLOCK, BLOCK)
    window = jnp.concatenate([cut[:, :, c : c + blocks] for c in range(reach)], axis=3)
    segments = jnp.concatenate([window[0], window[1]], axis=2)
    product = lax.dot_general(
        segments,
        band_matrix(filt, BLOCK, rows),
        (((2,), (0,)), ((), ())),
        preferred_element_type=jnp.float32,
    )
    real_part = product[:, :, :BLOCK].reshape(count, blocks * BLOCK)
    imag_part = product[:, :, BLOCK:].reshape(count, blocks * BLOCK)
    return jnp.stack([real_part, imag_part])


def merge_kernel(beams, chained, weight_ref, kid_ref, table_ref, out_ref):
    length = kid_ref.shape[-1]
    reach = MARGIN - MAXOFF + 1
    acc = [[None, None], [None, None]]
    for c in range(2):
        interp = []
        for part in range(2):
            x = kid_ref[c, part]
            total = weight_ref[c, 0] * x
            for offset in range(1, reach):
                total = total + weight_ref[c, offset] * pltpu.roll(x, length - offset, 1)
            interp.append(total)
        for half in range(2):
            moved = []
            for part in range(2):
                pick = interp[part]
                for bit in (2, 1, 0):
                    hit = table_ref[bit, c, half][:, 0:1] > 0.5
                    pick = jnp.where(hit, pltpu.roll(pick, length - (1 << bit), 1), pick)
                moved.append(pick)
            cos_row = table_ref[3, c, half][:, 0:1]
            sin_row = table_ref[4, c, half][:, 0:1]
            real_part = cos_row * moved[0] - sin_row * moved[1]
            imag_part = sin_row * moved[0] + cos_row * moved[1]
            if c == 0:
                acc[half] = [real_part, imag_part]
            else:
                acc[half] = [acc[half][0] + real_part, acc[half][1] + imag_part]
    rows = kid_ref.shape[2]
    for half in range(2):
        for part in range(2):
            value = acc[half][part] * half_root
            for group in range(rows // beams):
                block = value[group * beams : (group + 1) * beams]
                if chained:
                    start = (group // 2) * 2 * beams + half * beams
                    out_ref[group % 2, part, start : start + beams] = block
                else:
                    start = group * 2 * beams + half * beams
                    out_ref[part, start : start + beams] = block


def merge_call(beams, chained, weights, kids, table):
    _, _, rows, length = kids.shape
    vmem = pltpu.VMEM
    elems = 2 * 2 * rows * length
    shape = (2, 2, rows, length) if chained else (2, 2 * rows, length)
    return pl.pallas_call(
        functools.partial(merge_kernel, beams, chained),
        out_shape=jax.ShapeDtypeStruct(shape, jnp.float32),
        in_specs=[
            pl.BlockSpec(memory_space=pltpu.SMEM),
            pl.BlockSpec(memory_space=vmem),
            pl.BlockSpec(memory_space=vmem),
        ],
        out_specs=pl.BlockSpec(memory_space=vmem),
        cost_estimate=pl.CostEstimate(flops=60 * elems, transcendentals=0, bytes_accessed=8 * elems),
    )(weights, kids, table)


def tap_weights(taps, weights):
    reach = MARGIN - MAXOFF + 1
    hit = taps[..., :, None] == jnp.arange(reach, dtype=taps.dtype)
    return jnp.sum(jnp.where(hit, weights[..., :, None], 0.0), axis=-2)


def per_row(table, groups):
    beams = table.shape[-1] // 2
    halves = table.reshape(table.shape[:-1] + (2, beams))
    return jnp.tile(halves, (1,) * (halves.ndim - 1) + (groups,))


def split_kids(level, beams):
    parts, rows, length = level.shape
    groups = rows // (2 * beams)
    pairs = level.reshape(parts, groups, 2, beams, length)
    return jnp.stack([pairs[:, :, c].reshape(parts, rows // 2, length) for c in range(2)])


def merge_section(kids, beams, chained, weights, packed):
    rows = kids.shape[2]
    groups = rows // beams
    table = jnp.broadcast_to(per_row(packed, groups)[..., None], (5, 2, 2, rows, LANE))
    return merge_call(beams, chained, weights, kids, table)


def padded_lanes(level, width):
    length = level.shape[-1]
    target = -(-width // LANE) * LANE
    if target > length:
        return jnp.pad(level, ((0, 0), (0, 0), (0, target - length)))
    return level[..., :target]


def on_device(raw, filt, tap_index, tap_weight, beam_shift, beam_phase):
    pulse_count = lax.axis_size("pulse")
    parts, local_beams, bins = raw.shape
    taps_len = filt.shape[1]
    local_sections = local_beams.bit_length() - 1
    cross_sections = pulse_count.bit_length() - 1
    sections = local_sections + cross_sections
    extra = sections * MARGIN
    blocks = -(-(bins + extra) // BLOCK)
    reach = -(-(BLOCK + taps_len - 1) // BLOCK)
    rim_len = (blocks + reach - 1) * BLOCK - bins
    rim = shifted(raw[:, :, :rim_len], "range", -1)
    wide = jnp.concatenate([raw, rim], axis=2)
    level = padded_lanes(compress(wide, filt, blocks), bins + extra)
    all_weights = tap_weights(tap_index, tap_weight)
    bits = [((beam_shift >> bit) & 1).astype(jnp.float32) for bit in range(3)]
    all_rows = jnp.stack(bits + [jnp.cos(beam_phase), jnp.sin(beam_phase)])

    def run_section(kids, section, beams, chained):
        start = 2 * beams - 2
        stop = start + 2 * beams
        return merge_section(kids, beams, chained, all_weights[section], all_rows[:, :, start:stop])

    level = split_kids(level, 1)
    for section in range(local_sections):
        level = run_section(level, section, 1 << section, section < local_sections - 1)
    piece_bins = bins // pulse_count
    need = cross_sections * MARGIN
    flat = level[:, :, : bins + need]
    flat = jnp.pad(flat, ((0, 0), (0, 0), (0, piece_bins - need)))
    head = flat[:, :, :bins].reshape(parts, local_beams, pulse_count, piece_bins)
    tail = flat[:, :, piece_bins:].reshape(parts, local_beams, pulse_count, piece_bins)[
        :, :, :, :need
    ]
    pieces = jnp.transpose(jnp.concatenate([head, tail], axis=3), (0, 2, 1, 3))
    level = lax.all_to_all(pieces, "pulse", split_axis=1, concat_axis=1, tiled=True)
    level = padded_lanes(level.reshape(parts, pulse_count * local_beams, piece_bins + need), piece_bins + need)
    level = split_kids(level, local_beams)
    for bit in range(cross_sections):
        section = local_sections + bit
        level = run_section(level, section, local_beams << bit, bit < cross_sections - 1)
    level = level[..., :piece_bins].reshape(parts, pulse_count, local_beams, piece_bins)
    level = lax.all_to_all(level, "pulse", split_axis=1, concat_axis=3, tiled=True)
    return level.reshape(parts, local_beams, bins)


def solution(mesh):
    return jax.shard_map(
        on_device,
        mesh=mesh,
        in_specs=(P(None, "pulse", "range"), P(), P(), P(), P(), P()),
        out_specs=P(None, "pulse", "range"),
        check_vma=False,
    )
```

```python
import functools

import jax
import jax.numpy as jnp
from jax import lax
from jax.sharding import PartitionSpec as P
from jax.experimental import pallas as pl
from jax.experimental.pallas import tpu as pltpu

TAPS = 4
MAXOFF = 8
MARGIN = 15
BLOCK = 256
LANE = 128


half_root = 0.7071067811865476


def shifted(shard, axis, by):
    count = lax.axis_size(axis)
    pairs = [(i, i + by) for i in range(count) if 0 <= i + by < count]
    return lax.ppermute(shard, axis, pairs)


def toeplitz_rows(vector, block, rows):
    taps_len = vector.shape[0]
    width = rows + 1
    line = jnp.concatenate([vector, jnp.zeros((width - taps_len,), vector.dtype)])
    return jnp.tile(line, block)[: block * rows].reshape(block, rows)


def band_matrix(filt, block, rows):
    real_band = toeplitz_rows(filt[0], block, rows).T
    imag_band = toeplitz_rows(filt[1], block, rows).T
    upper = jnp.concatenate([real_band, imag_band], axis=1)
    lower = jnp.concatenate([-imag_band, real_band], axis=1)
    return jnp.concatenate([upper, lower], axis=0)


def compress(wide, filt, blocks):
    parts, count, length = wide.shape
    taps_len = filt.shape[1]
    reach = -(-(BLOCK + taps_len - 1) // BLOCK)
    rows = reach * BLOCK
    cut = wide.reshape(parts, count, length // BLOCK, BLOCK)
    window = jnp.concatenate([cut[:, :, c : c + blocks] for c in range(reach)], axis=3)
    segments = jnp.concatenate([window[0], window[1]], axis=2)
    product = lax.dot_general(
        segments,
        band_matrix(filt, BLOCK, rows),
        (((2,), (0,)), ((), ())),
        preferred_element_type=jnp.float32,
    )
    real_part = product[:, :, :BLOCK].reshape(count, blocks * BLOCK)
    imag_part = product[:, :, BLOCK:].reshape(count, blocks * BLOCK)
    return jnp.stack([real_part, imag_part])


def merge_kernel(beams, chained, weight_ref, kid_ref, table_ref, out_ref):
    length = kid_ref.shape[-1]
    reach = MARGIN - MAXOFF + 1
    acc = [[None, None], [None, None]]
    for c in range(2):
        interp = []
        for part in range(2):
            x = kid_ref[c, part]
            total = weight_ref[c, 0] * x
            for offset in range(1, reach):
                total = total + weight_ref[c, offset] * pltpu.roll(x, length - offset, 1)
            interp.append(total)
        for half in range(2):
            moved = []
            for part in range(2):
                pick = interp[part]
                for bit in (2, 1, 0):
                    hit = table_ref[bit, c, half][:, 0:1] > 0.5
                    pick = jnp.where(hit, pltpu.roll(pick, length - (1 << bit), 1), pick)
                moved.append(pick)
            cos_row = table_ref[3, c, half][:, 0:1]
            sin_row = table_ref[4, c, half][:, 0:1]
            real_part = cos_row * moved[0] - sin_row * moved[1]
            imag_part = sin_row * moved[0] + cos_row * moved[1]
            if c == 0:
                acc[half] = [real_part, imag_part]
            else:
                acc[half] = [acc[half][0] + real_part, acc[half][1] + imag_part]
    rows = kid_ref.shape[2]
    for half in range(2):
        for part in range(2):
            value = acc[half][part] * half_root
            for group in range(rows // beams):
                block = value[group * beams : (group + 1) * beams]
                if chained:
                    start = (group // 2) * 2 * beams + half * beams
                    out_ref[group % 2, part, start : start + beams] = block
                else:
                    start = group * 2 * beams + half * beams
                    out_ref[part, start : start + beams] = block


def merge_call(beams, chained, weights, kids, table):
    _, _, rows, length = kids.shape
    vmem = pltpu.VMEM
    elems = 2 * 2 * rows * length
    shape = (2, 2, rows, length) if chained else (2, 2 * rows, length)
    return pl.pallas_call(
        functools.partial(merge_kernel, beams, chained),
        out_shape=jax.ShapeDtypeStruct(shape, jnp.float32),
        in_specs=[
            pl.BlockSpec(memory_space=pltpu.SMEM),
            pl.BlockSpec(memory_space=vmem),
            pl.BlockSpec(memory_space=vmem),
        ],
        out_specs=pl.BlockSpec(memory_space=vmem),
        cost_estimate=pl.CostEstimate(flops=60 * elems, transcendentals=0, bytes_accessed=8 * elems),
    )(weights, kids, table)


def tap_weights(taps, weights):
    reach = MARGIN - MAXOFF + 1
    hit = taps[..., :, None] == jnp.arange(reach, dtype=taps.dtype)
    return jnp.sum(jnp.where(hit, weights[..., :, None], 0.0), axis=-2)


def per_row(table, groups):
    beams = table.shape[-1] // 2
    halves = table.reshape(table.shape[:-1] + (2, beams))
    return jnp.tile(halves, (1,) * (halves.ndim - 1) + (groups,))


def split_kids(level, beams):
    parts, rows, length = level.shape
    groups = rows // (2 * beams)
    pairs = level.reshape(parts, groups, 2, beams, length)
    return jnp.stack([pairs[:, :, c].reshape(parts, rows // 2, length) for c in range(2)])


def row_table(packed, beams, rows):
    return jnp.broadcast_to(per_row(packed, rows // beams)[..., None], (5, 2, 2, rows, LANE))


def merge_section(kids, beams, chained, weights, packed, table=None):
    if table is None:
        table = row_table(packed, beams, kids.shape[2])
    return merge_call(beams, chained, weights, kids, table)


def padded_lanes(level, width):
    length = level.shape[-1]
    target = -(-width // LANE) * LANE
    if target > length:
        return jnp.pad(level, ((0, 0), (0, 0), (0, target - length)))
    return level[..., :target]


def on_device(raw, filt, tap_index, tap_weight, beam_shift, beam_phase):
    pulse_count = lax.axis_size("pulse")
    parts, local_beams, bins = raw.shape
    taps_len = filt.shape[1]
    local_sections = local_beams.bit_length() - 1
    cross_sections = pulse_count.bit_length() - 1
    sections = local_sections + cross_sections
    extra = sections * MARGIN
    blocks = -(-(bins + extra) // BLOCK)
    reach = -(-(BLOCK + taps_len - 1) // BLOCK)
    rim_len = (blocks + reach - 1) * BLOCK - bins
    rim = shifted(raw[:, :, :rim_len], "range", -1)
    wide = jnp.concatenate([raw, rim], axis=2)
    level = padded_lanes(compress(wide, filt, blocks), bins + extra)
    all_weights = tap_weights(tap_index, tap_weight)
    bits = [((beam_shift >> bit) & 1).astype(jnp.float32) for bit in range(3)]
    all_rows = jnp.stack(bits + [jnp.cos(beam_phase), jnp.sin(beam_phase)])

    def section_rows(beams):
        start = 2 * beams - 2
        return all_rows[:, :, start : start + 2 * beams]

    def run_section(kids, section, beams, chained, table=None):
        return merge_section(kids, beams, chained, all_weights[section], section_rows(beams), table)

    level = split_kids(level, 1)
    for section in range(local_sections):
        level = run_section(level, section, 1 << section, section < local_sections - 1)
    piece_bins = bins // pulse_count
    need = cross_sections * MARGIN
    flat = level[:, :, : bins + need]
    flat = jnp.pad(flat, ((0, 0), (0, 0), (0, piece_bins - need)))
    head = flat[:, :, :bins].reshape(parts, local_beams, pulse_count, piece_bins)
    tail = flat[:, :, piece_bins:].reshape(parts, local_beams, pulse_count, piece_bins)[
        :, :, :, :need
    ]
    pieces = jnp.transpose(jnp.concatenate([head, tail], axis=3), (0, 2, 1, 3))
    cross_rows = pulse_count * local_beams // 2
    tables = [row_table(section_rows(local_beams << bit), local_beams << bit, cross_rows) for bit in range(cross_sections)]
    tables = lax.optimization_barrier(tables)
    level = lax.all_to_all(pieces, "pulse", split_axis=1, concat_axis=1, tiled=True)
    level, tables = lax.optimization_barrier((level, tables))
    level = padded_lanes(level.reshape(parts, pulse_count * local_beams, piece_bins + need), piece_bins + need)
    level = split_kids(level, local_beams)
    for bit in range(cross_sections):
        section = local_sections + bit
        level = run_section(level, section, local_beams << bit, bit < cross_sections - 1, tables[bit])
    level = level[..., :piece_bins].reshape(parts, pulse_count, local_beams, piece_bins)
    level = lax.all_to_all(level, "pulse", split_axis=1, concat_axis=3, tiled=True)
    return level.reshape(parts, local_beams, bins)


def solution(mesh):
    return jax.shard_map(
        on_device,
        mesh=mesh,
        in_specs=(P(None, "pulse", "range"), P(), P(), P(), P(), P()),
        out_specs=P(None, "pulse", "range"),
        check_vma=False,
    )
```

```python
import functools

import jax
import jax.numpy as jnp
from jax import lax
from jax.sharding import PartitionSpec as P
from jax.experimental import pallas as pl
from jax.experimental.pallas import tpu as pltpu

TAPS = 4
MAXOFF = 8
MARGIN = 15
BLOCK = 256
LANE = 128


half_root = 0.7071067811865476


def shifted(shard, axis, by):
    count = lax.axis_size(axis)
    pairs = [(i, i + by) for i in range(count) if 0 <= i + by < count]
    return lax.ppermute(shard, axis, pairs)


def toeplitz_rows(vector, block, rows):
    taps_len = vector.shape[0]
    width = rows + 1
    line = jnp.concatenate([vector, jnp.zeros((width - taps_len,), vector.dtype)])
    return jnp.tile(line, block)[: block * rows].reshape(block, rows)


def band_matrix(filt, block, rows):
    real_band = toeplitz_rows(filt[0], block, rows).T
    imag_band = toeplitz_rows(filt[1], block, rows).T
    upper = jnp.concatenate([real_band, imag_band], axis=1)
    lower = jnp.concatenate([-imag_band, real_band], axis=1)
    return jnp.concatenate([upper, lower], axis=0)


def compress(wide, filt, blocks):
    parts, count, length = wide.shape
    taps_len = filt.shape[1]
    reach = -(-(BLOCK + taps_len - 1) // BLOCK)
    rows = reach * BLOCK
    cut = wide.reshape(parts, count, length // BLOCK, BLOCK)
    window = jnp.concatenate([cut[:, :, c : c + blocks] for c in range(reach)], axis=3)
    segments = jnp.concatenate([window[0], window[1]], axis=2)
    product = lax.dot_general(
        segments,
        band_matrix(filt, BLOCK, rows),
        (((2,), (0,)), ((), ())),
        preferred_element_type=jnp.float32,
    )
    real_part = product[:, :, :BLOCK].reshape(count, blocks * BLOCK)
    imag_part = product[:, :, BLOCK:].reshape(count, blocks * BLOCK)
    return jnp.stack([real_part, imag_part])


def merge_kernel(beams, chained, weight_ref, kid_ref, table_ref, out_ref):
    length = kid_ref.shape[-1]
    reach = MARGIN - MAXOFF + 1
    acc = [[None, None], [None, None]]
    for c in range(2):
        interp = []
        for part in range(2):
            x = kid_ref[c, part]
            total = weight_ref[c, 0] * x
            for offset in range(1, reach):
                total = total + weight_ref[c, offset] * pltpu.roll(x, length - offset, 1)
            interp.append(total)
        for half in range(2):
            moved = []
            for part in range(2):
                pick = interp[part]
                for bit in (2, 1, 0):
                    hit = table_ref[bit, c, half][:, 0:1] > 0.5
                    pick = jnp.where(hit, pltpu.roll(pick, length - (1 << bit), 1), pick)
                moved.append(pick)
            cos_row = table_ref[3, c, half][:, 0:1]
            sin_row = table_ref[4, c, half][:, 0:1]
            real_part = cos_row * moved[0] - sin_row * moved[1]
            imag_part = sin_row * moved[0] + cos_row * moved[1]
            if c == 0:
                acc[half] = [real_part, imag_part]
            else:
                acc[half] = [acc[half][0] + real_part, acc[half][1] + imag_part]
    rows = kid_ref.shape[2]
    for half in range(2):
        for part in range(2):
            value = acc[half][part] * half_root
            for group in range(rows // beams):
                block = value[group * beams : (group + 1) * beams]
                if chained:
                    start = (group // 2) * 2 * beams + half * beams
                    out_ref[group % 2, part, start : start + beams] = block
                else:
                    start = group * 2 * beams + half * beams
                    out_ref[part, start : start + beams] = block


def merge_call(beams, chained, weights, kids, table):
    _, _, rows, length = kids.shape
    vmem = pltpu.VMEM
    elems = 2 * 2 * rows * length
    shape = (2, 2, rows, length) if chained else (2, 2 * rows, length)
    return pl.pallas_call(
        functools.partial(merge_kernel, beams, chained),
        out_shape=jax.ShapeDtypeStruct(shape, jnp.float32),
        in_specs=[
            pl.BlockSpec(memory_space=pltpu.SMEM),
            pl.BlockSpec(memory_space=vmem),
            pl.BlockSpec(memory_space=vmem),
        ],
        out_specs=pl.BlockSpec(memory_space=vmem),
        cost_estimate=pl.CostEstimate(flops=60 * elems, transcendentals=0, bytes_accessed=8 * elems),
    )(weights, kids, table)


def tap_weights(taps, weights):
    reach = MARGIN - MAXOFF + 1
    hit = taps[..., :, None] == jnp.arange(reach, dtype=taps.dtype)
    return jnp.sum(jnp.where(hit, weights[..., :, None], 0.0), axis=-2)


def per_row(table, groups):
    beams = table.shape[-1] // 2
    halves = table.reshape(table.shape[:-1] + (2, beams))
    return jnp.tile(halves, (1,) * (halves.ndim - 1) + (groups,))


def split_kids(level, beams):
    parts, rows, length = level.shape
    groups = rows // (2 * beams)
    pairs = level.reshape(parts, groups, 2, beams, length)
    return jnp.stack([pairs[:, :, c].reshape(parts, rows // 2, length) for c in range(2)])


def row_table(packed, beams, rows):
    return jnp.broadcast_to(per_row(packed, rows // beams)[..., None], (5, 2, 2, rows, LANE))


def merge_section(kids, beams, chained, weights, packed, table=None):
    if table is None:
        table = row_table(packed, beams, kids.shape[2])
    return merge_call(beams, chained, weights, kids, table)


def padded_lanes(level, width):
    length = level.shape[-1]
    target = -(-width // LANE) * LANE
    if target > length:
        return jnp.pad(level, ((0, 0), (0, 0), (0, target - length)))
    return level[..., :target]


def on_device(raw, filt, tap_index, tap_weight, beam_shift, beam_phase):
    pulse_count = lax.axis_size("pulse")
    parts, local_beams, bins = raw.shape
    taps_len = filt.shape[1]
    local_sections = local_beams.bit_length() - 1
    cross_sections = pulse_count.bit_length() - 1
    sections = local_sections + cross_sections
    extra = sections * MARGIN
    blocks = -(-(bins + extra) // BLOCK)
    reach = -(-(BLOCK + taps_len - 1) // BLOCK)
    rim_len = (blocks + reach - 1) * BLOCK - bins
    rim = shifted(raw[:, :, :rim_len], "range", -1)
    wide = jnp.concatenate([raw, rim], axis=2)
    level = padded_lanes(compress(wide, filt, blocks), bins + extra)
    all_weights = tap_weights(tap_index, tap_weight)
    bits = [((beam_shift >> bit) & 1).astype(jnp.float32) for bit in range(3)]
    all_rows = jnp.stack(bits + [jnp.cos(beam_phase), jnp.sin(beam_phase)])

    def section_rows(beams):
        start = 2 * beams - 2
        return all_rows[:, :, start : start + 2 * beams]

    def run_section(kids, section, beams, chained, table=None):
        return merge_section(kids, beams, chained, all_weights[section], section_rows(beams), table)

    level = split_kids(level, 1)
    for section in range(local_sections):
        level = run_section(level, section, 1 << section, section < local_sections - 1)
    piece_bins = bins // pulse_count
    need = cross_sections * MARGIN
    flat = level[:, :, : bins + need]
    flat = jnp.pad(flat, ((0, 0), (0, 0), (0, piece_bins - need)))
    head = flat[:, :, :bins].reshape(parts, local_beams, pulse_count, piece_bins)
    tail = flat[:, :, piece_bins:].reshape(parts, local_beams, pulse_count, piece_bins)[
        :, :, :, :need
    ]
    pieces = jnp.transpose(jnp.concatenate([head, tail], axis=3), (0, 2, 1, 3))
    cross_rows = pulse_count * local_beams // 2
    sources = [section_rows(local_beams << bit) for bit in range(cross_sections)]
    pieces, sources = lax.optimization_barrier((pieces, sources))
    tables = [row_table(sources[bit], local_beams << bit, cross_rows) for bit in range(cross_sections)]
    tables = lax.optimization_barrier(tables)
    level = lax.all_to_all(pieces, "pulse", split_axis=1, concat_axis=1, tiled=True)
    level, tables = lax.optimization_barrier((level, tables))
    level = padded_lanes(level.reshape(parts, pulse_count * local_beams, piece_bins + need), piece_bins + need)
    level = split_kids(level, local_beams)
    for bit in range(cross_sections):
        section = local_sections + bit
        level = run_section(level, section, local_beams << bit, bit < cross_sections - 1, tables[bit])
    level = level[..., :piece_bins].reshape(parts, pulse_count, local_beams, piece_bins)
    level = lax.all_to_all(level, "pulse", split_axis=1, concat_axis=3, tiled=True)
    return level.reshape(parts, local_beams, bins)


def solution(mesh):
    return jax.shard_map(
        on_device,
        mesh=mesh,
        in_specs=(P(None, "pulse", "range"), P(), P(), P(), P(), P()),
        out_specs=P(None, "pulse", "range"),
        check_vma=False,
    )
```

```python
import functools

import jax
import jax.numpy as jnp
from jax import lax
from jax.sharding import PartitionSpec as P
from jax.experimental import pallas as pl
from jax.experimental.pallas import tpu as pltpu

TAPS = 4
MAXOFF = 8
MARGIN = 15
BLOCK = 256
LANE = 128


half_root = 0.7071067811865476


def shifted(shard, axis, by):
    count = lax.axis_size(axis)
    pairs = [(i, i + by) for i in range(count) if 0 <= i + by < count]
    return lax.ppermute(shard, axis, pairs)


def toeplitz_rows(vector, block, rows):
    taps_len = vector.shape[0]
    width = rows + 1
    line = jnp.concatenate([vector, jnp.zeros((width - taps_len,), vector.dtype)])
    return jnp.tile(line, block)[: block * rows].reshape(block, rows)


def band_matrix(filt, block, rows):
    real_band = toeplitz_rows(filt[0], block, rows).T
    imag_band = toeplitz_rows(filt[1], block, rows).T
    upper = jnp.concatenate([real_band, imag_band], axis=1)
    lower = jnp.concatenate([-imag_band, real_band], axis=1)
    return jnp.concatenate([upper, lower], axis=0)


def compress(wide, filt, blocks):
    parts, count, length = wide.shape
    taps_len = filt.shape[1]
    reach = -(-(BLOCK + taps_len - 1) // BLOCK)
    rows = reach * BLOCK
    cut = wide.reshape(parts, count, length // BLOCK, BLOCK)
    window = jnp.concatenate([cut[:, :, c : c + blocks] for c in range(reach)], axis=3)
    segments = jnp.concatenate([window[0], window[1]], axis=2)
    product = lax.dot_general(
        segments,
        band_matrix(filt, BLOCK, rows),
        (((2,), (0,)), ((), ())),
        preferred_element_type=jnp.float32,
    )
    real_part = product[:, :, :BLOCK].reshape(count, blocks * BLOCK)
    imag_part = product[:, :, BLOCK:].reshape(count, blocks * BLOCK)
    return jnp.stack([real_part, imag_part])


def merge_kernel(beams, chained, weight_ref, kid_ref, table_ref, out_ref):
    length = kid_ref.shape[-1]
    reach = MARGIN - MAXOFF + 1
    acc = [[None, None], [None, None]]
    for c in range(2):
        interp = []
        for part in range(2):
            x = kid_ref[c, part]
            total = weight_ref[c, 0] * x
            for offset in range(1, reach):
                total = total + weight_ref[c, offset] * pltpu.roll(x, length - offset, 1)
            interp.append(total)
        for half in range(2):
            moved = []
            for part in range(2):
                pick = interp[part]
                for bit in (2, 1, 0):
                    hit = table_ref[bit, c, half][:, 0:1] > 0.5
                    pick = jnp.where(hit, pltpu.roll(pick, length - (1 << bit), 1), pick)
                moved.append(pick)
            cos_row = table_ref[3, c, half][:, 0:1]
            sin_row = table_ref[4, c, half][:, 0:1]
            real_part = cos_row * moved[0] - sin_row * moved[1]
            imag_part = sin_row * moved[0] + cos_row * moved[1]
            if c == 0:
                acc[half] = [real_part, imag_part]
            else:
                acc[half] = [acc[half][0] + real_part, acc[half][1] + imag_part]
    rows = kid_ref.shape[2]
    for half in range(2):
        for part in range(2):
            value = acc[half][part] * half_root
            for group in range(rows // beams):
                block = value[group * beams : (group + 1) * beams]
                if chained:
                    start = (group // 2) * 2 * beams + half * beams
                    out_ref[group % 2, part, start : start + beams] = block
                else:
                    start = group * 2 * beams + half * beams
                    out_ref[part, start : start + beams] = block


def merge_call(beams, chained, weights, kids, table):
    _, _, rows, length = kids.shape
    vmem = pltpu.VMEM
    elems = 2 * 2 * rows * length
    shape = (2, 2, rows, length) if chained else (2, 2 * rows, length)
    return pl.pallas_call(
        functools.partial(merge_kernel, beams, chained),
        out_shape=jax.ShapeDtypeStruct(shape, jnp.float32),
        in_specs=[
            pl.BlockSpec(memory_space=pltpu.SMEM),
            pl.BlockSpec(memory_space=vmem),
            pl.BlockSpec(memory_space=vmem),
        ],
        out_specs=pl.BlockSpec(memory_space=vmem),
        cost_estimate=pl.CostEstimate(flops=60 * elems, transcendentals=0, bytes_accessed=8 * elems),
    )(weights, kids, table)


def tap_weights(taps, weights):
    reach = MARGIN - MAXOFF + 1
    hit = taps[..., :, None] == jnp.arange(reach, dtype=taps.dtype)
    return jnp.sum(jnp.where(hit, weights[..., :, None], 0.0), axis=-2)


def per_row(table, groups):
    beams = table.shape[-1] // 2
    halves = table.reshape(table.shape[:-1] + (2, beams))
    return jnp.tile(halves, (1,) * (halves.ndim - 1) + (groups,))


def split_kids(level, beams):
    parts, rows, length = level.shape
    groups = rows // (2 * beams)
    pairs = level.reshape(parts, groups, 2, beams, length)
    return jnp.stack([pairs[:, :, c].reshape(parts, rows // 2, length) for c in range(2)])


def row_table(packed, beams, rows):
    return jnp.broadcast_to(per_row(packed, rows // beams)[..., None], (5, 2, 2, rows, LANE))


def merge_section(kids, beams, chained, weights, packed, table=None):
    if table is None:
        table = row_table(packed, beams, kids.shape[2])
    return merge_call(beams, chained, weights, kids, table)


def padded_lanes(level, width):
    length = level.shape[-1]
    target = -(-width // LANE) * LANE
    if target > length:
        return jnp.pad(level, ((0, 0), (0, 0), (0, target - length)))
    return level[..., :target]


def on_device(raw, filt, tap_index, tap_weight, beam_shift, beam_phase):
    pulse_count = lax.axis_size("pulse")
    parts, local_beams, bins = raw.shape
    taps_len = filt.shape[1]
    local_sections = local_beams.bit_length() - 1
    cross_sections = pulse_count.bit_length() - 1
    sections = local_sections + cross_sections
    extra = sections * MARGIN
    blocks = -(-(bins + extra) // BLOCK)
    reach = -(-(BLOCK + taps_len - 1) // BLOCK)
    rim_len = (blocks + reach - 1) * BLOCK - bins
    rim = shifted(raw[:, :, :rim_len], "range", -1)
    wide = jnp.concatenate([raw, rim], axis=2)
    level = padded_lanes(compress(wide, filt, blocks), bins + extra)
    all_weights = tap_weights(tap_index, tap_weight)
    bits = [((beam_shift >> bit) & 1).astype(jnp.float32) for bit in range(3)]
    all_rows = jnp.stack(bits + [jnp.cos(beam_phase), jnp.sin(beam_phase)])

    def section_rows(beams):
        start = 2 * beams - 2
        return all_rows[:, :, start : start + 2 * beams]

    def run_section(kids, section, beams, chained, table=None):
        return merge_section(kids, beams, chained, all_weights[section], section_rows(beams), table)

    level = split_kids(level, 1)
    for section in range(local_sections):
        level = run_section(level, section, 1 << section, section < local_sections - 1)
    piece_bins = bins // pulse_count
    need = cross_sections * MARGIN
    chunk_beams = local_beams // 2
    outputs = []
    for chunk in range(2):
        flat = level[:, chunk * chunk_beams : (chunk + 1) * chunk_beams, : bins + need]
        flat = jnp.pad(flat, ((0, 0), (0, 0), (0, piece_bins - need)))
        head = flat[:, :, :bins].reshape(parts, chunk_beams, pulse_count, piece_bins)
        tail = flat[:, :, piece_bins:].reshape(parts, chunk_beams, pulse_count, piece_bins)[
            :, :, :, :need
        ]
        pieces = jnp.transpose(jnp.concatenate([head, tail], axis=3), (0, 2, 1, 3))
        cross_rows = pulse_count * chunk_beams // 2
        sources = []
        for bit in range(cross_sections):
            beams = local_beams << bit
            first = 2 * beams - 2
            picks = [
                first + (g // chunk_beams) * local_beams + chunk * chunk_beams + g % chunk_beams
                for g in range(2 * (chunk_beams << bit))
            ]
            sources.append(all_rows[:, :, jnp.array(picks, dtype=jnp.int32)])
        pieces, sources = lax.optimization_barrier((pieces, sources))
        tables = [
            row_table(sources[bit], chunk_beams << bit, cross_rows) for bit in range(cross_sections)
        ]
        tables = lax.optimization_barrier(tables)
        part = lax.all_to_all(pieces, "pulse", split_axis=1, concat_axis=1, tiled=True)
        part, tables = lax.optimization_barrier((part, tables))
        part = padded_lanes(part.reshape(parts, pulse_count * chunk_beams, piece_bins + need), piece_bins + need)
        part = split_kids(part, chunk_beams)
        for bit in range(cross_sections):
            section = local_sections + bit
            part = merge_section(
                part,
                chunk_beams << bit,
                bit < cross_sections - 1,
                all_weights[section],
                None,
                tables[bit],
            )
        part = part[..., :piece_bins].reshape(parts, pulse_count, chunk_beams, piece_bins)
        part = lax.all_to_all(part, "pulse", split_axis=1, concat_axis=3, tiled=True)
        outputs.append(part.reshape(parts, chunk_beams, bins))
    return jnp.concatenate(outputs, axis=1)


def solution(mesh):
    return jax.shard_map(
        on_device,
        mesh=mesh,
        in_specs=(P(None, "pulse", "range"), P(), P(), P(), P(), P()),
        out_specs=P(None, "pulse", "range"),
        check_vma=False,
    )
```

```python
import functools

import jax
import jax.numpy as jnp
from jax import lax
from jax.sharding import PartitionSpec as P
from jax.experimental import pallas as pl
from jax.experimental.pallas import tpu as pltpu

TAPS = 4
MAXOFF = 8
MARGIN = 15
BLOCK = 256
LANE = 128


half_root = 0.7071067811865476


def shifted(shard, axis, by):
    count = lax.axis_size(axis)
    pairs = [(i, i + by) for i in range(count) if 0 <= i + by < count]
    return lax.ppermute(shard, axis, pairs)


def toeplitz_rows(vector, block, rows):
    taps_len = vector.shape[0]
    width = rows + 1
    line = jnp.concatenate([vector, jnp.zeros((width - taps_len,), vector.dtype)])
    return jnp.tile(line, block)[: block * rows].reshape(block, rows)


def band_matrix(filt, block, rows):
    real_band = toeplitz_rows(filt[0], block, rows).T
    imag_band = toeplitz_rows(filt[1], block, rows).T
    upper = jnp.concatenate([real_band, imag_band], axis=1)
    lower = jnp.concatenate([-imag_band, real_band], axis=1)
    return jnp.concatenate([upper, lower], axis=0)


def compress(wide, filt, blocks):
    parts, count, length = wide.shape
    taps_len = filt.shape[1]
    reach = -(-(BLOCK + taps_len - 1) // BLOCK)
    rows = reach * BLOCK
    cut = wide.reshape(parts, count, length // BLOCK, BLOCK)
    window = jnp.concatenate([cut[:, :, c : c + blocks] for c in range(reach)], axis=3)
    segments = jnp.concatenate([window[0], window[1]], axis=2)
    product = lax.dot_general(
        segments,
        band_matrix(filt, BLOCK, rows),
        (((2,), (0,)), ((), ())),
        preferred_element_type=jnp.float32,
    )
    real_part = product[:, :, :BLOCK].reshape(count, blocks * BLOCK)
    imag_part = product[:, :, BLOCK:].reshape(count, blocks * BLOCK)
    return jnp.stack([real_part, imag_part])


def merge_kernel(beams, chained, weight_ref, kid_ref, table_ref, out_ref):
    length = kid_ref.shape[-1]
    reach = MARGIN - MAXOFF + 1
    acc = [[None, None], [None, None]]
    for c in range(2):
        interp = []
        for part in range(2):
            x = kid_ref[c, part]
            total = weight_ref[c, 0] * x
            for offset in range(1, reach):
                total = total + weight_ref[c, offset] * pltpu.roll(x, length - offset, 1)
            interp.append(total)
        for half in range(2):
            moved = []
            for part in range(2):
                pick = interp[part]
                for bit in (2, 1, 0):
                    hit = table_ref[bit, c, half][:, 0:1] > 0.5
                    pick = jnp.where(hit, pltpu.roll(pick, length - (1 << bit), 1), pick)
                moved.append(pick)
            cos_row = table_ref[3, c, half][:, 0:1]
            sin_row = table_ref[4, c, half][:, 0:1]
            real_part = cos_row * moved[0] - sin_row * moved[1]
            imag_part = sin_row * moved[0] + cos_row * moved[1]
            if c == 0:
                acc[half] = [real_part, imag_part]
            else:
                acc[half] = [acc[half][0] + real_part, acc[half][1] + imag_part]
    rows = kid_ref.shape[2]
    for half in range(2):
        for part in range(2):
            value = acc[half][part] * half_root
            for group in range(rows // beams):
                block = value[group * beams : (group + 1) * beams]
                if chained:
                    start = (group // 2) * 2 * beams + half * beams
                    out_ref[group % 2, part, start : start + beams] = block
                else:
                    start = group * 2 * beams + half * beams
                    out_ref[part, start : start + beams] = block


def merge_call(beams, chained, weights, kids, table):
    _, _, rows, length = kids.shape
    vmem = pltpu.VMEM
    elems = 2 * 2 * rows * length
    shape = (2, 2, rows, length) if chained else (2, 2 * rows, length)
    return pl.pallas_call(
        functools.partial(merge_kernel, beams, chained),
        out_shape=jax.ShapeDtypeStruct(shape, jnp.float32),
        in_specs=[
            pl.BlockSpec(memory_space=pltpu.SMEM),
            pl.BlockSpec(memory_space=vmem),
            pl.BlockSpec(memory_space=vmem),
        ],
        out_specs=pl.BlockSpec(memory_space=vmem),
        cost_estimate=pl.CostEstimate(flops=60 * elems, transcendentals=0, bytes_accessed=8 * elems),
    )(weights, kids, table)


def tap_weights(taps, weights):
    reach = MARGIN - MAXOFF + 1
    hit = taps[..., :, None] == jnp.arange(reach, dtype=taps.dtype)
    return jnp.sum(jnp.where(hit, weights[..., :, None], 0.0), axis=-2)


def per_row(table, groups):
    beams = table.shape[-1] // 2
    halves = table.reshape(table.shape[:-1] + (2, beams))
    return jnp.tile(halves, (1,) * (halves.ndim - 1) + (groups,))


def split_kids(level, beams):
    parts, rows, length = level.shape
    groups = rows // (2 * beams)
    pairs = level.reshape(parts, groups, 2, beams, length)
    return jnp.stack([pairs[:, :, c].reshape(parts, rows // 2, length) for c in range(2)])


def row_table(packed, beams, rows):
    return jnp.broadcast_to(per_row(packed, rows // beams)[..., None], (5, 2, 2, rows, LANE))


def merge_section(kids, beams, chained, weights, packed, table=None):
    if table is None:
        table = row_table(packed, beams, kids.shape[2])
    return merge_call(beams, chained, weights, kids, table)


def padded_lanes(level, width):
    length = level.shape[-1]
    target = -(-width // LANE) * LANE
    if target > length:
        return jnp.pad(level, ((0, 0), (0, 0), (0, target - length)))
    return level[..., :target]


def on_device(raw, filt, tap_index, tap_weight, beam_shift, beam_phase):
    pulse_count = lax.axis_size("pulse")
    parts, local_beams, bins = raw.shape
    taps_len = filt.shape[1]
    local_sections = local_beams.bit_length() - 1
    cross_sections = pulse_count.bit_length() - 1
    sections = local_sections + cross_sections
    extra = sections * MARGIN
    blocks = -(-(bins + extra) // BLOCK)
    reach = -(-(BLOCK + taps_len - 1) // BLOCK)
    rim_len = (blocks + reach - 1) * BLOCK - bins
    rim = shifted(raw[:, :, :rim_len], "range", -1)
    wide = jnp.concatenate([raw, rim], axis=2)
    level = padded_lanes(compress(wide, filt, blocks), bins + extra)
    all_weights = tap_weights(tap_index, tap_weight)
    bits = [((beam_shift >> bit) & 1).astype(jnp.float32) for bit in range(3)]
    all_rows = jnp.stack(bits + [jnp.cos(beam_phase), jnp.sin(beam_phase)])

    def section_rows(beams):
        start = 2 * beams - 2
        return all_rows[:, :, start : start + 2 * beams]

    def run_section(kids, section, beams, chained, table=None):
        return merge_section(kids, beams, chained, all_weights[section], section_rows(beams), table)

    level = split_kids(level, 1)
    for section in range(local_sections):
        level = run_section(level, section, 1 << section, section < local_sections - 1)
    piece_bins = bins // pulse_count
    need = cross_sections * MARGIN
    flat = level[:, :, : bins + need]
    flat = jnp.pad(flat, ((0, 0), (0, 0), (0, piece_bins - need)))
    head = flat[:, :, :bins].reshape(parts, local_beams, pulse_count, piece_bins)
    tail = flat[:, :, piece_bins:].reshape(parts, local_beams, pulse_count, piece_bins)[
        :, :, :, :need
    ]
    pieces = jnp.transpose(jnp.concatenate([head, tail], axis=3), (2, 0, 1, 3))
    cross_rows = pulse_count * local_beams // 2
    tables = [row_table(section_rows(local_beams << bit), local_beams << bit, cross_rows) for bit in range(cross_sections)]
    tables = lax.optimization_barrier(tables)
    level = lax.all_to_all(pieces, "pulse", split_axis=0, concat_axis=0, tiled=True)
    level, tables = lax.optimization_barrier((level, tables))
    level = jnp.transpose(level, (1, 0, 2, 3))
    level = padded_lanes(level.reshape(parts, pulse_count * local_beams, piece_bins + need), piece_bins + need)
    level = split_kids(level, local_beams)
    for bit in range(cross_sections):
        section = local_sections + bit
        level = run_section(level, section, local_beams << bit, bit < cross_sections - 1, tables[bit])
    level = level[..., :piece_bins].reshape(parts, pulse_count, local_beams, piece_bins)
    level = jnp.transpose(level, (1, 0, 2, 3))
    level = lax.all_to_all(level, "pulse", split_axis=0, concat_axis=0, tiled=True)
    return jnp.transpose(level, (1, 2, 0, 3)).reshape(parts, local_beams, bins)


def solution(mesh):
    return jax.shard_map(
        on_device,
        mesh=mesh,
        in_specs=(P(None, "pulse", "range"), P(), P(), P(), P(), P()),
        out_specs=P(None, "pulse", "range"),
        check_vma=False,
    )
```

```python
import functools

import jax
import jax.numpy as jnp
from jax import lax
from jax.sharding import PartitionSpec as P
from jax.experimental import pallas as pl
from jax.experimental.pallas import tpu as pltpu

TAPS = 4
MAXOFF = 8
MARGIN = 15
BLOCK = 256
LANE = 128


half_root = 0.7071067811865476


def shifted(shard, axis, by):
    count = lax.axis_size(axis)
    pairs = [(i, i + by) for i in range(count) if 0 <= i + by < count]
    return lax.ppermute(shard, axis, pairs)


def toeplitz_rows(filt, block, rows):
    taps_len = filt.shape[1]
    width = rows + 1
    line = jnp.concatenate([filt, jnp.zeros((filt.shape[0], width - taps_len), filt.dtype)], axis=1)
    return jnp.tile(line, (1, block))[:, : block * rows].reshape(filt.shape[0], block, rows)


def band_matrix(filt, block, rows):
    bands = toeplitz_rows(filt, block, rows)
    real_band = bands[0].T
    imag_band = bands[1].T
    upper = jnp.concatenate([real_band, imag_band], axis=1)
    lower = jnp.concatenate([-imag_band, real_band], axis=1)
    return jnp.concatenate([upper, lower], axis=0)


def compress(wide, filt, blocks):
    parts, count, length = wide.shape
    taps_len = filt.shape[1]
    reach = -(-(BLOCK + taps_len - 1) // BLOCK)
    rows = reach * BLOCK
    cut = wide.reshape(parts, count, length // BLOCK, BLOCK)
    window = jnp.concatenate([cut[:, :, c : c + blocks] for c in range(reach)], axis=3)
    segments = jnp.concatenate([window[0], window[1]], axis=2)
    product = lax.dot_general(
        segments,
        band_matrix(filt, BLOCK, rows),
        (((2,), (0,)), ((), ())),
        preferred_element_type=jnp.float32,
    )
    real_part = product[:, :, :BLOCK].reshape(count, blocks * BLOCK)
    imag_part = product[:, :, BLOCK:].reshape(count, blocks * BLOCK)
    return jnp.stack([real_part, imag_part])


def merge_kernel(beams, chained, weight_ref, kid_ref, table_ref, out_ref):
    length = kid_ref.shape[-1]
    reach = MARGIN - MAXOFF + 1
    acc = [[None, None], [None, None]]
    for c in range(2):
        interp = []
        for part in range(2):
            x = kid_ref[c, part]
            total = weight_ref[c, 0] * x
            for offset in range(1, reach):
                total = total + weight_ref[c, offset] * pltpu.roll(x, length - offset, 1)
            interp.append(total)
        for half in range(2):
            moved = []
            for part in range(2):
                pick = interp[part]
                for bit in (2, 1, 0):
                    hit = table_ref[bit, c, half][:, 0:1] > 0.5
                    pick = jnp.where(hit, pltpu.roll(pick, length - (1 << bit), 1), pick)
                moved.append(pick)
            cos_row = table_ref[3, c, half][:, 0:1]
            sin_row = table_ref[4, c, half][:, 0:1]
            real_part = cos_row * moved[0] - sin_row * moved[1]
            imag_part = sin_row * moved[0] + cos_row * moved[1]
            if c == 0:
                acc[half] = [real_part, imag_part]
            else:
                acc[half] = [acc[half][0] + real_part, acc[half][1] + imag_part]
    rows = kid_ref.shape[2]
    for half in range(2):
        for part in range(2):
            value = acc[half][part] * half_root
            for group in range(rows // beams):
                block = value[group * beams : (group + 1) * beams]
                if chained:
                    start = (group // 2) * 2 * beams + half * beams
                    out_ref[group % 2, part, start : start + beams] = block
                else:
                    start = group * 2 * beams + half * beams
                    out_ref[part, start : start + beams] = block


def merge_call(beams, chained, weights, kids, table):
    _, _, rows, length = kids.shape
    vmem = pltpu.VMEM
    elems = 2 * 2 * rows * length
    shape = (2, 2, rows, length) if chained else (2, 2 * rows, length)
    return pl.pallas_call(
        functools.partial(merge_kernel, beams, chained),
        out_shape=jax.ShapeDtypeStruct(shape, jnp.float32),
        in_specs=[
            pl.BlockSpec(memory_space=pltpu.SMEM),
            pl.BlockSpec(memory_space=vmem),
            pl.BlockSpec(memory_space=vmem),
        ],
        out_specs=pl.BlockSpec(memory_space=vmem),
        cost_estimate=pl.CostEstimate(flops=60 * elems, transcendentals=0, bytes_accessed=8 * elems),
    )(weights, kids, table)


def tap_weights(taps, weights):
    spots = jnp.arange(MARGIN - MAXOFF + 1, dtype=taps.dtype)
    total = jnp.where(taps[..., 0, None] == spots, weights[..., 0, None], 0.0)
    for tap in range(1, taps.shape[-1]):
        total = total + jnp.where(taps[..., tap, None] == spots, weights[..., tap, None], 0.0)
    return total


def per_row(table, groups):
    beams = table.shape[-1] // 2
    halves = table.reshape(table.shape[:-1] + (2, beams))
    return jnp.tile(halves, (1,) * (halves.ndim - 1) + (groups,))


def split_kids(level, beams):
    parts, rows, length = level.shape
    groups = rows // (2 * beams)
    pairs = level.reshape(parts, groups, 2, beams, length)
    return jnp.stack([pairs[:, :, c].reshape(parts, rows // 2, length) for c in range(2)])


def row_table(packed, beams, rows):
    return jnp.broadcast_to(per_row(packed, rows // beams)[..., None], (5, 2, 2, rows, LANE))


def merge_section(kids, beams, chained, weights, packed, table=None):
    if table is None:
        table = row_table(packed, beams, kids.shape[2])
    return merge_call(beams, chained, weights, kids, table)


def padded_lanes(level, width):
    length = level.shape[-1]
    target = -(-width // LANE) * LANE
    if target > length:
        return jnp.pad(level, ((0, 0), (0, 0), (0, target - length)))
    return level[..., :target]


def on_device(raw, filt, tap_index, tap_weight, beam_shift, beam_phase):
    pulse_count = lax.axis_size("pulse")
    parts, local_beams, bins = raw.shape
    taps_len = filt.shape[1]
    local_sections = local_beams.bit_length() - 1
    cross_sections = pulse_count.bit_length() - 1
    sections = local_sections + cross_sections
    extra = sections * MARGIN
    blocks = -(-(bins + extra) // BLOCK)
    reach = -(-(BLOCK + taps_len - 1) // BLOCK)
    rim_len = (blocks + reach - 1) * BLOCK - bins
    rim = shifted(raw[:, :, :rim_len], "range", -1)
    wide = jnp.concatenate([raw, rim], axis=2)
    level = padded_lanes(compress(wide, filt, blocks), bins + extra)
    all_weights = tap_weights(tap_index, tap_weight)
    kind = lax.broadcasted_iota(jnp.int32, (5,) + beam_shift.shape, 0)
    bit_rows = ((beam_shift[None] >> jnp.minimum(kind, 2)) & 1).astype(jnp.float32)
    angle_rows = jnp.where(kind == 3, jnp.cos(beam_phase)[None], jnp.sin(beam_phase)[None])
    all_rows = jnp.where(kind < 3, bit_rows, angle_rows)

    def section_rows(beams):
        start = 2 * beams - 2
        return all_rows[:, :, start : start + 2 * beams]

    def run_section(kids, section, beams, chained, table=None):
        return merge_section(kids, beams, chained, all_weights[section], section_rows(beams), table)

    level = split_kids(level, 1)
    for section in range(local_sections):
        level = run_section(level, section, 1 << section, section < local_sections - 1)
    piece_bins = bins // pulse_count
    need = cross_sections * MARGIN
    flat = level[:, :, : bins + need]
    flat = jnp.pad(flat, ((0, 0), (0, 0), (0, piece_bins - need)))
    head = flat[:, :, :bins].reshape(parts, local_beams, pulse_count, piece_bins)
    tail = flat[:, :, piece_bins:].reshape(parts, local_beams, pulse_count, piece_bins)[
        :, :, :, :need
    ]
    pieces = jnp.transpose(jnp.concatenate([head, tail], axis=3), (2, 0, 1, 3))
    cross_rows = pulse_count * local_beams // 2
    tables = [row_table(section_rows(local_beams << bit), local_beams << bit, cross_rows) for bit in range(cross_sections)]
    tables = lax.optimization_barrier(tables)
    level = lax.all_to_all(pieces, "pulse", split_axis=0, concat_axis=0, tiled=True)
    level, tables = lax.optimization_barrier((level, tables))
    level = jnp.transpose(level, (1, 0, 2, 3))
    level = padded_lanes(level.reshape(parts, pulse_count * local_beams, piece_bins + need), piece_bins + need)
    level = split_kids(level, local_beams)
    for bit in range(cross_sections):
        section = local_sections + bit
        level = run_section(level, section, local_beams << bit, bit < cross_sections - 1, tables[bit])
    level = level[..., :piece_bins].reshape(parts, pulse_count, local_beams, piece_bins)
    level = jnp.transpose(level, (1, 0, 2, 3))
    level = lax.all_to_all(level, "pulse", split_axis=0, concat_axis=0, tiled=True)
    return jnp.transpose(level, (1, 2, 0, 3)).reshape(parts, local_beams, bins)


def solution(mesh):
    return jax.shard_map(
        on_device,
        mesh=mesh,
        in_specs=(P(None, "pulse", "range"), P(), P(), P(), P(), P()),
        out_specs=P(None, "pulse", "range"),
        check_vma=False,
    )
```

```python
import functools

import jax
import jax.numpy as jnp
from jax import lax
from jax.sharding import PartitionSpec as P
from jax.experimental import pallas as pl
from jax.experimental.pallas import tpu as pltpu

TAPS = 4
MAXOFF = 8
MARGIN = 15
BLOCK = 256
LANE = 128


half_root = 0.7071067811865476


def shifted(shard, axis, by):
    count = lax.axis_size(axis)
    pairs = [(i, i + by) for i in range(count) if 0 <= i + by < count]
    return lax.ppermute(shard, axis, pairs)


def toeplitz_rows(vector, block, rows):
    taps_len = vector.shape[0]
    width = rows + 1
    line = jnp.concatenate([vector, jnp.zeros((width - taps_len,), vector.dtype)])
    return jnp.tile(line, block)[: block * rows].reshape(block, rows)


def band_matrix(filt, block, rows):
    real_band = toeplitz_rows(filt[0], block, rows).T
    imag_band = toeplitz_rows(filt[1], block, rows).T
    upper = jnp.concatenate([real_band, imag_band], axis=1)
    lower = jnp.concatenate([-imag_band, real_band], axis=1)
    return jnp.concatenate([upper, lower], axis=0)


def compress(wide, filt, blocks):
    parts, count, length = wide.shape
    taps_len = filt.shape[1]
    reach = -(-(BLOCK + taps_len - 1) // BLOCK)
    rows = reach * BLOCK
    cut = wide.reshape(parts, count, length // BLOCK, BLOCK)
    window = jnp.concatenate([cut[:, :, c : c + blocks] for c in range(reach)], axis=3)
    segments = jnp.concatenate([window[0], window[1]], axis=2)
    product = lax.dot_general(
        segments,
        band_matrix(filt, BLOCK, rows),
        (((2,), (0,)), ((), ())),
        preferred_element_type=jnp.float32,
    )
    real_part = product[:, :, :BLOCK].reshape(count, blocks * BLOCK)
    imag_part = product[:, :, BLOCK:].reshape(count, blocks * BLOCK)
    return jnp.stack([real_part, imag_part])


def merge_kernel(beams, chained, weight_ref, kid_ref, table_ref, out_ref):
    length = kid_ref.shape[-1]
    reach = MARGIN - MAXOFF + 1
    acc = [[None, None], [None, None]]
    for c in range(2):
        interp = []
        for part in range(2):
            x = kid_ref[c, part]
            total = weight_ref[c, 0] * x
            for offset in range(1, reach):
                total = total + weight_ref[c, offset] * pltpu.roll(x, length - offset, 1)
            interp.append(total)
        for half in range(2):
            moved = []
            for part in range(2):
                pick = interp[part]
                for bit in (2, 1, 0):
                    hit = table_ref[bit, c, half][:, 0:1] > 0.5
                    pick = jnp.where(hit, pltpu.roll(pick, length - (1 << bit), 1), pick)
                moved.append(pick)
            cos_row = table_ref[3, c, half][:, 0:1]
            sin_row = table_ref[4, c, half][:, 0:1]
            real_part = cos_row * moved[0] - sin_row * moved[1]
            imag_part = sin_row * moved[0] + cos_row * moved[1]
            if c == 0:
                acc[half] = [real_part, imag_part]
            else:
                acc[half] = [acc[half][0] + real_part, acc[half][1] + imag_part]
    rows = kid_ref.shape[2]
    for half in range(2):
        for part in range(2):
            value = acc[half][part] * half_root
            for group in range(rows // beams):
                block = value[group * beams : (group + 1) * beams]
                if chained:
                    start = (group // 2) * 2 * beams + half * beams
                    out_ref[group % 2, part, start : start + beams] = block
                else:
                    start = group * 2 * beams + half * beams
                    out_ref[part, start : start + beams] = block


def merge_call(beams, chained, weights, kids, table):
    _, _, rows, length = kids.shape
    vmem = pltpu.VMEM
    elems = 2 * 2 * rows * length
    shape = (2, 2, rows, length) if chained else (2, 2 * rows, length)
    return pl.pallas_call(
        functools.partial(merge_kernel, beams, chained),
        out_shape=jax.ShapeDtypeStruct(shape, jnp.float32),
        in_specs=[
            pl.BlockSpec(memory_space=pltpu.SMEM),
            pl.BlockSpec(memory_space=vmem),
            pl.BlockSpec(memory_space=vmem),
        ],
        out_specs=pl.BlockSpec(memory_space=vmem),
        cost_estimate=pl.CostEstimate(flops=60 * elems, transcendentals=0, bytes_accessed=8 * elems),
    )(weights, kids, table)


def tap_weights(taps, weights):
    spots = jnp.arange(MARGIN - MAXOFF + 1, dtype=taps.dtype)
    total = jnp.where(taps[..., 0, None] == spots, weights[..., 0, None], 0.0)
    for tap in range(1, taps.shape[-1]):
        total = total + jnp.where(taps[..., tap, None] == spots, weights[..., tap, None], 0.0)
    return total


def per_row(table, groups):
    beams = table.shape[-1] // 2
    halves = table.reshape(table.shape[:-1] + (2, beams))
    return jnp.tile(halves, (1,) * (halves.ndim - 1) + (groups,))


def split_kids(level, beams):
    parts, rows, length = level.shape
    groups = rows // (2 * beams)
    pairs = level.reshape(parts, groups, 2, beams, length)
    return jnp.stack([pairs[:, :, c].reshape(parts, rows // 2, length) for c in range(2)])


def row_table(packed, beams, rows):
    return jnp.broadcast_to(per_row(packed, rows // beams)[..., None], (5, 2, 2, rows, LANE))


def merge_section(kids, beams, chained, weights, packed, table=None):
    if table is None:
        table = row_table(packed, beams, kids.shape[2])
    return merge_call(beams, chained, weights, kids, table)


def padded_lanes(level, width):
    length = level.shape[-1]
    target = -(-width // LANE) * LANE
    if target > length:
        return jnp.pad(level, ((0, 0), (0, 0), (0, target - length)))
    return level[..., :target]


def on_device(raw, filt, tap_index, tap_weight, beam_shift, beam_phase):
    pulse_count = lax.axis_size("pulse")
    parts, local_beams, bins = raw.shape
    taps_len = filt.shape[1]
    local_sections = local_beams.bit_length() - 1
    cross_sections = pulse_count.bit_length() - 1
    sections = local_sections + cross_sections
    extra = sections * MARGIN
    blocks = -(-(bins + extra) // BLOCK)
    reach = -(-(BLOCK + taps_len - 1) // BLOCK)
    rim_len = (blocks + reach - 1) * BLOCK - bins
    rim = shifted(raw[:, :, :rim_len], "range", -1)
    wide = jnp.concatenate([raw, rim], axis=2)
    level = padded_lanes(compress(wide, filt, blocks), bins + extra)
    all_weights = tap_weights(tap_index, tap_weight)
    kind = lax.broadcasted_iota(jnp.int32, (5,) + beam_shift.shape, 0)
    bit_rows = ((beam_shift[None] >> jnp.minimum(kind, 2)) & 1).astype(jnp.float32)
    angle_rows = jnp.where(kind == 3, jnp.cos(beam_phase)[None], jnp.sin(beam_phase)[None])
    all_rows = jnp.where(kind < 3, bit_rows, angle_rows)

    def section_rows(beams):
        start = 2 * beams - 2
        return all_rows[:, :, start : start + 2 * beams]

    def run_section(kids, section, beams, chained, table=None):
        return merge_section(kids, beams, chained, all_weights[section], section_rows(beams), table)

    level = split_kids(level, 1)
    for section in range(local_sections):
        level = run_section(level, section, 1 << section, section < local_sections - 1)
    piece_bins = bins // pulse_count
    need = cross_sections * MARGIN
    flat = level[:, :, : bins + need]
    flat = jnp.pad(flat, ((0, 0), (0, 0), (0, piece_bins - need)))
    head = flat[:, :, :bins].reshape(parts, local_beams, pulse_count, piece_bins)
    tail = flat[:, :, piece_bins:].reshape(parts, local_beams, pulse_count, piece_bins)[
        :, :, :, :need
    ]
    pieces = jnp.transpose(jnp.concatenate([head, tail], axis=3), (2, 0, 1, 3))
    cross_rows = pulse_count * local_beams // 2
    tables = [row_table(section_rows(local_beams << bit), local_beams << bit, cross_rows) for bit in range(cross_sections)]
    tables = lax.optimization_barrier(tables)
    level = lax.all_to_all(pieces, "pulse", split_axis=0, concat_axis=0, tiled=True)
    level, tables = lax.optimization_barrier((level, tables))
    level = jnp.transpose(level, (1, 0, 2, 3))
    level = padded_lanes(level.reshape(parts, pulse_count * local_beams, piece_bins + need), piece_bins + need)
    level = split_kids(level, local_beams)
    for bit in range(cross_sections):
        section = local_sections + bit
        level = run_section(level, section, local_beams << bit, bit < cross_sections - 1, tables[bit])
    level = level[..., :piece_bins].reshape(parts, pulse_count, local_beams, piece_bins)
    level = jnp.transpose(level, (1, 0, 2, 3))
    level = lax.all_to_all(level, "pulse", split_axis=0, concat_axis=0, tiled=True)
    return jnp.transpose(level, (1, 2, 0, 3)).reshape(parts, local_beams, bins)


def solution(mesh):
    return jax.shard_map(
        on_device,
        mesh=mesh,
        in_specs=(P(None, "pulse", "range"), P(), P(), P(), P(), P()),
        out_specs=P(None, "pulse", "range"),
        check_vma=False,
    )
```

```python
import functools

import jax
import jax.numpy as jnp
from jax import lax
from jax.sharding import PartitionSpec as P
from jax.experimental import pallas as pl
from jax.experimental.pallas import tpu as pltpu

TAPS = 4
MAXOFF = 8
MARGIN = 15
BLOCK = 256
LANE = 128


half_root = 0.7071067811865476


def shifted(shard, axis, by):
    count = lax.axis_size(axis)
    pairs = [(i, i + by) for i in range(count) if 0 <= i + by < count]
    return lax.ppermute(shard, axis, pairs)


def toeplitz_rows(vector, block, rows):
    taps_len = vector.shape[0]
    width = rows + 1
    line = jnp.concatenate([vector, jnp.zeros((width - taps_len,), vector.dtype)])
    return jnp.tile(line, block)[: block * rows].reshape(block, rows)


def band_matrix(filt, block, rows):
    real_band = toeplitz_rows(filt[0], block, rows).T
    imag_band = toeplitz_rows(filt[1], block, rows).T
    upper = jnp.concatenate([real_band, imag_band], axis=1)
    lower = jnp.concatenate([-imag_band, real_band], axis=1)
    return jnp.concatenate([upper, lower], axis=0)


def compress(wide, filt, blocks):
    parts, count, length = wide.shape
    taps_len = filt.shape[1]
    reach = -(-(BLOCK + taps_len - 1) // BLOCK)
    rows = reach * BLOCK
    cut = wide.reshape(parts, count, length // BLOCK, BLOCK)
    window = jnp.concatenate([cut[:, :, c : c + blocks] for c in range(reach)], axis=3)
    segments = jnp.concatenate([window[0], window[1]], axis=2)
    product = lax.dot_general(
        segments,
        band_matrix(filt, BLOCK, rows),
        (((2,), (0,)), ((), ())),
        preferred_element_type=jnp.float32,
    )
    real_part = product[:, :, :BLOCK].reshape(count, blocks * BLOCK)
    imag_part = product[:, :, BLOCK:].reshape(count, blocks * BLOCK)
    return jnp.stack([real_part, imag_part])


def merge_kernel(beams, chained, weight_ref, kid_ref, table_ref, out_ref):
    length = kid_ref.shape[-1]
    reach = MARGIN - MAXOFF + 1
    acc = [[None, None], [None, None]]
    for c in range(2):
        interp = []
        for part in range(2):
            x = kid_ref[c, part]
            total = weight_ref[c, 0] * x
            for offset in range(1, reach):
                total = total + weight_ref[c, offset] * pltpu.roll(x, length - offset, 1)
            interp.append(total)
        for half in range(2):
            moved = []
            for part in range(2):
                pick = interp[part]
                for bit in (2, 1, 0):
                    hit = table_ref[bit, c, half][:, 0:1] > 0.5
                    pick = jnp.where(hit, pltpu.roll(pick, length - (1 << bit), 1), pick)
                moved.append(pick)
            cos_row = table_ref[3, c, half][:, 0:1]
            sin_row = table_ref[4, c, half][:, 0:1]
            real_part = cos_row * moved[0] - sin_row * moved[1]
            imag_part = sin_row * moved[0] + cos_row * moved[1]
            if c == 0:
                acc[half] = [real_part, imag_part]
            else:
                acc[half] = [acc[half][0] + real_part, acc[half][1] + imag_part]
    rows = kid_ref.shape[2]
    for half in range(2):
        for part in range(2):
            value = acc[half][part] * half_root
            for group in range(rows // beams):
                block = value[group * beams : (group + 1) * beams]
                if chained:
                    start = (group // 2) * 2 * beams + half * beams
                    out_ref[group % 2, part, start : start + beams] = block
                else:
                    start = group * 2 * beams + half * beams
                    out_ref[part, start : start + beams] = block


def merge_call(beams, chained, weights, kids, table):
    _, _, rows, length = kids.shape
    vmem = pltpu.VMEM
    elems = 2 * 2 * rows * length
    shape = (2, 2, rows, length) if chained else (2, 2 * rows, length)
    return pl.pallas_call(
        functools.partial(merge_kernel, beams, chained),
        out_shape=jax.ShapeDtypeStruct(shape, jnp.float32),
        in_specs=[
            pl.BlockSpec(memory_space=pltpu.SMEM),
            pl.BlockSpec(memory_space=vmem),
            pl.BlockSpec(memory_space=vmem),
        ],
        out_specs=pl.BlockSpec(memory_space=vmem),
        cost_estimate=pl.CostEstimate(flops=60 * elems, transcendentals=0, bytes_accessed=8 * elems),
    )(weights, kids, table)


def tap_weights(taps, weights):
    spots = jnp.arange(MARGIN - MAXOFF + 1, dtype=taps.dtype)
    total = jnp.where(taps[..., 0, None] == spots, weights[..., 0, None], 0.0)
    for tap in range(1, taps.shape[-1]):
        total = total + jnp.where(taps[..., tap, None] == spots, weights[..., tap, None], 0.0)
    return total


def per_row(table, groups):
    beams = table.shape[-1] // 2
    halves = table.reshape(table.shape[:-1] + (2, beams))
    return jnp.tile(halves, (1,) * (halves.ndim - 1) + (groups,))


def split_kids(level, beams):
    parts, rows, length = level.shape
    groups = rows // (2 * beams)
    pairs = level.reshape(parts, groups, 2, beams, length)
    return jnp.stack([pairs[:, :, c].reshape(parts, rows // 2, length) for c in range(2)])


def row_table(packed, beams, rows):
    return jnp.broadcast_to(per_row(packed, rows // beams)[..., None], (5, 2, 2, rows, LANE))


def merge_section(kids, beams, chained, weights, packed, table=None):
    if table is None:
        table = row_table(packed, beams, kids.shape[2])
    return merge_call(beams, chained, weights, kids, table)


def padded_lanes(level, width):
    length = level.shape[-1]
    target = -(-width // LANE) * LANE
    if target > length:
        return jnp.pad(level, ((0, 0), (0, 0), (0, target - length)))
    return level[..., :target]


def on_device(raw, filt, tap_index, tap_weight, beam_shift, beam_phase):
    pulse_count = lax.axis_size("pulse")
    parts, local_beams, bins = raw.shape
    taps_len = filt.shape[1]
    local_sections = local_beams.bit_length() - 1
    cross_sections = pulse_count.bit_length() - 1
    sections = local_sections + cross_sections
    extra = sections * MARGIN
    blocks = -(-(bins + extra) // BLOCK)
    reach = -(-(BLOCK + taps_len - 1) // BLOCK)
    rim_len = (blocks + reach - 1) * BLOCK - bins
    rim = shifted(raw[:, :, :rim_len], "range", -1)
    wide = jnp.concatenate([raw, rim], axis=2)
    level = padded_lanes(compress(wide, filt, blocks), bins + extra)
    all_weights = tap_weights(tap_index, tap_weight)
    kind = lax.broadcasted_iota(jnp.int32, (5,) + beam_shift.shape, 0)
    bit_rows = ((beam_shift[None] >> jnp.minimum(kind, 2)) & 1).astype(jnp.float32)
    angle_rows = jnp.where(kind == 3, jnp.cos(beam_phase)[None], jnp.sin(beam_phase)[None])
    all_rows = jnp.where(kind < 3, bit_rows, angle_rows)

    def section_rows(beams):
        start = 2 * beams - 2
        return all_rows[:, :, start : start + 2 * beams]

    def run_section(kids, section, beams, chained, table=None):
        return merge_section(kids, beams, chained, all_weights[section], section_rows(beams), table)

    level = split_kids(level, 1)
    for section in range(local_sections):
        level = run_section(level, section, 1 << section, section < local_sections - 1)
    piece_bins = bins // pulse_count
    need = cross_sections * MARGIN
    flat = level[:, :, : bins + need]
    flat = jnp.pad(flat, ((0, 0), (0, 0), (0, piece_bins - need)))
    head = flat[:, :, :bins].reshape(parts, local_beams, pulse_count, piece_bins)
    tail = flat[:, :, piece_bins:].reshape(parts, local_beams, pulse_count, piece_bins)[
        :, :, :, :need
    ]
    pieces = jnp.transpose(jnp.concatenate([head, tail], axis=3), (2, 0, 1, 3))
    cross_rows = pulse_count * local_beams // 2
    tables = [row_table(section_rows(local_beams << bit), local_beams << bit, cross_rows) for bit in range(cross_sections)]
    tables = lax.optimization_barrier(tables)
    level = lax.all_to_all(pieces, "pulse", split_axis=0, concat_axis=0, tiled=True)
    level, tables = lax.optimization_barrier((level, tables))
    level = jnp.transpose(level, (1, 0, 2, 3))
    level = padded_lanes(level.reshape(parts, pulse_count * local_beams, piece_bins + need), piece_bins + need)
    level = split_kids(level, local_beams)
    for bit in range(cross_sections):
        section = local_sections + bit
        level = run_section(level, section, local_beams << bit, bit < cross_sections - 1, tables[bit])
    blocks = level[..., :piece_bins].reshape(parts, pulse_count, local_beams, piece_bins)
    me = lax.axis_index("pulse")
    received = [lax.dynamic_index_in_dim(blocks, me, axis=1, keepdims=False)]
    for step in range(1, pulse_count):
        outgoing = lax.dynamic_index_in_dim(blocks, (me + step) % pulse_count, axis=1, keepdims=False)
        pairs = [(i, (i + step) % pulse_count) for i in range(pulse_count)]
        received.append(lax.ppermute(outgoing, "pulse", pairs))
    by_offset = jnp.stack([received[(pulse_count - j) % pulse_count] for j in range(pulse_count)], axis=2)
    ordered = jnp.roll(by_offset, me, axis=2)
    return ordered.reshape(parts, local_beams, bins)


def solution(mesh):
    return jax.shard_map(
        on_device,
        mesh=mesh,
        in_specs=(P(None, "pulse", "range"), P(), P(), P(), P(), P()),
        out_specs=P(None, "pulse", "range"),
        check_vma=False,
    )
```

```python
import functools

import jax
import jax.numpy as jnp
from jax import lax
from jax.sharding import PartitionSpec as P
from jax.experimental import pallas as pl
from jax.experimental.pallas import tpu as pltpu

TAPS = 4
MAXOFF = 8
MARGIN = 15
BLOCK = 256
LANE = 128


half_root = 0.7071067811865476


def shifted(shard, axis, by):
    count = lax.axis_size(axis)
    pairs = [(i, i + by) for i in range(count) if 0 <= i + by < count]
    return lax.ppermute(shard, axis, pairs)


def toeplitz_rows(vector, block, rows):
    taps_len = vector.shape[0]
    width = rows + 1
    line = jnp.concatenate([vector, jnp.zeros((width - taps_len,), vector.dtype)])
    return jnp.tile(line, block)[: block * rows].reshape(block, rows)


def band_matrix(filt, block, rows):
    real_band = toeplitz_rows(filt[0], block, rows).T
    imag_band = toeplitz_rows(filt[1], block, rows).T
    upper = jnp.concatenate([real_band, imag_band], axis=1)
    lower = jnp.concatenate([-imag_band, real_band], axis=1)
    return jnp.concatenate([upper, lower], axis=0)


def compress(wide, filt, blocks):
    parts, count, length = wide.shape
    taps_len = filt.shape[1]
    reach = -(-(BLOCK + taps_len - 1) // BLOCK)
    rows = reach * BLOCK
    cut = wide.reshape(parts, count, length // BLOCK, BLOCK)
    window = jnp.concatenate([cut[:, :, c : c + blocks] for c in range(reach)], axis=3)
    segments = jnp.concatenate([window[0], window[1]], axis=2)
    product = lax.dot_general(
        segments,
        band_matrix(filt, BLOCK, rows),
        (((2,), (0,)), ((), ())),
        preferred_element_type=jnp.float32,
    )
    real_part = product[:, :, :BLOCK].reshape(count, blocks * BLOCK)
    imag_part = product[:, :, BLOCK:].reshape(count, blocks * BLOCK)
    return jnp.stack([real_part, imag_part])


def merge_kernel(beams, chained, weight_ref, kid_ref, table_ref, out_ref):
    length = kid_ref.shape[-1]
    reach = MARGIN - MAXOFF + 1
    acc = [[None, None], [None, None]]
    for c in range(2):
        interp = []
        for part in range(2):
            x = kid_ref[c, part]
            total = weight_ref[c, 0] * x
            for offset in range(1, reach):
                total = total + weight_ref[c, offset] * pltpu.roll(x, length - offset, 1)
            interp.append(total)
        for half in range(2):
            moved = []
            for part in range(2):
                pick = interp[part]
                for bit in (2, 1, 0):
                    hit = table_ref[bit, c, half][:, 0:1] > 0.5
                    pick = jnp.where(hit, pltpu.roll(pick, length - (1 << bit), 1), pick)
                moved.append(pick)
            cos_row = table_ref[3, c, half][:, 0:1]
            sin_row = table_ref[4, c, half][:, 0:1]
            real_part = cos_row * moved[0] - sin_row * moved[1]
            imag_part = sin_row * moved[0] + cos_row * moved[1]
            if c == 0:
                acc[half] = [real_part, imag_part]
            else:
                acc[half] = [acc[half][0] + real_part, acc[half][1] + imag_part]
    rows = kid_ref.shape[2]
    for half in range(2):
        for part in range(2):
            value = acc[half][part] * half_root
            for group in range(rows // beams):
                block = value[group * beams : (group + 1) * beams]
                if chained:
                    start = (group // 2) * 2 * beams + half * beams
                    out_ref[group % 2, part, start : start + beams] = block
                else:
                    start = group * 2 * beams + half * beams
                    out_ref[part, start : start + beams] = block


def merge_call(beams, chained, weights, kids, table):
    _, _, rows, length = kids.shape
    vmem = pltpu.VMEM
    elems = 2 * 2 * rows * length
    shape = (2, 2, rows, length) if chained else (2, 2 * rows, length)
    return pl.pallas_call(
        functools.partial(merge_kernel, beams, chained),
        out_shape=jax.ShapeDtypeStruct(shape, jnp.float32),
        in_specs=[
            pl.BlockSpec(memory_space=pltpu.SMEM),
            pl.BlockSpec(memory_space=vmem),
            pl.BlockSpec(memory_space=vmem),
        ],
        out_specs=pl.BlockSpec(memory_space=vmem),
        cost_estimate=pl.CostEstimate(flops=60 * elems, transcendentals=0, bytes_accessed=8 * elems),
    )(weights, kids, table)


def tap_weights(taps, weights):
    spots = jnp.arange(MARGIN - MAXOFF + 1, dtype=taps.dtype)
    total = jnp.where(taps[..., 0, None] == spots, weights[..., 0, None], 0.0)
    for tap in range(1, taps.shape[-1]):
        total = total + jnp.where(taps[..., tap, None] == spots, weights[..., tap, None], 0.0)
    return total


def per_row(table, groups):
    beams = table.shape[-1] // 2
    halves = table.reshape(table.shape[:-1] + (2, beams))
    return jnp.tile(halves, (1,) * (halves.ndim - 1) + (groups,))


def split_kids(level, beams):
    parts, rows, length = level.shape
    groups = rows // (2 * beams)
    pairs = level.reshape(parts, groups, 2, beams, length)
    return jnp.stack([pairs[:, :, c].reshape(parts, rows // 2, length) for c in range(2)])


def row_table(packed, beams, rows):
    return jnp.broadcast_to(per_row(packed, rows // beams)[..., None], (5, 2, 2, rows, LANE))


def merge_section(kids, beams, chained, weights, packed, table=None):
    if table is None:
        table = row_table(packed, beams, kids.shape[2])
    return merge_call(beams, chained, weights, kids, table)


def padded_lanes(level, width):
    length = level.shape[-1]
    target = -(-width // LANE) * LANE
    if target > length:
        return jnp.pad(level, ((0, 0), (0, 0), (0, target - length)))
    return level[..., :target]


def on_device(raw, filt, tap_index, tap_weight, beam_shift, beam_phase):
    pulse_count = lax.axis_size("pulse")
    parts, local_beams, bins = raw.shape
    taps_len = filt.shape[1]
    local_sections = local_beams.bit_length() - 1
    cross_sections = pulse_count.bit_length() - 1
    sections = local_sections + cross_sections
    extra = sections * MARGIN
    blocks = -(-(bins + extra) // BLOCK)
    reach = -(-(BLOCK + taps_len - 1) // BLOCK)
    rim_len = (blocks + reach - 1) * BLOCK - bins
    rim = shifted(raw[:, :, :rim_len], "range", -1)
    wide = jnp.concatenate([raw, rim], axis=2)
    level = padded_lanes(compress(wide, filt, blocks), bins + extra)
    all_weights = tap_weights(tap_index, tap_weight)
    kind = lax.broadcasted_iota(jnp.int32, (5,) + beam_shift.shape, 0)
    bit_rows = ((beam_shift[None] >> jnp.minimum(kind, 2)) & 1).astype(jnp.float32)
    angle_rows = jnp.where(kind == 3, jnp.cos(beam_phase)[None], jnp.sin(beam_phase)[None])
    all_rows = jnp.where(kind < 3, bit_rows, angle_rows)

    def section_rows(beams):
        start = 2 * beams - 2
        return all_rows[:, :, start : start + 2 * beams]

    def run_section(kids, section, beams, chained, table=None):
        return merge_section(kids, beams, chained, all_weights[section], section_rows(beams), table)

    level = split_kids(level, 1)
    for section in range(local_sections):
        level = run_section(level, section, 1 << section, section < local_sections - 1)
    piece_bins = bins // pulse_count
    need = cross_sections * MARGIN
    carry = -(-(piece_bins + need) // LANE) * LANE - piece_bins
    flat = padded_lanes(level, bins + piece_bins)
    head = flat[:, :, :bins].reshape(parts, local_beams, pulse_count, piece_bins)
    tail = flat[:, :, piece_bins:].reshape(parts, local_beams, pulse_count, piece_bins)[
        :, :, :, :carry
    ]
    pieces = jnp.transpose(jnp.concatenate([head, tail], axis=3), (2, 0, 1, 3))
    cross_rows = pulse_count * local_beams // 2
    tables = [row_table(section_rows(local_beams << bit), local_beams << bit, cross_rows) for bit in range(cross_sections)]
    tables = lax.optimization_barrier(tables)
    level = lax.all_to_all(pieces, "pulse", split_axis=0, concat_axis=0, tiled=True)
    level, tables = lax.optimization_barrier((level, tables))
    level = jnp.transpose(level, (1, 0, 2, 3))
    level = level.reshape(parts, pulse_count * local_beams, piece_bins + carry)
    level = split_kids(level, local_beams)
    for bit in range(cross_sections):
        section = local_sections + bit
        level = run_section(level, section, local_beams << bit, bit < cross_sections - 1, tables[bit])
    level = level[..., :piece_bins].reshape(parts, pulse_count, local_beams, piece_bins)
    level = jnp.transpose(level, (1, 0, 2, 3))
    level = lax.all_to_all(level, "pulse", split_axis=0, concat_axis=0, tiled=True)
    return jnp.transpose(level, (1, 2, 0, 3)).reshape(parts, local_beams, bins)


def solution(mesh):
    return jax.shard_map(
        on_device,
        mesh=mesh,
        in_specs=(P(None, "pulse", "range"), P(), P(), P(), P(), P()),
        out_specs=P(None, "pulse", "range"),
        check_vma=False,
    )
```

```python
import functools

import jax
import jax.numpy as jnp
from jax import lax
from jax.sharding import PartitionSpec as P
from jax.experimental import pallas as pl
from jax.experimental.pallas import tpu as pltpu

TAPS = 4
MAXOFF = 8
MARGIN = 15
BLOCK = 256
LANE = 128


half_root = 0.7071067811865476


def shifted(shard, axis, by):
    count = lax.axis_size(axis)
    pairs = [(i, i + by) for i in range(count) if 0 <= i + by < count]
    return lax.ppermute(shard, axis, pairs)


def toeplitz_rows(vector, block, rows):
    taps_len = vector.shape[0]
    width = rows + 1
    line = jnp.concatenate([vector, jnp.zeros((width - taps_len,), vector.dtype)])
    return jnp.tile(line, block)[: block * rows].reshape(block, rows)


def band_matrix(filt, block, rows):
    real_band = toeplitz_rows(filt[0], block, rows).T
    imag_band = toeplitz_rows(filt[1], block, rows).T
    upper = jnp.concatenate([real_band, imag_band], axis=1)
    lower = jnp.concatenate([-imag_band, real_band], axis=1)
    return jnp.concatenate([upper, lower], axis=0)


def compress(wide, filt, blocks):
    parts, count, length = wide.shape
    taps_len = filt.shape[1]
    reach = -(-(BLOCK + taps_len - 1) // BLOCK)
    rows = reach * BLOCK
    cut = wide.reshape(parts, count, length // BLOCK, BLOCK)
    window = jnp.concatenate([cut[:, :, c : c + blocks] for c in range(reach)], axis=3)
    segments = jnp.concatenate([window[0], window[1]], axis=2)
    product = lax.dot_general(
        segments,
        band_matrix(filt, BLOCK, rows),
        (((2,), (0,)), ((), ())),
        preferred_element_type=jnp.float32,
    )
    real_part = product[:, :, :BLOCK].reshape(count, blocks * BLOCK)
    imag_part = product[:, :, BLOCK:].reshape(count, blocks * BLOCK)
    return jnp.stack([real_part, imag_part])


def merge_kernel(beams, chained, grouped, weight_ref, kid_ref, table_ref, out_ref):
    length = kid_ref.shape[-1]
    reach = MARGIN - MAXOFF + 1
    acc = [[None, None], [None, None]]
    for c in range(2):
        interp = []
        for part in range(2):
            if grouped:
                x = jnp.concatenate([kid_ref[2 * g + c, part] for g in range(kid_ref.shape[0] // 2)], axis=0)
            else:
                x = kid_ref[c, part]
            total = weight_ref[c, 0] * x
            for offset in range(1, reach):
                total = total + weight_ref[c, offset] * pltpu.roll(x, length - offset, 1)
            interp.append(total)
        for half in range(2):
            moved = []
            for part in range(2):
                pick = interp[part]
                for bit in (2, 1, 0):
                    hit = table_ref[bit, c, half][:, 0:1] > 0.5
                    pick = jnp.where(hit, pltpu.roll(pick, length - (1 << bit), 1), pick)
                moved.append(pick)
            cos_row = table_ref[3, c, half][:, 0:1]
            sin_row = table_ref[4, c, half][:, 0:1]
            real_part = cos_row * moved[0] - sin_row * moved[1]
            imag_part = sin_row * moved[0] + cos_row * moved[1]
            if c == 0:
                acc[half] = [real_part, imag_part]
            else:
                acc[half] = [acc[half][0] + real_part, acc[half][1] + imag_part]
    rows = kid_ref.shape[0] // 2 * kid_ref.shape[2] if grouped else kid_ref.shape[2]
    for half in range(2):
        for part in range(2):
            value = acc[half][part] * half_root
            for group in range(rows // beams):
                block = value[group * beams : (group + 1) * beams]
                if chained:
                    start = (group // 2) * 2 * beams + half * beams
                    out_ref[group % 2, part, start : start + beams] = block
                else:
                    start = group * 2 * beams + half * beams
                    out_ref[part, start : start + beams] = block


def merge_call(beams, chained, weights, kids, table, grouped=False):
    length = kids.shape[-1]
    rows = kids.shape[0] // 2 * kids.shape[2] if grouped else kids.shape[2]
    vmem = pltpu.VMEM
    elems = 2 * 2 * rows * length
    shape = (2, 2, rows, length) if chained else (2, 2 * rows, length)
    return pl.pallas_call(
        functools.partial(merge_kernel, beams, chained, grouped),
        out_shape=jax.ShapeDtypeStruct(shape, jnp.float32),
        in_specs=[
            pl.BlockSpec(memory_space=pltpu.SMEM),
            pl.BlockSpec(memory_space=vmem),
            pl.BlockSpec(memory_space=vmem),
        ],
        out_specs=pl.BlockSpec(memory_space=vmem),
        cost_estimate=pl.CostEstimate(flops=60 * elems, transcendentals=0, bytes_accessed=8 * elems),
    )(weights, kids, table)


def tap_weights(taps, weights):
    spots = jnp.arange(MARGIN - MAXOFF + 1, dtype=taps.dtype)
    total = jnp.where(taps[..., 0, None] == spots, weights[..., 0, None], 0.0)
    for tap in range(1, taps.shape[-1]):
        total = total + jnp.where(taps[..., tap, None] == spots, weights[..., tap, None], 0.0)
    return total


def per_row(table, groups):
    beams = table.shape[-1] // 2
    halves = table.reshape(table.shape[:-1] + (2, beams))
    return jnp.tile(halves, (1,) * (halves.ndim - 1) + (groups,))


def split_kids(level, beams):
    parts, rows, length = level.shape
    groups = rows // (2 * beams)
    pairs = level.reshape(parts, groups, 2, beams, length)
    return jnp.stack([pairs[:, :, c].reshape(parts, rows // 2, length) for c in range(2)])


def row_table(packed, beams, rows):
    return jnp.broadcast_to(per_row(packed, rows // beams)[..., None], (5, 2, 2, rows, LANE))


def merge_section(kids, beams, chained, weights, packed, table=None, grouped=False):
    if table is None:
        table = row_table(packed, beams, kids.shape[2])
    return merge_call(beams, chained, weights, kids, table, grouped)


def padded_lanes(level, width):
    length = level.shape[-1]
    target = -(-width // LANE) * LANE
    if target > length:
        return jnp.pad(level, ((0, 0), (0, 0), (0, target - length)))
    return level[..., :target]


def on_device(raw, filt, tap_index, tap_weight, beam_shift, beam_phase):
    pulse_count = lax.axis_size("pulse")
    parts, local_beams, bins = raw.shape
    taps_len = filt.shape[1]
    local_sections = local_beams.bit_length() - 1
    cross_sections = pulse_count.bit_length() - 1
    sections = local_sections + cross_sections
    extra = sections * MARGIN
    blocks = -(-(bins + extra) // BLOCK)
    reach = -(-(BLOCK + taps_len - 1) // BLOCK)
    rim_len = (blocks + reach - 1) * BLOCK - bins
    rim = shifted(raw[:, :, :rim_len], "range", -1)
    wide = jnp.concatenate([raw, rim], axis=2)
    level = padded_lanes(compress(wide, filt, blocks), bins + extra)
    all_weights = tap_weights(tap_index, tap_weight)
    kind = lax.broadcasted_iota(jnp.int32, (5,) + beam_shift.shape, 0)
    bit_rows = ((beam_shift[None] >> jnp.minimum(kind, 2)) & 1).astype(jnp.float32)
    angle_rows = jnp.where(kind == 3, jnp.cos(beam_phase)[None], jnp.sin(beam_phase)[None])
    all_rows = jnp.where(kind < 3, bit_rows, angle_rows)

    def section_rows(beams):
        start = 2 * beams - 2
        return all_rows[:, :, start : start + 2 * beams]

    def run_section(kids, section, beams, chained, table=None, grouped=False):
        return merge_section(kids, beams, chained, all_weights[section], section_rows(beams), table, grouped)

    level = split_kids(level, 1)
    for section in range(local_sections):
        level = run_section(level, section, 1 << section, section < local_sections - 1)
    piece_bins = bins // pulse_count
    need = cross_sections * MARGIN
    carry = -(-(piece_bins + need) // LANE) * LANE - piece_bins
    flat = padded_lanes(level, bins + piece_bins)
    head = flat[:, :, :bins].reshape(parts, local_beams, pulse_count, piece_bins)
    tail = flat[:, :, piece_bins:].reshape(parts, local_beams, pulse_count, piece_bins)[
        :, :, :, :carry
    ]
    pieces = jnp.transpose(jnp.concatenate([head, tail], axis=3), (2, 0, 1, 3))
    cross_rows = pulse_count * local_beams // 2
    tables = [row_table(section_rows(local_beams << bit), local_beams << bit, cross_rows) for bit in range(cross_sections)]
    tables = lax.optimization_barrier(tables)
    level = lax.all_to_all(pieces, "pulse", split_axis=0, concat_axis=0, tiled=True)
    level, tables = lax.optimization_barrier((level, tables))
    for bit in range(cross_sections):
        section = local_sections + bit
        level = run_section(level, section, local_beams << bit, bit < cross_sections - 1, tables[bit], bit == 0)
    level = level[..., :piece_bins].reshape(parts, pulse_count, local_beams, piece_bins)
    level = jnp.transpose(level, (1, 0, 2, 3))
    level = lax.all_to_all(level, "pulse", split_axis=0, concat_axis=0, tiled=True)
    return jnp.transpose(level, (1, 2, 0, 3)).reshape(parts, local_beams, bins)


def solution(mesh):
    return jax.shard_map(
        on_device,
        mesh=mesh,
        in_specs=(P(None, "pulse", "range"), P(), P(), P(), P(), P()),
        out_specs=P(None, "pulse", "range"),
        check_vma=False,
    )
```

```python
import functools

import jax
import jax.numpy as jnp
from jax import lax
from jax.sharding import PartitionSpec as P
from jax.experimental import pallas as pl
from jax.experimental.pallas import tpu as pltpu

TAPS = 4
MAXOFF = 8
MARGIN = 15
BLOCK = 256
LANE = 128


half_root = 0.7071067811865476


def shifted(shard, axis, by):
    count = lax.axis_size(axis)
    pairs = [(i, i + by) for i in range(count) if 0 <= i + by < count]
    return lax.ppermute(shard, axis, pairs)


def toeplitz_rows(vector, block, rows):
    taps_len = vector.shape[0]
    width = rows + 1
    line = jnp.concatenate([vector, jnp.zeros((width - taps_len,), vector.dtype)])
    return jnp.tile(line, block)[: block * rows].reshape(block, rows)


def band_matrix(filt, block, rows):
    real_band = toeplitz_rows(filt[0], block, rows).T
    imag_band = toeplitz_rows(filt[1], block, rows).T
    upper = jnp.concatenate([real_band, imag_band], axis=1)
    lower = jnp.concatenate([-imag_band, real_band], axis=1)
    return jnp.concatenate([upper, lower], axis=0)


def compress(wide, filt, blocks):
    parts, count, length = wide.shape
    taps_len = filt.shape[1]
    reach = -(-(BLOCK + taps_len - 1) // BLOCK)
    rows = reach * BLOCK
    cut = wide.reshape(parts, count, length // BLOCK, BLOCK)
    window = jnp.concatenate([cut[:, :, c : c + blocks] for c in range(reach)], axis=3)
    segments = jnp.concatenate([window[0], window[1]], axis=2)
    product = lax.dot_general(
        segments,
        band_matrix(filt, BLOCK, rows),
        (((2,), (0,)), ((), ())),
        preferred_element_type=jnp.float32,
    )
    real_part = product[:, :, :BLOCK].reshape(count, blocks * BLOCK)
    imag_part = product[:, :, BLOCK:].reshape(count, blocks * BLOCK)
    return jnp.stack([real_part, imag_part])


def merge_kernel(beams, chained, slot, weight_ref, kid_ref, table_ref, out_ref):
    if slot is not None:
        table_ref = table_ref.at[slot]
    length = kid_ref.shape[-1]
    reach = MARGIN - MAXOFF + 1
    acc = [[None, None], [None, None]]
    for c in range(2):
        interp = []
        for part in range(2):
            x = kid_ref[c, part]
            total = weight_ref[c, 0] * x
            for offset in range(1, reach):
                total = total + weight_ref[c, offset] * pltpu.roll(x, length - offset, 1)
            interp.append(total)
        for half in range(2):
            moved = []
            for part in range(2):
                pick = interp[part]
                for bit in (2, 1, 0):
                    hit = table_ref[bit, c, half][:, 0:1] > 0.5
                    pick = jnp.where(hit, pltpu.roll(pick, length - (1 << bit), 1), pick)
                moved.append(pick)
            cos_row = table_ref[3, c, half][:, 0:1]
            sin_row = table_ref[4, c, half][:, 0:1]
            real_part = cos_row * moved[0] - sin_row * moved[1]
            imag_part = sin_row * moved[0] + cos_row * moved[1]
            if c == 0:
                acc[half] = [real_part, imag_part]
            else:
                acc[half] = [acc[half][0] + real_part, acc[half][1] + imag_part]
    rows = kid_ref.shape[2]
    for half in range(2):
        for part in range(2):
            value = acc[half][part] * half_root
            for group in range(rows // beams):
                block = value[group * beams : (group + 1) * beams]
                if chained:
                    start = (group // 2) * 2 * beams + half * beams
                    out_ref[group % 2, part, start : start + beams] = block
                else:
                    start = group * 2 * beams + half * beams
                    out_ref[part, start : start + beams] = block


def merge_call(beams, chained, weights, kids, table, slot=None):
    _, _, rows, length = kids.shape
    vmem = pltpu.VMEM
    elems = 2 * 2 * rows * length
    shape = (2, 2, rows, length) if chained else (2, 2 * rows, length)
    return pl.pallas_call(
        functools.partial(merge_kernel, beams, chained, slot),
        out_shape=jax.ShapeDtypeStruct(shape, jnp.float32),
        in_specs=[
            pl.BlockSpec(memory_space=pltpu.SMEM),
            pl.BlockSpec(memory_space=vmem),
            pl.BlockSpec(memory_space=vmem),
        ],
        out_specs=pl.BlockSpec(memory_space=vmem),
        cost_estimate=pl.CostEstimate(flops=60 * elems, transcendentals=0, bytes_accessed=8 * elems),
    )(weights, kids, table)


def tap_weights(taps, weights):
    spots = jnp.arange(MARGIN - MAXOFF + 1, dtype=taps.dtype)
    total = jnp.where(taps[..., 0, None] == spots, weights[..., 0, None], 0.0)
    for tap in range(1, taps.shape[-1]):
        total = total + jnp.where(taps[..., tap, None] == spots, weights[..., tap, None], 0.0)
    return total


def per_row(table, groups):
    beams = table.shape[-1] // 2
    halves = table.reshape(table.shape[:-1] + (2, beams))
    return jnp.tile(halves, (1,) * (halves.ndim - 1) + (groups,))


def split_kids(level, beams):
    parts, rows, length = level.shape
    groups = rows // (2 * beams)
    pairs = level.reshape(parts, groups, 2, beams, length)
    return jnp.stack([pairs[:, :, c].reshape(parts, rows // 2, length) for c in range(2)])


def row_table(packed, beams, rows):
    return jnp.broadcast_to(per_row(packed, rows // beams)[..., None], (5, 2, 2, rows, LANE))


def merge_section(kids, beams, chained, weights, packed, table=None, slot=None):
    if table is None:
        table = row_table(packed, beams, kids.shape[2])
    return merge_call(beams, chained, weights, kids, table, slot)


def padded_lanes(level, width):
    length = level.shape[-1]
    target = -(-width // LANE) * LANE
    if target > length:
        return jnp.pad(level, ((0, 0), (0, 0), (0, target - length)))
    return level[..., :target]


def on_device(raw, filt, tap_index, tap_weight, beam_shift, beam_phase):
    pulse_count = lax.axis_size("pulse")
    parts, local_beams, bins = raw.shape
    taps_len = filt.shape[1]
    local_sections = local_beams.bit_length() - 1
    cross_sections = pulse_count.bit_length() - 1
    sections = local_sections + cross_sections
    extra = sections * MARGIN
    blocks = -(-(bins + extra) // BLOCK)
    reach = -(-(BLOCK + taps_len - 1) // BLOCK)
    rim_len = (blocks + reach - 1) * BLOCK - bins
    rim = shifted(raw[:, :, :rim_len], "range", -1)
    wide = jnp.concatenate([raw, rim], axis=2)
    level = padded_lanes(compress(wide, filt, blocks), bins + extra)
    all_weights = tap_weights(tap_index, tap_weight)
    kind = lax.broadcasted_iota(jnp.int32, (5,) + beam_shift.shape, 0)
    bit_rows = ((beam_shift[None] >> jnp.minimum(kind, 2)) & 1).astype(jnp.float32)
    angle_rows = jnp.where(kind == 3, jnp.cos(beam_phase)[None], jnp.sin(beam_phase)[None])
    all_rows = jnp.where(kind < 3, bit_rows, angle_rows)

    def section_rows(beams):
        start = 2 * beams - 2
        return all_rows[:, :, start : start + 2 * beams]

    def run_section(kids, section, beams, chained, table=None, slot=None):
        return merge_section(kids, beams, chained, all_weights[section], section_rows(beams), table, slot)

    level = split_kids(level, 1)
    kid_rows = level.shape[2]
    local_tables = jnp.stack(
        [row_table(section_rows(1 << section), 1 << section, kid_rows) for section in range(local_sections)]
    )
    for section in range(local_sections):
        level = run_section(level, section, 1 << section, section < local_sections - 1, local_tables, section)
    piece_bins = bins // pulse_count
    need = cross_sections * MARGIN
    flat = level[:, :, : bins + need]
    flat = jnp.pad(flat, ((0, 0), (0, 0), (0, piece_bins - need)))
    head = flat[:, :, :bins].reshape(parts, local_beams, pulse_count, piece_bins)
    tail = flat[:, :, piece_bins:].reshape(parts, local_beams, pulse_count, piece_bins)[
        :, :, :, :need
    ]
    pieces = jnp.transpose(jnp.concatenate([head, tail], axis=3), (2, 0, 1, 3))
    cross_rows = pulse_count * local_beams // 2
    tables = [row_table(section_rows(local_beams << bit), local_beams << bit, cross_rows) for bit in range(cross_sections)]
    tables = lax.optimization_barrier(tables)
    level = lax.all_to_all(pieces, "pulse", split_axis=0, concat_axis=0, tiled=True)
    level, tables = lax.optimization_barrier((level, tables))
    level = jnp.transpose(level, (1, 0, 2, 3))
    level = padded_lanes(level.reshape(parts, pulse_count * local_beams, piece_bins + need), piece_bins + need)
    level = split_kids(level, local_beams)
    for bit in range(cross_sections):
        section = local_sections + bit
        level = run_section(level, section, local_beams << bit, bit < cross_sections - 1, tables[bit])
    level = level[..., :piece_bins].reshape(parts, pulse_count, local_beams, piece_bins)
    level = jnp.transpose(level, (1, 0, 2, 3))
    level = lax.all_to_all(level, "pulse", split_axis=0, concat_axis=0, tiled=True)
    return jnp.transpose(level, (1, 2, 0, 3)).reshape(parts, local_beams, bins)


def solution(mesh):
    return jax.shard_map(
        on_device,
        mesh=mesh,
        in_specs=(P(None, "pulse", "range"), P(), P(), P(), P(), P()),
        out_specs=P(None, "pulse", "range"),
        check_vma=False,
    )
```

```python
import functools

import jax
import jax.numpy as jnp
from jax import lax
from jax.sharding import PartitionSpec as P
from jax.experimental import pallas as pl
from jax.experimental.pallas import tpu as pltpu

TAPS = 4
MAXOFF = 8
MARGIN = 15
BLOCK = 256
LANE = 128


half_root = 0.7071067811865476


def shifted(shard, axis, by):
    count = lax.axis_size(axis)
    pairs = [(i, i + by) for i in range(count) if 0 <= i + by < count]
    return lax.ppermute(shard, axis, pairs)


def toeplitz_rows(vector, block, rows):
    taps_len = vector.shape[0]
    width = rows + 1
    line = jnp.concatenate([vector, jnp.zeros((width - taps_len,), vector.dtype)])
    return jnp.tile(line, block)[: block * rows].reshape(block, rows)


def band_matrix(filt, block, rows):
    real_band = toeplitz_rows(filt[0], block, rows).T
    imag_band = toeplitz_rows(filt[1], block, rows).T
    upper = jnp.concatenate([real_band, imag_band], axis=1)
    lower = jnp.concatenate([-imag_band, real_band], axis=1)
    return jnp.concatenate([upper, lower], axis=0)


def compress(wide, filt, blocks):
    parts, count, length = wide.shape
    taps_len = filt.shape[1]
    reach = -(-(BLOCK + taps_len - 1) // BLOCK)
    rows = reach * BLOCK
    cut = wide.reshape(parts, count, length // BLOCK, BLOCK)
    window = jnp.concatenate([cut[:, :, c : c + blocks] for c in range(reach)], axis=3)
    segments = jnp.concatenate([window[0], window[1]], axis=2)
    product = lax.dot_general(
        segments,
        band_matrix(filt, BLOCK, rows),
        (((2,), (0,)), ((), ())),
        preferred_element_type=jnp.float32,
    )
    real_part = product[:, :, :BLOCK].reshape(count, blocks * BLOCK)
    imag_part = product[:, :, BLOCK:].reshape(count, blocks * BLOCK)
    return jnp.stack([real_part, imag_part])


def merge_kernel(beams, chained, slot, section, index_ref, tap_ref, kid_ref, table_ref, out_ref):
    if slot is not None:
        table_ref = table_ref.at[slot]
    weight = []
    for c in range(2):
        row = []
        for d in range(MARGIN - MAXOFF + 1):
            total = jnp.where(index_ref[section, c, 0] == d, tap_ref[section, c, 0], 0.0)
            for tap in range(1, index_ref.shape[-1]):
                total = total + jnp.where(index_ref[section, c, tap] == d, tap_ref[section, c, tap], 0.0)
            row.append(total)
        weight.append(row)
    length = kid_ref.shape[-1]
    reach = MARGIN - MAXOFF + 1
    acc = [[None, None], [None, None]]
    for c in range(2):
        interp = []
        for part in range(2):
            x = kid_ref[c, part]
            total = weight[c][0] * x
            for offset in range(1, reach):
                total = total + weight[c][offset] * pltpu.roll(x, length - offset, 1)
            interp.append(total)
        for half in range(2):
            moved = []
            for part in range(2):
                pick = interp[part]
                for bit in (2, 1, 0):
                    hit = table_ref[bit, c, half][:, 0:1] > 0.5
                    pick = jnp.where(hit, pltpu.roll(pick, length - (1 << bit), 1), pick)
                moved.append(pick)
            cos_row = table_ref[3, c, half][:, 0:1]
            sin_row = table_ref[4, c, half][:, 0:1]
            real_part = cos_row * moved[0] - sin_row * moved[1]
            imag_part = sin_row * moved[0] + cos_row * moved[1]
            if c == 0:
                acc[half] = [real_part, imag_part]
            else:
                acc[half] = [acc[half][0] + real_part, acc[half][1] + imag_part]
    rows = kid_ref.shape[2]
    for half in range(2):
        for part in range(2):
            value = acc[half][part] * half_root
            for group in range(rows // beams):
                block = value[group * beams : (group + 1) * beams]
                if chained:
                    start = (group // 2) * 2 * beams + half * beams
                    out_ref[group % 2, part, start : start + beams] = block
                else:
                    start = group * 2 * beams + half * beams
                    out_ref[part, start : start + beams] = block


def merge_call(beams, chained, weights, kids, table, slot=None):
    section, tap_index, tap_weight = weights
    _, _, rows, length = kids.shape
    vmem = pltpu.VMEM
    elems = 2 * 2 * rows * length
    shape = (2, 2, rows, length) if chained else (2, 2 * rows, length)
    return pl.pallas_call(
        functools.partial(merge_kernel, beams, chained, slot, section),
        out_shape=jax.ShapeDtypeStruct(shape, jnp.float32),
        in_specs=[
            pl.BlockSpec(memory_space=pltpu.SMEM),
            pl.BlockSpec(memory_space=pltpu.SMEM),
            pl.BlockSpec(memory_space=vmem),
            pl.BlockSpec(memory_space=vmem),
        ],
        out_specs=pl.BlockSpec(memory_space=vmem),
        cost_estimate=pl.CostEstimate(flops=60 * elems, transcendentals=0, bytes_accessed=8 * elems),
    )(tap_index, tap_weight, kids, table)


def tap_weights(taps, weights):
    spots = jnp.arange(MARGIN - MAXOFF + 1, dtype=taps.dtype)
    total = jnp.where(taps[..., 0, None] == spots, weights[..., 0, None], 0.0)
    for tap in range(1, taps.shape[-1]):
        total = total + jnp.where(taps[..., tap, None] == spots, weights[..., tap, None], 0.0)
    return total


def per_row(table, groups):
    beams = table.shape[-1] // 2
    halves = table.reshape(table.shape[:-1] + (2, beams))
    return jnp.tile(halves, (1,) * (halves.ndim - 1) + (groups,))


def split_kids(level, beams):
    parts, rows, length = level.shape
    groups = rows // (2 * beams)
    pairs = level.reshape(parts, groups, 2, beams, length)
    return jnp.stack([pairs[:, :, c].reshape(parts, rows // 2, length) for c in range(2)])


def row_table(packed, beams, rows):
    return jnp.broadcast_to(per_row(packed, rows // beams)[..., None], (5, 2, 2, rows, LANE))


def merge_section(kids, beams, chained, weights, packed, table=None, slot=None):
    if table is None:
        table = row_table(packed, beams, kids.shape[2])
    return merge_call(beams, chained, weights, kids, table, slot)


def padded_lanes(level, width):
    length = level.shape[-1]
    target = -(-width // LANE) * LANE
    if target > length:
        return jnp.pad(level, ((0, 0), (0, 0), (0, target - length)))
    return level[..., :target]


def on_device(raw, filt, tap_index, tap_weight, beam_shift, beam_phase):
    pulse_count = lax.axis_size("pulse")
    parts, local_beams, bins = raw.shape
    taps_len = filt.shape[1]
    local_sections = local_beams.bit_length() - 1
    cross_sections = pulse_count.bit_length() - 1
    sections = local_sections + cross_sections
    extra = sections * MARGIN
    blocks = -(-(bins + extra) // BLOCK)
    reach = -(-(BLOCK + taps_len - 1) // BLOCK)
    rim_len = (blocks + reach - 1) * BLOCK - bins
    rim = shifted(raw[:, :, :rim_len], "range", -1)
    wide = jnp.concatenate([raw, rim], axis=2)
    level = padded_lanes(compress(wide, filt, blocks), bins + extra)
    kind = lax.broadcasted_iota(jnp.int32, (5,) + beam_shift.shape, 0)
    bit_rows = ((beam_shift[None] >> jnp.minimum(kind, 2)) & 1).astype(jnp.float32)
    angle_rows = jnp.where(kind == 3, jnp.cos(beam_phase)[None], jnp.sin(beam_phase)[None])
    all_rows = jnp.where(kind < 3, bit_rows, angle_rows)

    def section_rows(beams):
        start = 2 * beams - 2
        return all_rows[:, :, start : start + 2 * beams]

    def run_section(kids, section, beams, chained, table=None, slot=None):
        return merge_section(kids, beams, chained, (section, tap_index, tap_weight), section_rows(beams), table, slot)

    level = split_kids(level, 1)
    kid_rows = level.shape[2]
    local_tables = jnp.stack(
        [row_table(section_rows(1 << section), 1 << section, kid_rows) for section in range(local_sections)]
    )
    for section in range(local_sections):
        level = run_section(level, section, 1 << section, section < local_sections - 1, local_tables, section)
    piece_bins = bins // pulse_count
    need = cross_sections * MARGIN
    flat = level[:, :, : bins + need]
    flat = jnp.pad(flat, ((0, 0), (0, 0), (0, piece_bins - need)))
    head = flat[:, :, :bins].reshape(parts, local_beams, pulse_count, piece_bins)
    tail = flat[:, :, piece_bins:].reshape(parts, local_beams, pulse_count, piece_bins)[
        :, :, :, :need
    ]
    pieces = jnp.transpose(jnp.concatenate([head, tail], axis=3), (2, 0, 1, 3))
    cross_rows = pulse_count * local_beams // 2
    tables = [row_table(section_rows(local_beams << bit), local_beams << bit, cross_rows) for bit in range(cross_sections)]
    tables = lax.optimization_barrier(tables)
    level = lax.all_to_all(pieces, "pulse", split_axis=0, concat_axis=0, tiled=True)
    level, tables = lax.optimization_barrier((level, tables))
    level = jnp.transpose(level, (1, 0, 2, 3))
    level = padded_lanes(level.reshape(parts, pulse_count * local_beams, piece_bins + need), piece_bins + need)
    level = split_kids(level, local_beams)
    for bit in range(cross_sections):
        section = local_sections + bit
        level = run_section(level, section, local_beams << bit, bit < cross_sections - 1, tables[bit])
    level = level[..., :piece_bins].reshape(parts, pulse_count, local_beams, piece_bins)
    level = jnp.transpose(level, (1, 0, 2, 3))
    level = lax.all_to_all(level, "pulse", split_axis=0, concat_axis=0, tiled=True)
    return jnp.transpose(level, (1, 2, 0, 3)).reshape(parts, local_beams, bins)


def solution(mesh):
    return jax.shard_map(
        on_device,
        mesh=mesh,
        in_specs=(P(None, "pulse", "range"), P(), P(), P(), P(), P()),
        out_specs=P(None, "pulse", "range"),
        check_vma=False,
    )
```
